32 devices in a mesh: group: 2 (over x), tm: 16 (over z, y, core).
Axes of the slice: x: 2, y: 2, z: 4, core: 2. Of those that a mesh axis runs over, the one named last changes fastest.
Arguments:
- queries: bfloat16 [4096, 2560], P(('group', 'tm')), parts along dimension 0, may hold values from -120 to 120
- keys: bfloat16 [4096, 2560], P(('group', 'tm')), parts along dimension 0, may hold values from -6 to 6
- values: bfloat16 [4096, 2560], P(('group', 'tm')), parts along dimension 0, may hold values from -6 to 6
- out_grad: bfloat16 [4096, 2560], P(('group', 'tm')), parts along dimension 0, may hold values from -6 to 6
- frame_keep: int32 [8, 3], P('group'), parts along dimension 0, may hold values from 0 to 1, as said below
- band_window: int32 [8], P('group'), parts along dimension 0, may hold values from 65 to 128
Outputs:
- query_grad: bfloat16 [4096, 2560], P(('group', 'tm')), parts along dimension 0
- key_grad: bfloat16 [4096, 2560], P(('group', 'tm')), parts along dimension 0
- value_grad: bfloat16 [4096, 2560], P(('group', 'tm')), parts along dimension 0
The draws below stay inside these ranges and needn't reach their ends.
There are 2 independent parts, one for each index of `group`. The reference program is written for one: setup_inputs(seed, part) draws one part's arguments, and reference() takes and returns one part's arrays. A program takes and returns all parts, laid end to end along the dimension named above; each array names one. Nothing has to cross between parts.
Inputs may be any that keep to these rules, and one draw needn't show every extreme that they name: Every query frame attends its own frame: frame_keep[t, 1] = 1 for every t.
All inputs are finite; a program needn't handle non-finite values.
Results may differ from the reference program's by a relative error of at most 0.01.
Values may be sent and summed in bfloat16 or wider, within the bound.
No kernel may reach another device: no remote copies, remote signals or barrier semaphores. Data moves between devices by JAX's collectives and lax.ppermute only.
A program may use at most 128 MiB of HBM per device.

```python
import math
import jax
import jax.numpy as jnp
from jax import lax

H = 20
HD = 128
QD = 128
QUARTERS = 4
REACH = 5
FRAMES = 4
TOKENS = 2048
HC = 2560
N_TM = 16


def paired_rows(key):
    base = jnp.clip(jax.random.normal(jax.random.fold_in(key, 101), (TOKENS, H * HD), jnp.float32), -6.0, 6.0)
    fresh = jnp.clip(jax.random.normal(jax.random.fold_in(key, 202), (TOKENS, H * HD), jnp.float32), -6.0, 6.0)
    key_rows = base
    query_rows = fresh
    return (query_rows, key_rows)


def draw_queries(key, part):
    return paired_rows(key)[0].astype(jnp.bfloat16)


def draw_keys(key, part):
    return paired_rows(key)[1].astype(jnp.bfloat16)


def draw_frame_keep(key, part):
    codes = jax.random.randint(jax.random.fold_in(key, 303), (FRAMES, 3), 0, 4)
    kept_codes = (codes < 3).astype(jnp.int32)
    column = jnp.arange(3)[None, :]
    return jnp.where(column == 1, 1, kept_codes).astype(jnp.int32)


def draw_band_window(key, part):
    lowest = QD // 2 + 1
    picks = jax.random.randint(jax.random.fold_in(key, 404), (FRAMES,), lowest, QD + 1)
    chosen = jax.random.randint(jax.random.fold_in(key, 405), (), 0, FRAMES)
    frame_ids = jnp.arange(FRAMES)
    picks = jnp.where(frame_ids == chosen, QD, picks)
    picks = jnp.where(frame_ids == (chosen + 1) % FRAMES, lowest, picks)
    return picks.astype(jnp.int32)


def block_scale(rng, shape, split, smallest, top_value):
    def one(dim, shards_of):
        draws = jax.random.uniform(jax.random.fold_in(jax.random.fold_in(rng, 6), dim), (shards_of,), jnp.float32, smallest / len(split), top_value / len(split))
        return jnp.repeat(jnp.exp(draws), shape[dim] // shards_of).reshape((-1,) + (1,) * (len(shape) - dim - 1))

    level = one(*split[0])
    for cut in split[1:]:
        level = level * one(*cut)
    return level


def normal_values(stream_key, shape, spread, reach, pieces=(), kind=jnp.bfloat16):
    values = spread * jax.random.normal(stream_key, shape, jnp.float32)
    if pieces:
        values = values * block_scale(stream_key, shape, pieces, -0.22, 0.18)
    return jnp.clip(values, -reach, reach).astype(kind)


def setup_inputs(seed: int = 0, part: int = 0) -> dict:
    key_list = jax.random.split(jax.random.key(seed), 7)
    part_splits = jax.random.split(jax.random.fold_in(key_list[6], part), 7)
    queries = draw_queries(jax.random.fold_in(jax.random.fold_in(key_list[6], part), 71), part)
    keys = draw_keys(jax.random.fold_in(jax.random.fold_in(key_list[6], part), 71), part)
    values = normal_values(part_splits[2], (TOKENS, HC), 1.0, 6.0, ((0, 16),))
    out_grad = normal_values(part_splits[3], (TOKENS, HC), 1.0, 6.0, ((0, 16),))
    frame_keep = draw_frame_keep(jax.random.fold_in(jax.random.fold_in(key_list[6], part), 71), part)
    band_window = draw_band_window(jax.random.fold_in(jax.random.fold_in(key_list[6], part), 71), part)
    return {"queries": queries, "keys": keys, "values": values, "out_grad": out_grad, "frame_keep": frame_keep, "band_window": band_window}


def allowed(query_rows, key_rows, frame_keep, band_window, frame_len):
    frame_count = frame_keep.shape[0]
    query_frame = jnp.floor_divide(query_rows, frame_len)
    key_frame = jnp.floor_divide(key_rows, frame_len)
    query_place = query_rows - query_frame * frame_len
    key_place = key_rows - key_frame * frame_len
    query_inside = (query_rows >= 0) & (query_rows < frame_count * frame_len)
    key_inside = (key_rows >= 0) & (key_rows < frame_count * frame_len)
    inside = query_inside[:, None] & key_inside[None, :]
    onehot = (query_frame[:, None] == jnp.arange(frame_count, dtype=jnp.int32)[None, :]).astype(jnp.int32)
    keep_rows = lax.optimization_barrier(jnp.sum(onehot[:, :, None] * frame_keep[None, :, :], axis=1))
    window_rows = lax.optimization_barrier(jnp.sum(onehot * band_window[None, :], axis=1))
    frame_gap = key_frame[None, :] - query_frame[:, None]
    kept_pair = jnp.zeros(frame_gap.shape, jnp.int32)
    for column in range(3):
        kept_pair = kept_pair + jnp.where(frame_gap == column - 1, keep_rows[:, column:column + 1], 0)
    place_gap = jnp.abs(query_place[:, None] - key_place[None, :])
    nearby = (frame_gap == 0) | (place_gap <= window_rows[:, None])
    return inside & (kept_pair > 0) & nearby

def reference(queries, keys, values, out_grad, frame_keep, band_window):
    frame_len = QUARTERS * QD
    block_count = 2 * REACH + 1
    extent = block_count * QD
    margin = REACH * QD
    inv_root = 1.0 / math.sqrt(HD)
    padded_keys = jnp.pad(keys, ((margin, margin), (0, 0)))
    padded_values = jnp.pad(values, ((margin, margin), (0, 0)))
    span_rows = jnp.arange(extent, dtype=jnp.int32)
    own_rows = jnp.arange(QD, dtype=jnp.int32)

    def visit_block(carry, device):
        key_acc, value_acc = carry
        first_row = (device * QD).astype(jnp.int32)
        query_block = lax.dynamic_slice_in_dim(queries, first_row, QD, 0)
        grad_block = lax.dynamic_slice_in_dim(out_grad, first_row, QD, 0)
        key_block = lax.dynamic_slice_in_dim(padded_keys, first_row, extent, 0)
        value_block = lax.dynamic_slice_in_dim(padded_values, first_row, extent, 0)
        key_rows = first_row - margin + span_rows
        pair_mask = allowed(first_row + own_rows, key_rows, frame_keep, band_window, frame_len)
        query_heads = query_block.astype(jnp.float32).reshape(QD, H, HD)
        grad_heads = grad_block.astype(jnp.float32).reshape(QD, H, HD)
        key_heads = key_block.astype(jnp.float32).reshape(-1, H, HD)
        value_heads = value_block.astype(jnp.float32).reshape(-1, H, HD)
        scores = jnp.einsum('qhd,khd->hqk', query_heads, key_heads) * inv_root
        masked = jnp.where(pair_mask[None], scores, -1e+30)
        highest = lax.optimization_barrier(jnp.max(masked, axis=2, keepdims=True))
        total_mass = lax.optimization_barrier(jnp.sum(jnp.exp(masked - highest), axis=2, keepdims=True))
        log_total = highest + jnp.log(total_mass)
        attn_prob = jnp.exp(masked - log_total)
        prob_low = lax.optimization_barrier(attn_prob.astype(jnp.bfloat16)).astype(jnp.float32)
        attended = jnp.einsum('hqk,khd->qhd', prob_low, value_heads)
        delta_sum = lax.optimization_barrier(jnp.sum(grad_heads * attended, axis=2))
        prob_grad = jnp.einsum('qhd,khd->hqk', grad_heads, value_heads)
        score_grad = lax.optimization_barrier((attn_prob * (prob_grad - delta_sum.T[:, :, None])).astype(jnp.bfloat16)).astype(jnp.float32)
        query_grad = (jnp.einsum('hqk,khd->qhd', score_grad, key_heads) * inv_root).reshape(QD, H * HD).astype(jnp.bfloat16)
        key_part = (jnp.einsum('hqk,qhd->khd', score_grad, query_heads) * inv_root).reshape(-1, H * HD)
        value_part = jnp.einsum('hqk,qhd->khd', prob_low, grad_heads).reshape(-1, H * HD)
        key_part = lax.optimization_barrier(key_part.astype(jnp.bfloat16)).astype(jnp.float32)
        value_part = lax.optimization_barrier(value_part.astype(jnp.bfloat16)).astype(jnp.float32)
        key_acc = lax.dynamic_update_slice_in_dim(key_acc, lax.dynamic_slice_in_dim(key_acc, first_row, extent, 0) + key_part, first_row, 0)
        value_acc = lax.dynamic_update_slice_in_dim(value_acc, lax.dynamic_slice_in_dim(value_acc, first_row, extent, 0) + value_part, first_row, 0)
        return ((key_acc, value_acc), query_grad)
    empty_acc = jnp.zeros((TOKENS + 2 * margin, H * HD), jnp.float32)
    (key_acc, value_acc), query_parts = lax.scan(visit_block, (empty_acc, empty_acc), jnp.arange(N_TM, dtype=jnp.int32))
    query_grad = query_parts.reshape(TOKENS, H * HD)
    key_grad = key_acc[margin:margin + TOKENS].astype(jnp.bfloat16)
    value_grad = value_acc[margin:margin + TOKENS].astype(jnp.bfloat16)
    return (query_grad, key_grad, value_grad)
```

```python
import math

import jax
import jax.numpy as jnp
from jax import lax
from jax.sharding import PartitionSpec as P

HD = 128
QUARTERS = 4


def send(value, pairs):
    return lax.ppermute(value, "tm", pairs)


def pairs_of(count, target):
    pairs = []
    for source in range(count):
        dest = target(source)
        if dest is not None and 0 <= dest < count:
            pairs.append((source, dest))
    return pairs


def route(count):
    core = pairs_of(count, lambda t: t ^ 1)
    cross = pairs_of(count, lambda t: t ^ 2)
    down = pairs_of(count, lambda t: t - QUARTERS)
    up = pairs_of(count, lambda t: t + QUARTERS)

    def diag(step):
        def target(t):
            q = t % QUARTERS
            if q == 0:
                return t + step * QUARTERS + 1
            if q == QUARTERS - 1:
                return t + step * QUARTERS - 1
            return None

        return pairs_of(count, target)

    diag_up = diag(1)
    diag_down = diag(-1)
    back = lambda pairs: [(dest, source) for source, dest in pairs]
    return core, cross, down, up, diag_up, diag_down, back


def allowed(query_rows, key_rows, frame_keep, band_window, frame_len):
    frame_count = frame_keep.shape[0]
    query_frame = jnp.floor_divide(query_rows, frame_len)
    key_frame = jnp.floor_divide(key_rows, frame_len)
    query_place = query_rows - query_frame * frame_len
    key_place = key_rows - key_frame * frame_len
    query_inside = (query_rows >= 0) & (query_rows < frame_count * frame_len)
    key_inside = (key_rows >= 0) & (key_rows < frame_count * frame_len)
    inside = query_inside[:, None] & key_inside[None, :]
    onehot = (query_frame[:, None] == jnp.arange(frame_count, dtype=jnp.int32)[None, :]).astype(
        jnp.int32
    )
    keep_rows = jnp.sum(onehot[:, :, None] * frame_keep[None, :, :], axis=1)
    window_rows = jnp.sum(onehot * band_window[None, :], axis=1)
    frame_gap = key_frame[None, :] - query_frame[:, None]
    kept_pair = jnp.zeros(frame_gap.shape, jnp.int32)
    for column in range(3):
        kept_pair = kept_pair + jnp.where(
            frame_gap == column - 1, keep_rows[:, column : column + 1], 0
        )
    place_gap = jnp.abs(query_place[:, None] - key_place[None, :])
    nearby = (frame_gap == 0) | (place_gap <= window_rows[:, None])
    return inside & (kept_pair > 0) & nearby


def body(queries, keys, values, out_grad, frame_keep, band_window):
    rows_own, channel_total = queries.shape
    head_total = channel_total // HD
    group_heads = 4
    group_width = group_heads * HD
    frame_len = QUARTERS * rows_own
    inv_root = 1.0 / math.sqrt(HD)
    count = lax.axis_size("tm")
    core, cross, down, up, diag_up, diag_down, back = route(count)
    device = lax.axis_index("tm")
    quarter = device % QUARTERS
    partner = device ^ 1

    own = jnp.stack([keys, values])
    from_core = send(own, core)
    from_cross = send(own, cross)
    from_below = send(own, up)
    from_above = send(own, down)
    relayed = send(jnp.stack([from_cross, from_below, from_above]), core)
    diag_from_below = send(from_cross, diag_up)
    diag_from_above = send(from_cross, diag_down)
    slots = [own, from_core, from_cross, from_below, from_above,
             relayed[0], relayed[1], relayed[2], diag_from_below, diag_from_above]
    middle = (quarter == 1) | (quarter == 2)
    diag_quarter = QUARTERS - 1 - quarter
    absent = jnp.int32(-(1 << 20))
    sources = [
        device,
        partner,
        device ^ 2,
        device - QUARTERS,
        device + QUARTERS,
        device ^ 3,
        partner - QUARTERS,
        partner + QUARTERS,
        jnp.where(middle, device - quarter - QUARTERS + diag_quarter, absent),
        jnp.where(middle, device - quarter + QUARTERS + diag_quarter, absent),
    ]
    base_rows = jnp.arange(rows_own, dtype=jnp.int32)
    far_rows = jnp.concatenate([source * rows_own + base_rows for source in sources])
    own_rows = device * rows_own + base_rows
    key_all = jnp.concatenate([member[0] for member in slots])
    value_all = jnp.concatenate([member[1] for member in slots])
    forward_mask = allowed(own_rows, far_rows, frame_keep, band_window, frame_len)
    query_parts = []
    key_parts = []
    value_parts = []
    for group_index in range(head_total // group_heads):
        lower = group_index * group_width
        upper = lower + group_width
        query_heads = queries[:, lower:upper].reshape(rows_own, group_heads, HD)
        grad_heads = out_grad[:, lower:upper].reshape(rows_own, group_heads, HD)
        key_heads = key_all[:, lower:upper].reshape(-1, group_heads, HD)
        value_heads = value_all[:, lower:upper].reshape(-1, group_heads, HD)
        scores = (
            jnp.einsum("qhd,khd->hqk", query_heads, key_heads, preferred_element_type=jnp.float32)
            * inv_root
        )
        masked = jnp.where(forward_mask[None], scores, -1e30)
        highest = jnp.max(masked, axis=2, keepdims=True)
        total_mass = jnp.sum(jnp.exp(masked - highest), axis=2, keepdims=True)
        log_total = highest + jnp.log(total_mass)
        attn_prob = jnp.exp(masked - log_total)
        prob_low = attn_prob.astype(jnp.bfloat16)
        attended = jnp.einsum(
            "hqk,khd->qhd", prob_low, value_heads, preferred_element_type=jnp.float32
        )
        delta_sum = jnp.sum(grad_heads.astype(jnp.float32) * attended, axis=2)
        prob_grad = jnp.einsum(
            "qhd,khd->hqk", grad_heads, value_heads, preferred_element_type=jnp.float32
        )
        score_grad = (attn_prob * (prob_grad - delta_sum.T[:, :, None])).astype(jnp.bfloat16)
        query_part = (
            jnp.einsum("hqk,khd->qhd", score_grad, key_heads, preferred_element_type=jnp.float32)
            * inv_root
        )
        query_parts.append(query_part.reshape(rows_own, group_width))
        key_part = (
            jnp.einsum("hqk,qhd->khd", score_grad, query_heads, preferred_element_type=jnp.float32)
            * inv_root
        )
        value_part = jnp.einsum(
            "hqk,qhd->khd", prob_low, grad_heads, preferred_element_type=jnp.float32
        )
        key_parts.append(key_part.reshape(-1, group_width).astype(jnp.bfloat16))
        value_parts.append(value_part.reshape(-1, group_width).astype(jnp.bfloat16))
    query_grad = jnp.concatenate(query_parts, axis=1).astype(jnp.bfloat16)
    partials = jnp.stack([jnp.concatenate(key_parts, axis=1), jnp.concatenate(value_parts, axis=1)])
    part = [partials[:, slot * rows_own : (slot + 1) * rows_own] for slot in range(len(slots))]
    wide = lambda tensor: tensor.astype(jnp.float32)
    to_partner = send(jnp.stack([part[1], part[5], part[6], part[7]]), core)
    diag_back_below = send(part[8], back(diag_up))
    diag_back_above = send(part[9], back(diag_down))
    cross_sum = wide(part[2]) + wide(to_partner[1]) + wide(diag_back_below) + wide(diag_back_above)
    below_sum = wide(part[3]) + wide(to_partner[2])
    above_sum = wide(part[4]) + wide(to_partner[3])
    got_cross = send(cross_sum.astype(jnp.bfloat16), cross)
    got_below = send(below_sum.astype(jnp.bfloat16), down)
    got_above = send(above_sum.astype(jnp.bfloat16), up)
    summed = wide(part[0]) + wide(to_partner[0]) + wide(got_cross) + wide(got_below) + wide(got_above)
    key_grad = summed[0].astype(jnp.bfloat16)
    value_grad = summed[1].astype(jnp.bfloat16)
    return (query_grad, key_grad, value_grad)


def solution(mesh):
    placed = (
        P(("group", "tm"), None),
        P(("group", "tm"), None),
        P(("group", "tm"), None),
        P(("group", "tm"), None),
        P("group", None),
        P("group"),
    )
    return jax.shard_map(
        body,
        mesh=mesh,
        in_specs=placed,
        out_specs=(P(("group", "tm"), None), P(("group", "tm"), None), P(("group", "tm"), None)),
        check_vma=False,
    )
```

```python
import math

import jax
import jax.numpy as jnp
from jax import lax
from jax.experimental import pallas as pl
from jax.sharding import PartitionSpec as P

HD = 128
QUARTERS = 4


def send(value, pairs):
    return lax.ppermute(value, "tm", pairs)


def pairs_of(count, target):
    pairs = []
    for source in range(count):
        dest = target(source)
        if dest is not None and 0 <= dest < count:
            pairs.append((source, dest))
    return pairs


def route(count):
    core = pairs_of(count, lambda t: t ^ 1)
    cross = pairs_of(count, lambda t: t ^ 2)
    down = pairs_of(count, lambda t: t - QUARTERS)
    up = pairs_of(count, lambda t: t + QUARTERS)

    def diag(step):
        def target(t):
            q = t % QUARTERS
            if q == 0:
                return t + step * QUARTERS + 1
            if q == QUARTERS - 1:
                return t + step * QUARTERS - 1
            return None

        return pairs_of(count, target)

    diag_up = diag(1)
    diag_down = diag(-1)
    back = lambda pairs: [(dest, source) for source, dest in pairs]
    return core, cross, down, up, diag_up, diag_down, back


def allowed(query_rows, key_rows, frame_keep, band_window, frame_len):
    frame_count = frame_keep.shape[0]
    query_frame = jnp.floor_divide(query_rows, frame_len)
    key_frame = jnp.floor_divide(key_rows, frame_len)
    query_place = query_rows - query_frame * frame_len
    key_place = key_rows - key_frame * frame_len
    query_inside = (query_rows >= 0) & (query_rows < frame_count * frame_len)
    key_inside = (key_rows >= 0) & (key_rows < frame_count * frame_len)
    inside = query_inside[:, None] & key_inside[None, :]
    onehot = (query_frame[:, None] == jnp.arange(frame_count, dtype=jnp.int32)[None, :]).astype(
        jnp.int32
    )
    keep_rows = jnp.sum(onehot[:, :, None] * frame_keep[None, :, :], axis=1)
    window_rows = jnp.sum(onehot * band_window[None, :], axis=1)
    frame_gap = key_frame[None, :] - query_frame[:, None]
    kept_pair = jnp.zeros(frame_gap.shape, jnp.int32)
    for column in range(3):
        kept_pair = kept_pair + jnp.where(
            frame_gap == column - 1, keep_rows[:, column : column + 1], 0
        )
    place_gap = jnp.abs(query_place[:, None] - key_place[None, :])
    nearby = (frame_gap == 0) | (place_gap <= window_rows[:, None])
    return inside & (kept_pair > 0) & nearby


def attention_backward(mask, queries, out_grad, inputs, slot_in, out_lead, slot_out, inv_root):
    rows, channels = queries.shape
    heads = channels // HD
    slots = len(slot_in)
    n_in = len(inputs)

    def kernel(mask_ref, q_ref, g_ref, *refs):
        in_refs = refs[:n_in]
        dq_ref = refs[n_in]
        out_refs = refs[n_in + 1 :]
        k = jnp.concatenate([in_refs[i][lead + (0,)] for i, lead in slot_in], axis=0)
        v = jnp.concatenate([in_refs[i][lead + (1,)] for i, lead in slot_in], axis=0)
        q = q_ref[...]
        g = g_ref[...]
        nt = (((1,), (1,)), ((), ()))
        tn = (((0,), (0,)), ((), ()))
        scores = lax.dot_general(q, k, nt, preferred_element_type=jnp.float32) * inv_root
        masked = jnp.where(mask_ref[...] != 0, scores, -1e30)
        highest = jnp.max(masked, axis=1, keepdims=True)
        total_mass = jnp.sum(jnp.exp(masked - highest), axis=1, keepdims=True)
        log_total = highest + jnp.log(total_mass)
        prob = jnp.exp(masked - log_total)
        prob_low = prob.astype(jnp.bfloat16)
        attended = jnp.dot(prob_low, v, preferred_element_type=jnp.float32)
        delta = jnp.sum(g.astype(jnp.float32) * attended, axis=1, keepdims=True)
        prob_grad = lax.dot_general(g, v, nt, preferred_element_type=jnp.float32)
        score_grad = (prob * (prob_grad - delta)).astype(jnp.bfloat16)
        dq = jnp.dot(score_grad, k, preferred_element_type=jnp.float32) * inv_root
        dq_ref[...] = dq.astype(dq_ref.dtype)
        dk = lax.dot_general(score_grad, q, tn, preferred_element_type=jnp.float32) * inv_root
        dv = lax.dot_general(prob_low, g, tn, preferred_element_type=jnp.float32)
        for slot, (i, lead) in enumerate(slot_out):
            out_refs[i][lead + (0,)] = dk[slot * rows : (slot + 1) * rows].astype(jnp.bfloat16)
            out_refs[i][lead + (1,)] = dv[slot * rows : (slot + 1) * rows].astype(jnp.bfloat16)

    def head_spec(lead_shape):
        zeros = (0,) * len(lead_shape)
        return pl.BlockSpec(lead_shape + (2, rows, HD), lambda h: zeros + (0, 0, h))

    in_specs = [
        pl.BlockSpec((rows, slots * rows), lambda h: (0, 0)),
        pl.BlockSpec((rows, HD), lambda h: (0, h)),
        pl.BlockSpec((rows, HD), lambda h: (0, h)),
    ] + [head_spec(tuple(x.shape[:-3])) for x in inputs]
    out_specs = [pl.BlockSpec((rows, HD), lambda h: (0, h))] + [head_spec(lead) for lead in out_lead]
    out_shape = [jax.ShapeDtypeStruct((rows, channels), jnp.bfloat16)] + [
        jax.ShapeDtypeStruct(lead + (2, rows, channels), jnp.bfloat16) for lead in out_lead
    ]
    results = pl.pallas_call(
        kernel,
        grid=(heads,),
        in_specs=in_specs,
        out_specs=out_specs,
        out_shape=out_shape,
    )(mask, queries, out_grad, *inputs)
    return results[0], results[1:]


def body(queries, keys, values, out_grad, frame_keep, band_window):
    rows_own, channel_total = queries.shape
    frame_len = QUARTERS * rows_own
    inv_root = 1.0 / math.sqrt(HD)
    count = lax.axis_size("tm")
    core, cross, down, up, diag_up, diag_down, back = route(count)
    device = lax.axis_index("tm")
    quarter = device % QUARTERS
    partner = device ^ 1

    own = jnp.stack([keys, values])
    from_core = send(own, core)
    from_cross = send(own, cross)
    from_below = send(own, up)
    from_above = send(own, down)
    relayed = send(jnp.stack([from_cross, from_below, from_above]), core)
    diag_from_below = send(from_cross, diag_up)
    diag_from_above = send(from_cross, diag_down)
    slots = [own, from_core, from_cross, from_below, from_above,
             relayed[0], relayed[1], relayed[2], diag_from_below, diag_from_above]
    middle = (quarter == 1) | (quarter == 2)
    diag_quarter = QUARTERS - 1 - quarter
    absent = jnp.int32(-(1 << 20))
    sources = [
        device,
        partner,
        device ^ 2,
        device - QUARTERS,
        device + QUARTERS,
        device ^ 3,
        partner - QUARTERS,
        partner + QUARTERS,
        jnp.where(middle, device - quarter - QUARTERS + diag_quarter, absent),
        jnp.where(middle, device - quarter + QUARTERS + diag_quarter, absent),
    ]
    base_rows = jnp.arange(rows_own, dtype=jnp.int32)
    far_rows = jnp.concatenate([source * rows_own + base_rows for source in sources])
    own_rows = device * rows_own + base_rows
    forward_mask = allowed(own_rows, far_rows, frame_keep, band_window, frame_len).astype(jnp.int32)
    inputs = [own, from_core, from_cross, from_below, from_above, relayed, diag_from_below, diag_from_above]
    slot_in = [(0, ()), (1, ()), (2, ()), (3, ()), (4, ()), (5, (0,)), (5, (1,)), (5, (2,)), (6, ()), (7, ())]
    out_lead = [(), (4,), (), (), (), (), ()]
    slot_out = [(0, ()), (1, (0,)), (2, ()), (3, ()), (4, ()), (1, (1,)), (1, (2,)), (1, (3,)), (5, ()), (6, ())]
    query_grad, outs = attention_backward(
        forward_mask, queries, out_grad, inputs, slot_in, out_lead, slot_out, inv_root
    )
    own_part, to_core, cross_part, below_part, above_part, diag_b_part, diag_a_part = outs
    wide = lambda tensor: tensor.astype(jnp.float32)
    to_partner = send(to_core, core)
    diag_back_below = send(diag_b_part, back(diag_up))
    diag_back_above = send(diag_a_part, back(diag_down))
    cross_sum = wide(cross_part) + wide(to_partner[1]) + wide(diag_back_below) + wide(diag_back_above)
    below_sum = wide(below_part) + wide(to_partner[2])
    above_sum = wide(above_part) + wide(to_partner[3])
    got_cross = send(cross_sum.astype(jnp.bfloat16), cross)
    got_below = send(below_sum.astype(jnp.bfloat16), down)
    got_above = send(above_sum.astype(jnp.bfloat16), up)
    summed = wide(own_part) + wide(to_partner[0]) + wide(got_cross) + wide(got_below) + wide(got_above)
    key_grad = summed[0].astype(jnp.bfloat16)
    value_grad = summed[1].astype(jnp.bfloat16)
    return (query_grad, key_grad, value_grad)


def solution(mesh):
    placed = (
        P(("group", "tm"), None),
        P(("group", "tm"), None),
        P(("group", "tm"), None),
        P(("group", "tm"), None),
        P("group", None),
        P("group"),
    )
    return jax.shard_map(
        body,
        mesh=mesh,
        in_specs=placed,
        out_specs=(P(("group", "tm"), None), P(("group", "tm"), None), P(("group", "tm"), None)),
        check_vma=False,
    )
```

```python
import math

import jax
import jax.numpy as jnp
from jax import lax
from jax.experimental import pallas as pl
from jax.sharding import PartitionSpec as P

HD = 128
QUARTERS = 4
CHUNKS = 2


def send(value, pairs):
    return lax.ppermute(value, "tm", pairs)


def pairs_of(count, target):
    pairs = []
    for source in range(count):
        dest = target(source)
        if dest is not None and 0 <= dest < count:
            pairs.append((source, dest))
    return pairs


def route(count):
    core = pairs_of(count, lambda t: t ^ 1)
    cross = pairs_of(count, lambda t: t ^ 2)
    down = pairs_of(count, lambda t: t - QUARTERS)
    up = pairs_of(count, lambda t: t + QUARTERS)

    def diag(step):
        def target(t):
            q = t % QUARTERS
            if q == 0:
                return t + step * QUARTERS + 1
            if q == QUARTERS - 1:
                return t + step * QUARTERS - 1
            return None

        return pairs_of(count, target)

    diag_up = diag(1)
    diag_down = diag(-1)
    back = lambda pairs: [(dest, source) for source, dest in pairs]
    return core, cross, down, up, diag_up, diag_down, back


def allowed(query_rows, key_rows, frame_keep, band_window, frame_len):
    frame_count = frame_keep.shape[0]
    query_frame = jnp.floor_divide(query_rows, frame_len)
    key_frame = jnp.floor_divide(key_rows, frame_len)
    query_place = query_rows - query_frame * frame_len
    key_place = key_rows - key_frame * frame_len
    query_inside = (query_rows >= 0) & (query_rows < frame_count * frame_len)
    key_inside = (key_rows >= 0) & (key_rows < frame_count * frame_len)
    inside = query_inside[:, None] & key_inside[None, :]
    onehot = (query_frame[:, None] == jnp.arange(frame_count, dtype=jnp.int32)[None, :]).astype(
        jnp.int32
    )
    keep_rows = jnp.sum(onehot[:, :, None] * frame_keep[None, :, :], axis=1)
    window_rows = jnp.sum(onehot * band_window[None, :], axis=1)
    frame_gap = key_frame[None, :] - query_frame[:, None]
    kept_pair = jnp.zeros(frame_gap.shape, jnp.int32)
    for column in range(3):
        kept_pair = kept_pair + jnp.where(
            frame_gap == column - 1, keep_rows[:, column : column + 1], 0
        )
    place_gap = jnp.abs(query_place[:, None] - key_place[None, :])
    nearby = (frame_gap == 0) | (place_gap <= window_rows[:, None])
    return inside & (kept_pair > 0) & nearby


def attention_backward(mask, queries, out_grad, inputs, slot_in, out_lead, slot_out, inv_root, offset):
    rows, channels = inputs[0].shape[-2:]
    heads = channels // HD
    slots = len(slot_in)
    n_in = len(inputs)

    def kernel(mask_ref, q_ref, g_ref, *refs):
        in_refs = refs[:n_in]
        dq_ref = refs[n_in]
        out_refs = refs[n_in + 1 :]
        k = jnp.concatenate([in_refs[i][lead + (0,)] for i, lead in slot_in], axis=0)
        v = jnp.concatenate([in_refs[i][lead + (1,)] for i, lead in slot_in], axis=0)
        q = q_ref[...]
        g = g_ref[...]
        nt = (((1,), (1,)), ((), ()))
        tn = (((0,), (0,)), ((), ()))
        scores = lax.dot_general(q, k, nt, preferred_element_type=jnp.float32) * inv_root
        masked = jnp.where(mask_ref[...] != 0, scores, -1e30)
        highest = jnp.max(masked, axis=1, keepdims=True)
        total_mass = jnp.sum(jnp.exp(masked - highest), axis=1, keepdims=True)
        log_total = highest + jnp.log(total_mass)
        prob = jnp.exp(masked - log_total)
        prob_low = prob.astype(jnp.bfloat16)
        attended = jnp.dot(prob_low, v, preferred_element_type=jnp.float32)
        delta = jnp.sum(g.astype(jnp.float32) * attended, axis=1, keepdims=True)
        prob_grad = lax.dot_general(g, v, nt, preferred_element_type=jnp.float32)
        score_grad = (prob * (prob_grad - delta)).astype(jnp.bfloat16)
        dq = jnp.dot(score_grad, k, preferred_element_type=jnp.float32) * inv_root
        dq_ref[...] = dq.astype(dq_ref.dtype)
        dk = lax.dot_general(score_grad, q, tn, preferred_element_type=jnp.float32) * inv_root
        dv = lax.dot_general(prob_low, g, tn, preferred_element_type=jnp.float32)
        for slot, (i, lead) in enumerate(slot_out):
            out_refs[i][lead + (0,)] = dk[slot * rows : (slot + 1) * rows].astype(jnp.bfloat16)
            out_refs[i][lead + (1,)] = dv[slot * rows : (slot + 1) * rows].astype(jnp.bfloat16)

    def head_spec(lead_shape):
        zeros = (0,) * len(lead_shape)
        return pl.BlockSpec(lead_shape + (2, rows, HD), lambda h: zeros + (0, 0, h))

    in_specs = [
        pl.BlockSpec((rows, slots * rows), lambda h: (0, 0)),
        pl.BlockSpec((rows, HD), lambda h: (0, h + offset)),
        pl.BlockSpec((rows, HD), lambda h: (0, h + offset)),
    ] + [head_spec(tuple(x.shape[:-3])) for x in inputs]
    out_specs = [pl.BlockSpec((rows, HD), lambda h: (0, h))] + [head_spec(lead) for lead in out_lead]
    out_shape = [jax.ShapeDtypeStruct((rows, channels), jnp.bfloat16)] + [
        jax.ShapeDtypeStruct(lead + (2, rows, channels), jnp.bfloat16) for lead in out_lead
    ]
    results = pl.pallas_call(
        kernel,
        grid=(heads,),
        in_specs=in_specs,
        out_specs=out_specs,
        out_shape=out_shape,
        cost_estimate=pl.CostEstimate(
            flops=12 * heads * rows * slots * rows * HD,
            transcendentals=2 * heads * rows * slots * rows,
            bytes_accessed=2 * 4 * slots * rows * channels + 6 * rows * channels + 4 * rows * slots * rows,
        ),
    )(mask, queries, out_grad, *inputs)
    return results[0], results[1:]


def exchange_chunk(forward_mask, queries, out_grad, keys, values, head_offset, inv_root, count):
    core, cross, down, up, diag_up, diag_down, back = route(count)
    own = jnp.stack([keys, values])
    from_core = send(own, core)
    from_cross = send(own, cross)
    from_below = send(own, up)
    from_above = send(own, down)
    relayed = send(jnp.stack([from_cross, from_below, from_above]), core)
    diag_from_below = send(from_cross, diag_up)
    diag_from_above = send(from_cross, diag_down)
    inputs = [own, from_core, from_cross, from_below, from_above, relayed, diag_from_below, diag_from_above]
    slot_in = [(0, ()), (1, ()), (2, ()), (3, ()), (4, ()), (5, (0,)), (5, (1,)), (5, (2,)), (6, ()), (7, ())]
    out_lead = [(), (4,), (), (), (), (), ()]
    slot_out = [(0, ()), (1, (0,)), (2, ()), (3, ()), (4, ()), (1, (1,)), (1, (2,)), (1, (3,)), (5, ()), (6, ())]
    query_grad, outs = attention_backward(
        forward_mask, queries, out_grad, inputs, slot_in, out_lead, slot_out, inv_root, head_offset
    )
    own_part, to_core, cross_part, below_part, above_part, diag_b_part, diag_a_part = outs
    wide = lambda tensor: tensor.astype(jnp.float32)
    to_partner = send(to_core, core)
    diag_back_below = send(diag_b_part, back(diag_up))
    diag_back_above = send(diag_a_part, back(diag_down))
    cross_sum = wide(cross_part) + wide(to_partner[1]) + wide(diag_back_below) + wide(diag_back_above)
    below_sum = wide(below_part) + wide(to_partner[2])
    above_sum = wide(above_part) + wide(to_partner[3])
    got_cross = send(cross_sum.astype(jnp.bfloat16), cross)
    got_below = send(below_sum.astype(jnp.bfloat16), down)
    got_above = send(above_sum.astype(jnp.bfloat16), up)
    summed = wide(own_part) + wide(to_partner[0]) + wide(got_cross) + wide(got_below) + wide(got_above)
    return query_grad, summed[0].astype(jnp.bfloat16), summed[1].astype(jnp.bfloat16)


def body(queries, keys, values, out_grad, frame_keep, band_window):
    rows_own, channel_total = queries.shape
    frame_len = QUARTERS * rows_own
    inv_root = 1.0 / math.sqrt(HD)
    count = lax.axis_size("tm")
    device = lax.axis_index("tm")
    quarter = device % QUARTERS
    partner = device ^ 1

    middle = (quarter == 1) | (quarter == 2)
    diag_quarter = QUARTERS - 1 - quarter
    absent = jnp.int32(-(1 << 20))
    sources = [
        device,
        partner,
        device ^ 2,
        device - QUARTERS,
        device + QUARTERS,
        device ^ 3,
        partner - QUARTERS,
        partner + QUARTERS,
        jnp.where(middle, device - quarter - QUARTERS + diag_quarter, absent),
        jnp.where(middle, device - quarter + QUARTERS + diag_quarter, absent),
    ]
    base_rows = jnp.arange(rows_own, dtype=jnp.int32)
    far_rows = jnp.concatenate([source * rows_own + base_rows for source in sources])
    own_rows = device * rows_own + base_rows
    forward_mask = allowed(own_rows, far_rows, frame_keep, band_window, frame_len).astype(jnp.int32)
    heads = channel_total // HD
    chunk_heads = heads // CHUNKS if heads % CHUNKS == 0 else heads
    width = chunk_heads * HD
    grads = []
    for first in range(0, channel_total, width):
        grads.append(
            exchange_chunk(
                forward_mask, queries, out_grad, keys[:, first : first + width],
                values[:, first : first + width], first // HD, inv_root, count,
            )
        )
    query_grad = jnp.concatenate([grad[0] for grad in grads], axis=1)
    key_grad = jnp.concatenate([grad[1] for grad in grads], axis=1)
    value_grad = jnp.concatenate([grad[2] for grad in grads], axis=1)
    return (query_grad, key_grad, value_grad)


def solution(mesh):
    placed = (
        P(("group", "tm"), None),
        P(("group", "tm"), None),
        P(("group", "tm"), None),
        P(("group", "tm"), None),
        P("group", None),
        P("group"),
    )
    return jax.shard_map(
        body,
        mesh=mesh,
        in_specs=placed,
        out_specs=(P(("group", "tm"), None), P(("group", "tm"), None), P(("group", "tm"), None)),
        check_vma=False,
    )
```

```python
import math

import jax
import jax.numpy as jnp
from jax import lax
from jax.experimental import pallas as pl
from jax.sharding import PartitionSpec as P

HD = 128
QUARTERS = 4
CHUNKS = 2


def send(value, pairs):
    return lax.ppermute(value, "tm", pairs)


def pairs_of(count, target):
    pairs = []
    for source in range(count):
        dest = target(source)
        if dest is not None and 0 <= dest < count:
            pairs.append((source, dest))
    return pairs


def route(count):
    core = pairs_of(count, lambda t: t ^ 1)
    cross = pairs_of(count, lambda t: t ^ 2)
    down = pairs_of(count, lambda t: t - QUARTERS)
    up = pairs_of(count, lambda t: t + QUARTERS)

    def diag(step):
        def target(t):
            q = t % QUARTERS
            if q == 0:
                return t + step * QUARTERS + 1
            if q == QUARTERS - 1:
                return t + step * QUARTERS - 1
            return None

        return pairs_of(count, target)

    diag_up = diag(1)
    diag_down = diag(-1)
    back = lambda pairs: [(dest, source) for source, dest in pairs]
    return core, cross, down, up, diag_up, diag_down, back


def allowed(query_rows, key_rows, frame_keep, band_window, frame_len):
    frame_count = frame_keep.shape[0]
    query_frame = jnp.floor_divide(query_rows, frame_len)
    key_frame = jnp.floor_divide(key_rows, frame_len)
    query_place = query_rows - query_frame * frame_len
    key_place = key_rows - key_frame * frame_len
    query_inside = (query_rows >= 0) & (query_rows < frame_count * frame_len)
    key_inside = (key_rows >= 0) & (key_rows < frame_count * frame_len)
    inside = query_inside[:, None] & key_inside[None, :]
    onehot = (query_frame[:, None] == jnp.arange(frame_count, dtype=jnp.int32)[None, :]).astype(
        jnp.int32
    )
    keep_rows = jnp.sum(onehot[:, :, None] * frame_keep[None, :, :], axis=1)
    window_rows = jnp.sum(onehot * band_window[None, :], axis=1)
    frame_gap = key_frame[None, :] - query_frame[:, None]
    kept_pair = jnp.zeros(frame_gap.shape, jnp.int32)
    for column in range(3):
        kept_pair = kept_pair + jnp.where(
            frame_gap == column - 1, keep_rows[:, column : column + 1], 0
        )
    place_gap = jnp.abs(query_place[:, None] - key_place[None, :])
    nearby = (frame_gap == 0) | (place_gap <= window_rows[:, None])
    return inside & (kept_pair > 0) & nearby


def attention_backward(mask, queries, out_grad, inputs, slot_in, out_lead, slot_out, inv_root, offset):
    rows, channels = inputs[0].shape[-2:]
    heads = channels // HD
    slots = len(slot_in)
    n_in = len(inputs)

    def kernel(mask_ref, q_ref, g_ref, *refs):
        in_refs = refs[:n_in]
        dq_ref = refs[n_in]
        out_refs = refs[n_in + 1 :]
        k = jnp.concatenate([in_refs[i][lead + (0,)] for i, lead in slot_in], axis=0)
        v = jnp.concatenate([in_refs[i][lead + (1,)] for i, lead in slot_in], axis=0)
        q = q_ref[...]
        g = g_ref[...]
        nt = (((1,), (1,)), ((), ()))
        tn = (((0,), (0,)), ((), ()))
        scores = lax.dot_general(q, k, nt, preferred_element_type=jnp.float32) * inv_root
        masked = jnp.where(mask_ref[...] != 0, scores, -1e30)
        highest = jnp.max(masked, axis=1, keepdims=True)
        total_mass = jnp.sum(jnp.exp(masked - highest), axis=1, keepdims=True)
        log_total = highest + jnp.log(total_mass)
        prob = jnp.exp(masked - log_total)
        prob_low = prob.astype(jnp.bfloat16)
        attended = jnp.dot(prob_low, v, preferred_element_type=jnp.float32)
        delta = jnp.sum(g.astype(jnp.float32) * attended, axis=1, keepdims=True)
        prob_grad = lax.dot_general(g, v, nt, preferred_element_type=jnp.float32)
        score_grad = (prob * (prob_grad - delta)).astype(jnp.bfloat16)
        dq = jnp.dot(score_grad, k, preferred_element_type=jnp.float32) * inv_root
        dq_ref[...] = dq.astype(dq_ref.dtype)
        dk = lax.dot_general(score_grad, q, tn, preferred_element_type=jnp.float32) * inv_root
        dv = lax.dot_general(prob_low, g, tn, preferred_element_type=jnp.float32)
        for slot, (i, lead) in enumerate(slot_out):
            out_refs[i][lead + (0,)] = dk[slot * rows : (slot + 1) * rows].astype(jnp.bfloat16)
            out_refs[i][lead + (1,)] = dv[slot * rows : (slot + 1) * rows].astype(jnp.bfloat16)

    def head_spec(lead_shape):
        zeros = (0,) * len(lead_shape)
        return pl.BlockSpec(lead_shape + (2, rows, HD), lambda h: zeros + (0, 0, h))

    in_specs = [
        pl.BlockSpec((rows, slots * rows), lambda h: (0, 0)),
        pl.BlockSpec((rows, HD), lambda h: (0, h + offset)),
        pl.BlockSpec((rows, HD), lambda h: (0, h + offset)),
    ] + [head_spec(tuple(x.shape[:-3])) for x in inputs]
    out_specs = [pl.BlockSpec((rows, HD), lambda h: (0, h))] + [head_spec(lead) for lead in out_lead]
    out_shape = [jax.ShapeDtypeStruct((rows, channels), jnp.bfloat16)] + [
        jax.ShapeDtypeStruct(lead + (2, rows, channels), jnp.bfloat16) for lead in out_lead
    ]
    results = pl.pallas_call(
        kernel,
        grid=(heads,),
        in_specs=in_specs,
        out_specs=out_specs,
        out_shape=out_shape,
        cost_estimate=pl.CostEstimate(
            flops=12 * heads * rows * slots * rows * HD,
            transcendentals=2 * heads * rows * slots * rows,
            bytes_accessed=2 * 4 * slots * rows * channels + 6 * rows * channels + 4 * rows * slots * rows,
        ),
    )(mask, queries, out_grad, *inputs)
    return results[0], results[1:]


def forward_relay(own, count, after):
    core, cross, down, up, diag_up, diag_down, back = route(count)
    if after is not None:
        own, _ = lax.optimization_barrier((own, after))
    from_core = send(own, core)
    from_cross = send(own, cross)
    from_below = send(own, up)
    from_above = send(own, down)
    return [own, from_core, from_cross, from_below, from_above]


def forward_second(first, count, after):
    core, cross, down, up, diag_up, diag_down, back = route(count)
    own, from_core, from_cross, from_below, from_above = first
    ahead = jnp.stack([from_cross, from_below, from_above])
    if after is not None:
        (ahead, from_cross), _ = lax.optimization_barrier(((ahead, from_cross), after))
    relayed = send(ahead, core)
    diag_from_below = send(from_cross, diag_up)
    diag_from_above = send(from_cross, diag_down)
    return first + [relayed, diag_from_below, diag_from_above]


def chunk_kernel(forward_mask, queries, out_grad, inputs, head_offset, inv_root):
    slot_in = [(0, ()), (1, ()), (2, ()), (3, ()), (4, ()), (5, (0,)), (5, (1,)), (5, (2,)), (6, ()), (7, ())]
    out_lead = [(), (4,), (), (), (), (), ()]
    slot_out = [(0, ()), (1, (0,)), (2, ()), (3, ()), (4, ()), (1, (1,)), (1, (2,)), (1, (3,)), (5, ()), (6, ())]
    return attention_backward(
        forward_mask, queries, out_grad, inputs, slot_in, out_lead, slot_out, inv_root, head_offset
    )


def return_first(outs, count, after):
    core, cross, down, up, diag_up, diag_down, back = route(count)
    own_part, to_core, cross_part, below_part, above_part, diag_b_part, diag_a_part = outs
    if after is not None:
        (to_core, diag_b_part, diag_a_part), _ = lax.optimization_barrier(
            ((to_core, diag_b_part, diag_a_part), after)
        )
    to_partner = send(to_core, core)
    diag_back_below = send(diag_b_part, back(diag_up))
    diag_back_above = send(diag_a_part, back(diag_down))
    return [to_partner, diag_back_below, diag_back_above]


def return_second(outs, first, count, after):
    core, cross, down, up, diag_up, diag_down, back = route(count)
    own_part, to_core, cross_part, below_part, above_part, diag_b_part, diag_a_part = outs
    to_partner, diag_back_below, diag_back_above = first
    wide = lambda tensor: tensor.astype(jnp.float32)
    cross_sum = wide(cross_part) + wide(to_partner[1]) + wide(diag_back_below) + wide(diag_back_above)
    below_sum = wide(below_part) + wide(to_partner[2])
    above_sum = wide(above_part) + wide(to_partner[3])
    sums = (cross_sum.astype(jnp.bfloat16), below_sum.astype(jnp.bfloat16), above_sum.astype(jnp.bfloat16))
    if after is not None:
        sums, _ = lax.optimization_barrier((sums, after))
    got_cross = send(sums[0], cross)
    got_below = send(sums[1], down)
    got_above = send(sums[2], up)
    summed = wide(own_part) + wide(to_partner[0]) + wide(got_cross) + wide(got_below) + wide(got_above)
    return [got_cross, got_below, got_above], summed


def body(queries, keys, values, out_grad, frame_keep, band_window):
    rows_own, channel_total = queries.shape
    frame_len = QUARTERS * rows_own
    inv_root = 1.0 / math.sqrt(HD)
    count = lax.axis_size("tm")
    device = lax.axis_index("tm")
    quarter = device % QUARTERS
    partner = device ^ 1

    middle = (quarter == 1) | (quarter == 2)
    diag_quarter = QUARTERS - 1 - quarter
    absent = jnp.int32(-(1 << 20))
    sources = [
        device,
        partner,
        device ^ 2,
        device - QUARTERS,
        device + QUARTERS,
        device ^ 3,
        partner - QUARTERS,
        partner + QUARTERS,
        jnp.where(middle, device - quarter - QUARTERS + diag_quarter, absent),
        jnp.where(middle, device - quarter + QUARTERS + diag_quarter, absent),
    ]
    base_rows = jnp.arange(rows_own, dtype=jnp.int32)
    far_rows = jnp.concatenate([source * rows_own + base_rows for source in sources])
    own_rows = device * rows_own + base_rows
    forward_mask = allowed(own_rows, far_rows, frame_keep, band_window, frame_len).astype(jnp.int32)
    heads = channel_total // HD
    chunk_heads = heads // CHUNKS if heads % CHUNKS == 0 else heads
    width = chunk_heads * HD
    starts = list(range(0, channel_total, width))
    firsts, seconds, outs, backs, sums, dqs = [], [], [], [], [], []
    for c, first in enumerate(starts):
        own = jnp.stack([keys[:, first : first + width], values[:, first : first + width]])
        firsts.append(forward_relay(own, count, firsts[c - 1][1:] if c else None))
    for c in range(len(starts)):
        seconds.append(forward_second(firsts[c], count, seconds[c - 1][5:] if c else None))
    for c, first in enumerate(starts):
        dq, parts = chunk_kernel(forward_mask, queries, out_grad, seconds[c], first // HD, inv_root)
        dqs.append(dq)
        outs.append(parts)
    for c in range(len(starts)):
        backs.append(return_first(outs[c], count, backs[c - 1] if c else None))
    got = None
    for c in range(len(starts)):
        got, summed = return_second(outs[c], backs[c], count, got)
        sums.append(summed)
    grads = [(dqs[c], sums[c][0].astype(jnp.bfloat16), sums[c][1].astype(jnp.bfloat16)) for c in range(len(starts))]
    query_grad = jnp.concatenate([grad[0] for grad in grads], axis=1)
    key_grad = jnp.concatenate([grad[1] for grad in grads], axis=1)
    value_grad = jnp.concatenate([grad[2] for grad in grads], axis=1)
    return (query_grad, key_grad, value_grad)


def solution(mesh):
    placed = (
        P(("group", "tm"), None),
        P(("group", "tm"), None),
        P(("group", "tm"), None),
        P(("group", "tm"), None),
        P("group", None),
        P("group"),
    )
    return jax.shard_map(
        body,
        mesh=mesh,
        in_specs=placed,
        out_specs=(P(("group", "tm"), None), P(("group", "tm"), None), P(("group", "tm"), None)),
        check_vma=False,
    )
```

```python
import math

import jax
import jax.numpy as jnp
from jax import lax
from jax.experimental import pallas as pl
from jax.sharding import PartitionSpec as P

HD = 128
QUARTERS = 4
CHUNKS = 4


def send(value, pairs):
    return lax.ppermute(value, "tm", pairs)


def pairs_of(count, target):
    pairs = []
    for source in range(count):
        dest = target(source)
        if dest is not None and 0 <= dest < count:
            pairs.append((source, dest))
    return pairs


def route(count):
    core = pairs_of(count, lambda t: t ^ 1)
    cross = pairs_of(count, lambda t: t ^ 2)
    down = pairs_of(count, lambda t: t - QUARTERS)
    up = pairs_of(count, lambda t: t + QUARTERS)

    def diag(step):
        def target(t):
            q = t % QUARTERS
            if q == 0:
                return t + step * QUARTERS + 1
            if q == QUARTERS - 1:
                return t + step * QUARTERS - 1
            return None

        return pairs_of(count, target)

    diag_up = diag(1)
    diag_down = diag(-1)
    back = lambda pairs: [(dest, source) for source, dest in pairs]
    return core, cross, down, up, diag_up, diag_down, back


def allowed(query_rows, key_rows, frame_keep, band_window, frame_len):
    frame_count = frame_keep.shape[0]
    query_frame = jnp.floor_divide(query_rows, frame_len)
    key_frame = jnp.floor_divide(key_rows, frame_len)
    query_place = query_rows - query_frame * frame_len
    key_place = key_rows - key_frame * frame_len
    query_inside = (query_rows >= 0) & (query_rows < frame_count * frame_len)
    key_inside = (key_rows >= 0) & (key_rows < frame_count * frame_len)
    inside = query_inside[:, None] & key_inside[None, :]
    onehot = (query_frame[:, None] == jnp.arange(frame_count, dtype=jnp.int32)[None, :]).astype(
        jnp.int32
    )
    keep_rows = jnp.sum(onehot[:, :, None] * frame_keep[None, :, :], axis=1)
    window_rows = jnp.sum(onehot * band_window[None, :], axis=1)
    frame_gap = key_frame[None, :] - query_frame[:, None]
    kept_pair = jnp.zeros(frame_gap.shape, jnp.int32)
    for column in range(3):
        kept_pair = kept_pair + jnp.where(
            frame_gap == column - 1, keep_rows[:, column : column + 1], 0
        )
    place_gap = jnp.abs(query_place[:, None] - key_place[None, :])
    nearby = (frame_gap == 0) | (place_gap <= window_rows[:, None])
    return inside & (kept_pair > 0) & nearby


def attention_backward(mask, queries, out_grad, inputs, slot_in, out_lead, slot_out, inv_root, offset):
    rows, channels = inputs[0].shape[-2:]
    heads = channels // HD
    slots = len(slot_in)
    n_in = len(inputs)

    def kernel(mask_ref, q_ref, g_ref, *refs):
        in_refs = refs[:n_in]
        dq_ref = refs[n_in]
        out_refs = refs[n_in + 1 :]
        k = jnp.concatenate([in_refs[i][lead + (0,)] for i, lead in slot_in], axis=0)
        v = jnp.concatenate([in_refs[i][lead + (1,)] for i, lead in slot_in], axis=0)
        q = q_ref[...]
        g = g_ref[...]
        nt = (((1,), (1,)), ((), ()))
        tn = (((0,), (0,)), ((), ()))
        scores = lax.dot_general(q, k, nt, preferred_element_type=jnp.float32) * inv_root
        masked = jnp.where(mask_ref[...] != 0, scores, -1e30)
        highest = jnp.max(masked, axis=1, keepdims=True)
        total_mass = jnp.sum(jnp.exp(masked - highest), axis=1, keepdims=True)
        log_total = highest + jnp.log(total_mass)
        prob = jnp.exp(masked - log_total)
        prob_low = prob.astype(jnp.bfloat16)
        attended = jnp.dot(prob_low, v, preferred_element_type=jnp.float32)
        delta = jnp.sum(g.astype(jnp.float32) * attended, axis=1, keepdims=True)
        prob_grad = lax.dot_general(g, v, nt, preferred_element_type=jnp.float32)
        score_grad = (prob * (prob_grad - delta)).astype(jnp.bfloat16)
        dq = jnp.dot(score_grad, k, preferred_element_type=jnp.float32) * inv_root
        dq_ref[...] = dq.astype(dq_ref.dtype)
        dk = lax.dot_general(score_grad, q, tn, preferred_element_type=jnp.float32) * inv_root
        dv = lax.dot_general(prob_low, g, tn, preferred_element_type=jnp.float32)
        for slot, (i, lead) in enumerate(slot_out):
            out_refs[i][lead + (0,)] = dk[slot * rows : (slot + 1) * rows].astype(jnp.bfloat16)
            out_refs[i][lead + (1,)] = dv[slot * rows : (slot + 1) * rows].astype(jnp.bfloat16)

    def head_spec(lead_shape):
        zeros = (0,) * len(lead_shape)
        return pl.BlockSpec(lead_shape + (2, rows, HD), lambda h: zeros + (0, 0, h))

    in_specs = [
        pl.BlockSpec((rows, slots * rows), lambda h: (0, 0)),
        pl.BlockSpec((rows, HD), lambda h: (0, h + offset)),
        pl.BlockSpec((rows, HD), lambda h: (0, h + offset)),
    ] + [head_spec(tuple(x.shape[:-3])) for x in inputs]
    out_specs = [pl.BlockSpec((rows, HD), lambda h: (0, h))] + [head_spec(lead) for lead in out_lead]
    out_shape = [jax.ShapeDtypeStruct((rows, channels), jnp.bfloat16)] + [
        jax.ShapeDtypeStruct(lead + (2, rows, channels), jnp.bfloat16) for lead in out_lead
    ]
    results = pl.pallas_call(
        kernel,
        grid=(heads,),
        in_specs=in_specs,
        out_specs=out_specs,
        out_shape=out_shape,
        cost_estimate=pl.CostEstimate(
            flops=12 * heads * rows * slots * rows * HD,
            transcendentals=2 * heads * rows * slots * rows,
            bytes_accessed=2 * 4 * slots * rows * channels + 6 * rows * channels + 4 * rows * slots * rows,
        ),
    )(mask, queries, out_grad, *inputs)
    return results[0], results[1:]


def forward_relay(own, count, after):
    core, cross, down, up, diag_up, diag_down, back = route(count)
    if after is not None:
        own, _ = lax.optimization_barrier((own, after))
    from_core = send(own, core)
    from_cross = send(own, cross)
    from_below = send(own, up)
    from_above = send(own, down)
    return [own, from_core, from_cross, from_below, from_above]


def forward_second(first, count, after):
    core, cross, down, up, diag_up, diag_down, back = route(count)
    own, from_core, from_cross, from_below, from_above = first
    ahead = jnp.stack([from_cross, from_below, from_above])
    if after is not None:
        (ahead, from_cross), _ = lax.optimization_barrier(((ahead, from_cross), after))
    relayed = send(ahead, core)
    diag_from_below = send(from_cross, diag_up)
    diag_from_above = send(from_cross, diag_down)
    return first + [relayed, diag_from_below, diag_from_above]


def chunk_kernel(forward_mask, queries, out_grad, inputs, head_offset, inv_root):
    slot_in = [(0, ()), (1, ()), (2, ()), (3, ()), (4, ()), (5, (0,)), (5, (1,)), (5, (2,)), (6, ()), (7, ())]
    out_lead = [(), (4,), (), (), (), (), ()]
    slot_out = [(0, ()), (1, (0,)), (2, ()), (3, ()), (4, ()), (1, (1,)), (1, (2,)), (1, (3,)), (5, ()), (6, ())]
    return attention_backward(
        forward_mask, queries, out_grad, inputs, slot_in, out_lead, slot_out, inv_root, head_offset
    )


def return_first(outs, count, after):
    core, cross, down, up, diag_up, diag_down, back = route(count)
    own_part, to_core, cross_part, below_part, above_part, diag_b_part, diag_a_part = outs
    if after is not None:
        (to_core, diag_b_part, diag_a_part), _ = lax.optimization_barrier(
            ((to_core, diag_b_part, diag_a_part), after)
        )
    to_partner = send(to_core, core)
    diag_back_below = send(diag_b_part, back(diag_up))
    diag_back_above = send(diag_a_part, back(diag_down))
    return [to_partner, diag_back_below, diag_back_above]


def return_second(outs, first, count, after):
    core, cross, down, up, diag_up, diag_down, back = route(count)
    own_part, to_core, cross_part, below_part, above_part, diag_b_part, diag_a_part = outs
    to_partner, diag_back_below, diag_back_above = first
    wide = lambda tensor: tensor.astype(jnp.float32)
    cross_sum = wide(cross_part) + wide(to_partner[1]) + wide(diag_back_below) + wide(diag_back_above)
    below_sum = wide(below_part) + wide(to_partner[2])
    above_sum = wide(above_part) + wide(to_partner[3])
    sums = (cross_sum.astype(jnp.bfloat16), below_sum.astype(jnp.bfloat16), above_sum.astype(jnp.bfloat16))
    if after is not None:
        sums, _ = lax.optimization_barrier((sums, after))
    got_cross = send(sums[0], cross)
    got_below = send(sums[1], down)
    got_above = send(sums[2], up)
    summed = wide(own_part) + wide(to_partner[0]) + wide(got_cross) + wide(got_below) + wide(got_above)
    return [got_cross, got_below, got_above], summed


def body(queries, keys, values, out_grad, frame_keep, band_window):
    rows_own, channel_total = queries.shape
    frame_len = QUARTERS * rows_own
    inv_root = 1.0 / math.sqrt(HD)
    count = lax.axis_size("tm")
    device = lax.axis_index("tm")
    quarter = device % QUARTERS
    partner = device ^ 1

    middle = (quarter == 1) | (quarter == 2)
    diag_quarter = QUARTERS - 1 - quarter
    absent = jnp.int32(-(1 << 20))
    sources = [
        device,
        partner,
        device ^ 2,
        device - QUARTERS,
        device + QUARTERS,
        device ^ 3,
        partner - QUARTERS,
        partner + QUARTERS,
        jnp.where(middle, device - quarter - QUARTERS + diag_quarter, absent),
        jnp.where(middle, device - quarter + QUARTERS + diag_quarter, absent),
    ]
    base_rows = jnp.arange(rows_own, dtype=jnp.int32)
    far_rows = jnp.concatenate([source * rows_own + base_rows for source in sources])
    own_rows = device * rows_own + base_rows
    forward_mask = allowed(own_rows, far_rows, frame_keep, band_window, frame_len).astype(jnp.int32)
    heads = channel_total // HD
    chunk_heads = heads // CHUNKS if heads % CHUNKS == 0 else heads
    width = chunk_heads * HD
    starts = list(range(0, channel_total, width))
    firsts, seconds, outs, backs, sums, dqs = [], [], [], [], [], []
    for c, first in enumerate(starts):
        own = jnp.stack([keys[:, first : first + width], values[:, first : first + width]])
        firsts.append(forward_relay(own, count, firsts[c - 1][1:] if c else None))
    for c in range(len(starts)):
        seconds.append(forward_second(firsts[c], count, seconds[c - 1][5:] if c else None))
    for c, first in enumerate(starts):
        dq, parts = chunk_kernel(forward_mask, queries, out_grad, seconds[c], first // HD, inv_root)
        dqs.append(dq)
        outs.append(parts)
    for c in range(len(starts)):
        backs.append(return_first(outs[c], count, backs[c - 1] if c else None))
    got = None
    for c in range(len(starts)):
        got, summed = return_second(outs[c], backs[c], count, got)
        sums.append(summed)
    grads = [(dqs[c], sums[c][0].astype(jnp.bfloat16), sums[c][1].astype(jnp.bfloat16)) for c in range(len(starts))]
    query_grad = jnp.concatenate([grad[0] for grad in grads], axis=1)
    key_grad = jnp.concatenate([grad[1] for grad in grads], axis=1)
    value_grad = jnp.concatenate([grad[2] for grad in grads], axis=1)
    return (query_grad, key_grad, value_grad)


def solution(mesh):
    placed = (
        P(("group", "tm"), None),
        P(("group", "tm"), None),
        P(("group", "tm"), None),
        P(("group", "tm"), None),
        P("group", None),
        P("group"),
    )
    return jax.shard_map(
        body,
        mesh=mesh,
        in_specs=placed,
        out_specs=(P(("group", "tm"), None), P(("group", "tm"), None), P(("group", "tm"), None)),
        check_vma=False,
    )
```

```python
import math

import jax
import jax.numpy as jnp
from jax import lax
from jax.experimental import pallas as pl
from jax.sharding import PartitionSpec as P

HD = 128
QUARTERS = 4
CHUNKS = 2


def send(value, pairs):
    return lax.ppermute(value, "tm", pairs)


def pairs_of(count, target):
    pairs = []
    for source in range(count):
        dest = target(source)
        if dest is not None and 0 <= dest < count:
            pairs.append((source, dest))
    return pairs


def route(count):
    core = pairs_of(count, lambda t: t ^ 1)
    cross = pairs_of(count, lambda t: t ^ 2)
    down = pairs_of(count, lambda t: t - QUARTERS)
    up = pairs_of(count, lambda t: t + QUARTERS)

    def diag(step):
        def target(t):
            q = t % QUARTERS
            if q == 0:
                return t + step * QUARTERS + 1
            if q == QUARTERS - 1:
                return t + step * QUARTERS - 1
            return None

        return pairs_of(count, target)

    diag_up = diag(1)
    diag_down = diag(-1)
    back = lambda pairs: [(dest, source) for source, dest in pairs]
    return core, cross, down, up, diag_up, diag_down, back


def allowed(query_rows, key_rows, frame_keep, band_window, frame_len):
    frame_count = frame_keep.shape[0]
    query_frame = jnp.floor_divide(query_rows, frame_len)
    key_frame = jnp.floor_divide(key_rows, frame_len)
    query_place = query_rows - query_frame * frame_len
    key_place = key_rows - key_frame * frame_len
    query_inside = (query_rows >= 0) & (query_rows < frame_count * frame_len)
    key_inside = (key_rows >= 0) & (key_rows < frame_count * frame_len)
    inside = query_inside[:, None] & key_inside[None, :]
    onehot = (query_frame[:, None] == jnp.arange(frame_count, dtype=jnp.int32)[None, :]).astype(
        jnp.int32
    )
    keep_rows = jnp.sum(onehot[:, :, None] * frame_keep[None, :, :], axis=1)
    window_rows = jnp.sum(onehot * band_window[None, :], axis=1)
    frame_gap = key_frame[None, :] - query_frame[:, None]
    kept_pair = jnp.zeros(frame_gap.shape, jnp.int32)
    for column in range(3):
        kept_pair = kept_pair + jnp.where(
            frame_gap == column - 1, keep_rows[:, column : column + 1], 0
        )
    place_gap = jnp.abs(query_place[:, None] - key_place[None, :])
    nearby = (frame_gap == 0) | (place_gap <= window_rows[:, None])
    return inside & (kept_pair > 0) & nearby


def attention_backward(mask, queries, out_grad, inputs, slot_in, out_lead, slot_out, inv_root, offset):
    rows, channels = inputs[0].shape[-2:]
    heads = channels // HD
    slots = len(slot_in)
    n_in = len(inputs)

    def kernel(mask_ref, q_ref, g_ref, *refs):
        in_refs = refs[:n_in]
        dq_ref = refs[n_in]
        out_refs = refs[n_in + 1 :]
        k = jnp.concatenate([in_refs[i][lead + (0,)] for i, lead in slot_in], axis=0)
        v = jnp.concatenate([in_refs[i][lead + (1,)] for i, lead in slot_in], axis=0)
        q = q_ref[...]
        g = g_ref[...]
        nt = (((1,), (1,)), ((), ()))
        tn = (((0,), (0,)), ((), ()))
        scores = lax.dot_general(q, k, nt, preferred_element_type=jnp.float32) * inv_root
        masked = jnp.where(mask_ref[...] != 0, scores, -1e30)
        highest = jnp.max(masked, axis=1, keepdims=True)
        total_mass = jnp.sum(jnp.exp(masked - highest), axis=1, keepdims=True)
        log_total = highest + jnp.log(total_mass)
        prob = jnp.exp(masked - log_total)
        prob_low = prob.astype(jnp.bfloat16)
        attended = jnp.dot(prob_low, v, preferred_element_type=jnp.float32)
        delta = jnp.sum(g.astype(jnp.float32) * attended, axis=1, keepdims=True)
        prob_grad = lax.dot_general(g, v, nt, preferred_element_type=jnp.float32)
        score_grad = (prob * (prob_grad - delta)).astype(jnp.bfloat16)
        dq = jnp.dot(score_grad, k, preferred_element_type=jnp.float32) * inv_root
        dq_ref[...] = dq.astype(dq_ref.dtype)
        dk = lax.dot_general(score_grad, q, tn, preferred_element_type=jnp.float32) * inv_root
        dv = lax.dot_general(prob_low, g, tn, preferred_element_type=jnp.float32)
        for slot, (i, lead) in enumerate(slot_out):
            out_refs[i][lead + (0,)] = dk[slot * rows : (slot + 1) * rows].astype(jnp.bfloat16)
            out_refs[i][lead + (1,)] = dv[slot * rows : (slot + 1) * rows].astype(jnp.bfloat16)

    def head_spec(lead_shape):
        zeros = (0,) * len(lead_shape)
        return pl.BlockSpec(lead_shape + (2, rows, HD), lambda h: zeros + (0, 0, h))

    in_specs = [
        pl.BlockSpec((rows, slots * rows), lambda h: (0, 0)),
        pl.BlockSpec((rows, HD), lambda h: (0, h + offset)),
        pl.BlockSpec((rows, HD), lambda h: (0, h + offset)),
    ] + [head_spec(tuple(x.shape[:-3])) for x in inputs]
    out_specs = [pl.BlockSpec((rows, HD), lambda h: (0, h))] + [head_spec(lead) for lead in out_lead]
    out_shape = [jax.ShapeDtypeStruct((rows, channels), jnp.bfloat16)] + [
        jax.ShapeDtypeStruct(lead + (2, rows, channels), jnp.bfloat16) for lead in out_lead
    ]
    results = pl.pallas_call(
        kernel,
        grid=(heads,),
        in_specs=in_specs,
        out_specs=out_specs,
        out_shape=out_shape,
        cost_estimate=pl.CostEstimate(
            flops=12 * heads * rows * slots * rows * HD,
            transcendentals=2 * heads * rows * slots * rows,
            bytes_accessed=2 * 4 * slots * rows * channels + 6 * rows * channels + 4 * rows * slots * rows,
        ),
    )(mask, queries, out_grad, *inputs)
    return results[0], results[1:]


def forward_relay(own, count, after):
    core, cross, down, up, diag_up, diag_down, back = route(count)
    if after is not None:
        own, _ = lax.optimization_barrier((own, after))
    from_cross = send(own, cross)
    from_below = send(own, up)
    from_above = send(own, down)
    return [own, from_cross, from_below, from_above]


def forward_second(first, count, after):
    core, cross, down, up, diag_up, diag_down, back = route(count)
    own, from_cross, from_below, from_above = first
    ahead = jnp.stack([own, from_cross, from_below, from_above])
    if after is not None:
        (ahead, from_cross), _ = lax.optimization_barrier(((ahead, from_cross), after))
    relayed = send(ahead, core)
    diag_from_below = send(from_cross, diag_up)
    diag_from_above = send(from_cross, diag_down)
    return first + [relayed, diag_from_below, diag_from_above]


def chunk_kernel(forward_mask, queries, out_grad, inputs, head_offset, inv_root):
    slot_in = [(0, ()), (4, (0,)), (1, ()), (2, ()), (3, ()), (4, (1,)), (4, (2,)), (4, (3,)), (5, ()), (6, ())]
    out_lead = [(), (4,), (), (), (), (), ()]
    slot_out = [(0, ()), (1, (0,)), (2, ()), (3, ()), (4, ()), (1, (1,)), (1, (2,)), (1, (3,)), (5, ()), (6, ())]
    return attention_backward(
        forward_mask, queries, out_grad, inputs, slot_in, out_lead, slot_out, inv_root, head_offset
    )


def return_first(outs, count, after):
    core, cross, down, up, diag_up, diag_down, back = route(count)
    own_part, to_core, cross_part, below_part, above_part, diag_b_part, diag_a_part = outs
    if after is not None:
        (to_core, diag_b_part, diag_a_part), _ = lax.optimization_barrier(
            ((to_core, diag_b_part, diag_a_part), after)
        )
    to_partner = send(to_core, core)
    diag_back_below = send(diag_b_part, back(diag_up))
    diag_back_above = send(diag_a_part, back(diag_down))
    return [to_partner, diag_back_below, diag_back_above]


def return_second(outs, first, count, after):
    core, cross, down, up, diag_up, diag_down, back = route(count)
    own_part, to_core, cross_part, below_part, above_part, diag_b_part, diag_a_part = outs
    to_partner, diag_back_below, diag_back_above = first
    wide = lambda tensor: tensor.astype(jnp.float32)
    cross_sum = wide(cross_part) + wide(to_partner[1]) + wide(diag_back_below) + wide(diag_back_above)
    below_sum = wide(below_part) + wide(to_partner[2])
    above_sum = wide(above_part) + wide(to_partner[3])
    sums = (cross_sum.astype(jnp.bfloat16), below_sum.astype(jnp.bfloat16), above_sum.astype(jnp.bfloat16))
    if after is not None:
        sums, _ = lax.optimization_barrier((sums, after))
    got_cross = send(sums[0], cross)
    got_below = send(sums[1], down)
    got_above = send(sums[2], up)
    summed = wide(own_part) + wide(to_partner[0]) + wide(got_cross) + wide(got_below) + wide(got_above)
    return [got_cross, got_below, got_above], summed


def body(queries, keys, values, out_grad, frame_keep, band_window):
    rows_own, channel_total = queries.shape
    frame_len = QUARTERS * rows_own
    inv_root = 1.0 / math.sqrt(HD)
    count = lax.axis_size("tm")
    device = lax.axis_index("tm")
    quarter = device % QUARTERS
    partner = device ^ 1

    middle = (quarter == 1) | (quarter == 2)
    diag_quarter = QUARTERS - 1 - quarter
    absent = jnp.int32(-(1 << 20))
    sources = [
        device,
        partner,
        device ^ 2,
        device - QUARTERS,
        device + QUARTERS,
        device ^ 3,
        partner - QUARTERS,
        partner + QUARTERS,
        jnp.where(middle, device - quarter - QUARTERS + diag_quarter, absent),
        jnp.where(middle, device - quarter + QUARTERS + diag_quarter, absent),
    ]
    base_rows = jnp.arange(rows_own, dtype=jnp.int32)
    far_rows = jnp.concatenate([source * rows_own + base_rows for source in sources])
    own_rows = device * rows_own + base_rows
    forward_mask = allowed(own_rows, far_rows, frame_keep, band_window, frame_len).astype(jnp.int32)
    heads = channel_total // HD
    chunk_heads = heads // CHUNKS if heads % CHUNKS == 0 else heads
    width = chunk_heads * HD
    starts = list(range(0, channel_total, width))
    firsts, seconds, outs, backs, sums, dqs = [], [], [], [], [], []
    for c, first in enumerate(starts):
        own = jnp.stack([keys[:, first : first + width], values[:, first : first + width]])
        firsts.append(forward_relay(own, count, firsts[c - 1][1:] if c else None))
    for c in range(len(starts)):
        seconds.append(forward_second(firsts[c], count, seconds[c - 1][4:] if c else None))
    for c, first in enumerate(starts):
        inputs = seconds[c]
        if c:
            inputs, _ = lax.optimization_barrier((inputs, backs[c - 1]))
        dq, parts = chunk_kernel(forward_mask, queries, out_grad, inputs, first // HD, inv_root)
        dqs.append(dq)
        outs.append(parts)
        backs.append(return_first(parts, count, backs[c - 1] if c else None))
    got = None
    for c in range(len(starts)):
        got, summed = return_second(outs[c], backs[c], count, got)
        sums.append(summed)
    grads = [(dqs[c], sums[c][0].astype(jnp.bfloat16), sums[c][1].astype(jnp.bfloat16)) for c in range(len(starts))]
    query_grad = jnp.concatenate([grad[0] for grad in grads], axis=1)
    key_grad = jnp.concatenate([grad[1] for grad in grads], axis=1)
    value_grad = jnp.concatenate([grad[2] for grad in grads], axis=1)
    return (query_grad, key_grad, value_grad)


def solution(mesh):
    placed = (
        P(("group", "tm"), None),
        P(("group", "tm"), None),
        P(("group", "tm"), None),
        P(("group", "tm"), None),
        P("group", None),
        P("group"),
    )
    return jax.shard_map(
        body,
        mesh=mesh,
        in_specs=placed,
        out_specs=(P(("group", "tm"), None), P(("group", "tm"), None), P(("group", "tm"), None)),
        check_vma=False,
    )
```

```python
import math

import jax
import jax.numpy as jnp
from jax import lax
from jax.experimental import pallas as pl
from jax.sharding import PartitionSpec as P

HD = 128
QUARTERS = 4
CHUNKS = 2
STEP_HEADS = 2


def send(value, pairs):
    return lax.ppermute(value, "tm", pairs)


def pairs_of(count, target):
    pairs = []
    for source in range(count):
        dest = target(source)
        if dest is not None and 0 <= dest < count:
            pairs.append((source, dest))
    return pairs


def route(count):
    core = pairs_of(count, lambda t: t ^ 1)
    cross = pairs_of(count, lambda t: t ^ 2)
    down = pairs_of(count, lambda t: t - QUARTERS)
    up = pairs_of(count, lambda t: t + QUARTERS)

    def diag(step):
        def target(t):
            q = t % QUARTERS
            if q == 0:
                return t + step * QUARTERS + 1
            if q == QUARTERS - 1:
                return t + step * QUARTERS - 1
            return None

        return pairs_of(count, target)

    diag_up = diag(1)
    diag_down = diag(-1)
    back = lambda pairs: [(dest, source) for source, dest in pairs]
    return core, cross, down, up, diag_up, diag_down, back


def allowed(query_rows, key_rows, frame_keep, band_window, frame_len):
    frame_count = frame_keep.shape[0]
    query_frame = jnp.floor_divide(query_rows, frame_len)
    key_frame = jnp.floor_divide(key_rows, frame_len)
    query_place = query_rows - query_frame * frame_len
    key_place = key_rows - key_frame * frame_len
    query_inside = (query_rows >= 0) & (query_rows < frame_count * frame_len)
    key_inside = (key_rows >= 0) & (key_rows < frame_count * frame_len)
    inside = query_inside[:, None] & key_inside[None, :]
    onehot = (query_frame[:, None] == jnp.arange(frame_count, dtype=jnp.int32)[None, :]).astype(
        jnp.int32
    )
    keep_rows = jnp.sum(onehot[:, :, None] * frame_keep[None, :, :], axis=1)
    window_rows = jnp.sum(onehot * band_window[None, :], axis=1)
    frame_gap = key_frame[None, :] - query_frame[:, None]
    kept_pair = jnp.zeros(frame_gap.shape, jnp.int32)
    for column in range(3):
        kept_pair = kept_pair + jnp.where(
            frame_gap == column - 1, keep_rows[:, column : column + 1], 0
        )
    place_gap = jnp.abs(query_place[:, None] - key_place[None, :])
    nearby = (frame_gap == 0) | (place_gap <= window_rows[:, None])
    return inside & (kept_pair > 0) & nearby


def attention_backward(mask, queries, out_grad, inputs, slot_in, out_lead, slot_out, inv_root, offset):
    rows, channels = inputs[0].shape[-2:]
    heads = channels // HD
    slots = len(slot_in)
    n_in = len(inputs)

    def kernel(mask_ref, q_ref, g_ref, *refs):
        in_refs = refs[:n_in]
        dq_ref = refs[n_in]
        out_refs = refs[n_in + 1 :]
        nt = (((1,), (1,)), ((), ()))
        tn = (((0,), (0,)), ((), ()))
        for j in range(STEP_HEADS):
            cols = slice(j * HD, (j + 1) * HD)
            k = jnp.concatenate([in_refs[i][lead + (0, slice(None), cols)] for i, lead in slot_in], axis=0)
            v = jnp.concatenate([in_refs[i][lead + (1, slice(None), cols)] for i, lead in slot_in], axis=0)
            q = q_ref[:, cols]
            g = g_ref[:, cols]
            scores = lax.dot_general(q, k, nt, preferred_element_type=jnp.float32) * inv_root
            masked = jnp.where(mask_ref[...] != 0, scores, -1e30)
            highest = jnp.max(masked, axis=1, keepdims=True)
            total_mass = jnp.sum(jnp.exp(masked - highest), axis=1, keepdims=True)
            log_total = highest + jnp.log(total_mass)
            prob = jnp.exp(masked - log_total)
            prob_low = prob.astype(jnp.bfloat16)
            attended = jnp.dot(prob_low, v, preferred_element_type=jnp.float32)
            delta = jnp.sum(g.astype(jnp.float32) * attended, axis=1, keepdims=True)
            prob_grad = lax.dot_general(g, v, nt, preferred_element_type=jnp.float32)
            score_grad = (prob * (prob_grad - delta)).astype(jnp.bfloat16)
            dq = jnp.dot(score_grad, k, preferred_element_type=jnp.float32) * inv_root
            dq_ref[:, cols] = dq.astype(dq_ref.dtype)
            dk = lax.dot_general(score_grad, q, tn, preferred_element_type=jnp.float32) * inv_root
            dv = lax.dot_general(prob_low, g, tn, preferred_element_type=jnp.float32)
            for slot, (i, lead) in enumerate(slot_out):
                part = slice(slot * rows, (slot + 1) * rows)
                out_refs[i][lead + (0, slice(None), cols)] = dk[part].astype(jnp.bfloat16)
                out_refs[i][lead + (1, slice(None), cols)] = dv[part].astype(jnp.bfloat16)

    def head_spec(lead_shape):
        zeros = (0,) * len(lead_shape)
        return pl.BlockSpec(lead_shape + (2, rows, STEP_HEADS * HD), lambda h: zeros + (0, 0, h))

    in_specs = [
        pl.BlockSpec((rows, slots * rows), lambda h: (0, 0)),
        pl.BlockSpec((rows, STEP_HEADS * HD), lambda h: (0, h + offset // STEP_HEADS)),
        pl.BlockSpec((rows, STEP_HEADS * HD), lambda h: (0, h + offset // STEP_HEADS)),
    ] + [head_spec(tuple(x.shape[:-3])) for x in inputs]
    out_specs = [pl.BlockSpec((rows, STEP_HEADS * HD), lambda h: (0, h))] + [head_spec(lead) for lead in out_lead]
    out_shape = [jax.ShapeDtypeStruct((rows, channels), jnp.bfloat16)] + [
        jax.ShapeDtypeStruct(lead + (2, rows, channels), jnp.bfloat16) for lead in out_lead
    ]
    results = pl.pallas_call(
        kernel,
        grid=(heads // STEP_HEADS,),
        in_specs=in_specs,
        out_specs=out_specs,
        out_shape=out_shape,
        cost_estimate=pl.CostEstimate(
            flops=12 * heads * rows * slots * rows * HD,
            transcendentals=2 * heads * rows * slots * rows,
            bytes_accessed=2 * 4 * slots * rows * channels + 6 * rows * channels + 4 * rows * slots * rows,
        ),
    )(mask, queries, out_grad, *inputs)
    return results[0], results[1:]


def forward_relay(own, count, after):
    core, cross, down, up, diag_up, diag_down, back = route(count)
    if after is not None:
        own, _ = lax.optimization_barrier((own, after))
    from_core = send(own, core)
    from_cross = send(own, cross)
    from_below = send(own, up)
    from_above = send(own, down)
    return [own, from_core, from_cross, from_below, from_above]


def forward_second(first, count, after):
    core, cross, down, up, diag_up, diag_down, back = route(count)
    own, from_core, from_cross, from_below, from_above = first
    ahead = jnp.stack([from_cross, from_below, from_above])
    if after is not None:
        (ahead, from_cross), _ = lax.optimization_barrier(((ahead, from_cross), after))
    relayed = send(ahead, core)
    diag_from_below = send(from_cross, diag_up)
    diag_from_above = send(from_cross, diag_down)
    return first + [relayed, diag_from_below, diag_from_above]


def chunk_kernel(forward_mask, queries, out_grad, inputs, head_offset, inv_root):
    slot_in = [(0, ()), (1, ()), (2, ()), (3, ()), (4, ()), (5, (0,)), (5, (1,)), (5, (2,)), (6, ()), (7, ())]
    out_lead = [(), (4,), (), (), (), (), ()]
    slot_out = [(0, ()), (1, (0,)), (2, ()), (3, ()), (4, ()), (1, (1,)), (1, (2,)), (1, (3,)), (5, ()), (6, ())]
    return attention_backward(
        forward_mask, queries, out_grad, inputs, slot_in, out_lead, slot_out, inv_root, head_offset
    )


def return_first(outs, count, after):
    core, cross, down, up, diag_up, diag_down, back = route(count)
    own_part, to_core, cross_part, below_part, above_part, diag_b_part, diag_a_part = outs
    if after is not None:
        (to_core, diag_b_part, diag_a_part), _ = lax.optimization_barrier(
            ((to_core, diag_b_part, diag_a_part), after)
        )
    to_partner = send(to_core, core)
    diag_back_below = send(diag_b_part, back(diag_up))
    diag_back_above = send(diag_a_part, back(diag_down))
    return [to_partner, diag_back_below, diag_back_above]


def return_second(outs, first, count, after):
    core, cross, down, up, diag_up, diag_down, back = route(count)
    own_part, to_core, cross_part, below_part, above_part, diag_b_part, diag_a_part = outs
    to_partner, diag_back_below, diag_back_above = first
    wide = lambda tensor: tensor.astype(jnp.float32)
    cross_sum = wide(cross_part) + wide(to_partner[1]) + wide(diag_back_below) + wide(diag_back_above)
    below_sum = wide(below_part) + wide(to_partner[2])
    above_sum = wide(above_part) + wide(to_partner[3])
    sums = (cross_sum.astype(jnp.bfloat16), below_sum.astype(jnp.bfloat16), above_sum.astype(jnp.bfloat16))
    if after is not None:
        sums, _ = lax.optimization_barrier((sums, after))
    got_cross = send(sums[0], cross)
    got_below = send(sums[1], down)
    got_above = send(sums[2], up)
    summed = wide(own_part) + wide(to_partner[0]) + wide(got_cross) + wide(got_below) + wide(got_above)
    return [got_cross, got_below, got_above], summed


def body(queries, keys, values, out_grad, frame_keep, band_window):
    rows_own, channel_total = queries.shape
    frame_len = QUARTERS * rows_own
    inv_root = 1.0 / math.sqrt(HD)
    count = lax.axis_size("tm")
    device = lax.axis_index("tm")
    quarter = device % QUARTERS
    partner = device ^ 1

    middle = (quarter == 1) | (quarter == 2)
    diag_quarter = QUARTERS - 1 - quarter
    absent = jnp.int32(-(1 << 20))
    sources = [
        device,
        partner,
        device ^ 2,
        device - QUARTERS,
        device + QUARTERS,
        device ^ 3,
        partner - QUARTERS,
        partner + QUARTERS,
        jnp.where(middle, device - quarter - QUARTERS + diag_quarter, absent),
        jnp.where(middle, device - quarter + QUARTERS + diag_quarter, absent),
    ]
    base_rows = jnp.arange(rows_own, dtype=jnp.int32)
    far_rows = jnp.concatenate([source * rows_own + base_rows for source in sources])
    own_rows = device * rows_own + base_rows
    forward_mask = allowed(own_rows, far_rows, frame_keep, band_window, frame_len).astype(jnp.int32)
    heads = channel_total // HD
    chunk_heads = heads // CHUNKS if heads % CHUNKS == 0 else heads
    width = chunk_heads * HD
    starts = list(range(0, channel_total, width))
    firsts, seconds, outs, backs, sums, dqs = [], [], [], [], [], []
    for c, first in enumerate(starts):
        own = jnp.stack([keys[:, first : first + width], values[:, first : first + width]])
        firsts.append(forward_relay(own, count, None))
    for c in range(len(starts)):
        seconds.append(forward_second(firsts[c], count, None))
    for c, first in enumerate(starts):
        dq, parts = chunk_kernel(forward_mask, queries, out_grad, seconds[c], first // HD, inv_root)
        dqs.append(dq)
        outs.append(parts)
    for c in range(len(starts)):
        backs.append(return_first(outs[c], count, None))
    got = None
    for c in range(len(starts)):
        got, summed = return_second(outs[c], backs[c], count, None)
        sums.append(summed)
    grads = [(dqs[c], sums[c][0].astype(jnp.bfloat16), sums[c][1].astype(jnp.bfloat16)) for c in range(len(starts))]
    query_grad = jnp.concatenate([grad[0] for grad in grads], axis=1)
    key_grad = jnp.concatenate([grad[1] for grad in grads], axis=1)
    value_grad = jnp.concatenate([grad[2] for grad in grads], axis=1)
    return (query_grad, key_grad, value_grad)


def solution(mesh):
    placed = (
        P(("group", "tm"), None),
        P(("group", "tm"), None),
        P(("group", "tm"), None),
        P(("group", "tm"), None),
        P("group", None),
        P("group"),
    )
    return jax.shard_map(
        body,
        mesh=mesh,
        in_specs=placed,
        out_specs=(P(("group", "tm"), None), P(("group", "tm"), None), P(("group", "tm"), None)),
        check_vma=False,
    )
```

```python
import math

import jax
import jax.numpy as jnp
from jax import lax
from jax.experimental import pallas as pl
from jax.sharding import PartitionSpec as P

HD = 128
QUARTERS = 4
CHUNKS = 2
STEP_HEADS = 2


def send(value, pairs):
    return lax.ppermute(value, "tm", pairs)


def pairs_of(count, target):
    pairs = []
    for source in range(count):
        dest = target(source)
        if dest is not None and 0 <= dest < count:
            pairs.append((source, dest))
    return pairs


def route(count):
    core = pairs_of(count, lambda t: t ^ 1)
    cross = pairs_of(count, lambda t: t ^ 2)
    down = pairs_of(count, lambda t: t - QUARTERS)
    up = pairs_of(count, lambda t: t + QUARTERS)

    def diag(step):
        def target(t):
            q = t % QUARTERS
            if q == 0:
                return t + step * QUARTERS + 1
            if q == QUARTERS - 1:
                return t + step * QUARTERS - 1
            return None

        return pairs_of(count, target)

    diag_up = diag(1)
    diag_down = diag(-1)
    back = lambda pairs: [(dest, source) for source, dest in pairs]
    return core, cross, down, up, diag_up, diag_down, back


def allowed(query_rows, key_rows, frame_keep, band_window, frame_len):
    frame_count = frame_keep.shape[0]
    query_frame = jnp.floor_divide(query_rows, frame_len)
    key_frame = jnp.floor_divide(key_rows, frame_len)
    query_place = query_rows - query_frame * frame_len
    key_place = key_rows - key_frame * frame_len
    query_inside = (query_rows >= 0) & (query_rows < frame_count * frame_len)
    key_inside = (key_rows >= 0) & (key_rows < frame_count * frame_len)
    inside = query_inside[:, None] & key_inside[None, :]
    onehot = (query_frame[:, None] == jnp.arange(frame_count, dtype=jnp.int32)[None, :]).astype(
        jnp.int32
    )
    keep_rows = jnp.sum(onehot[:, :, None] * frame_keep[None, :, :], axis=1)
    window_rows = jnp.sum(onehot * band_window[None, :], axis=1)
    frame_gap = key_frame[None, :] - query_frame[:, None]
    kept_pair = jnp.zeros(frame_gap.shape, jnp.int32)
    for column in range(3):
        kept_pair = kept_pair + jnp.where(
            frame_gap == column - 1, keep_rows[:, column : column + 1], 0
        )
    place_gap = jnp.abs(query_place[:, None] - key_place[None, :])
    nearby = (frame_gap == 0) | (place_gap <= window_rows[:, None])
    return inside & (kept_pair > 0) & nearby


def attention_backward(mask, queries, out_grad, inputs, slot_in, out_lead, slot_out, inv_root, offset):
    rows, channels = inputs[0].shape[-2:]
    heads = channels // HD
    slots = len(slot_in)
    n_in = len(inputs)

    def kernel(mask_ref, q_ref, g_ref, *refs):
        in_refs = refs[:n_in]
        dq_ref = refs[n_in]
        out_refs = refs[n_in + 1 :]
        nt = (((1,), (1,)), ((), ()))
        tn = (((0,), (0,)), ((), ()))
        for j in range(STEP_HEADS):
            cols = slice(j * HD, (j + 1) * HD)
            k = jnp.concatenate([in_refs[i][lead + (0, slice(None), cols)] for i, lead in slot_in], axis=0)
            v = jnp.concatenate([in_refs[i][lead + (1, slice(None), cols)] for i, lead in slot_in], axis=0)
            q = q_ref[:, cols]
            g = g_ref[:, cols]
            scores = lax.dot_general(q, k, nt, preferred_element_type=jnp.float32) * inv_root
            masked = jnp.where(mask_ref[...] != 0, scores, -1e30)
            highest = jnp.max(masked, axis=1, keepdims=True)
            total_mass = jnp.sum(jnp.exp(masked - highest), axis=1, keepdims=True)
            log_total = highest + jnp.log(total_mass)
            prob = jnp.exp(masked - log_total)
            prob_low = prob.astype(jnp.bfloat16)
            attended = jnp.dot(prob_low, v, preferred_element_type=jnp.float32)
            delta = jnp.sum(g.astype(jnp.float32) * attended, axis=1, keepdims=True)
            prob_grad = lax.dot_general(g, v, nt, preferred_element_type=jnp.float32)
            score_grad = (prob * (prob_grad - delta)).astype(jnp.bfloat16)
            dq = jnp.dot(score_grad, k, preferred_element_type=jnp.float32) * inv_root
            dq_ref[:, cols] = dq.astype(dq_ref.dtype)
            dk = lax.dot_general(score_grad, q, tn, preferred_element_type=jnp.float32) * inv_root
            dv = lax.dot_general(prob_low, g, tn, preferred_element_type=jnp.float32)
            for slot, (i, lead) in enumerate(slot_out):
                part = slice(slot * rows, (slot + 1) * rows)
                out_refs[i][lead + (0, slice(None), cols)] = dk[part].astype(jnp.bfloat16)
                out_refs[i][lead + (1, slice(None), cols)] = dv[part].astype(jnp.bfloat16)

    def head_spec(lead_shape):
        zeros = (0,) * len(lead_shape)
        return pl.BlockSpec(lead_shape + (2, rows, STEP_HEADS * HD), lambda h: zeros + (0, 0, h))

    in_specs = [
        pl.BlockSpec((rows, slots * rows), lambda h: (0, 0)),
        pl.BlockSpec((rows, STEP_HEADS * HD), lambda h: (0, h + offset // STEP_HEADS)),
        pl.BlockSpec((rows, STEP_HEADS * HD), lambda h: (0, h + offset // STEP_HEADS)),
    ] + [head_spec(tuple(x.shape[:-3])) for x in inputs]
    out_specs = [pl.BlockSpec((rows, STEP_HEADS * HD), lambda h: (0, h))] + [head_spec(lead) for lead in out_lead]
    out_shape = [jax.ShapeDtypeStruct((rows, channels), jnp.bfloat16)] + [
        jax.ShapeDtypeStruct(lead + (2, rows, channels), jnp.bfloat16) for lead in out_lead
    ]
    results = pl.pallas_call(
        kernel,
        grid=(heads // STEP_HEADS,),
        in_specs=in_specs,
        out_specs=out_specs,
        out_shape=out_shape,
        cost_estimate=pl.CostEstimate(
            flops=12 * heads * rows * slots * rows * HD,
            transcendentals=2 * heads * rows * slots * rows,
            bytes_accessed=2 * 4 * slots * rows * channels + 6 * rows * channels + 4 * rows * slots * rows,
        ),
    )(mask, queries, out_grad, *inputs)
    return results[0], results[1:]


def forward_relay(own, count, after):
    core, cross, down, up, diag_up, diag_down, back = route(count)
    own_cross = own_links = own
    if after is not None:
        own_cross, _ = lax.optimization_barrier((own, after[0]))
        own_links, _ = lax.optimization_barrier((own, after[1]))
    from_core = send(own, core)
    from_cross = send(own_cross, cross)
    from_below = send(own_links, up)
    from_above = send(own_links, down)
    return [own, from_core, from_cross, from_below, from_above]


def forward_second(first, count, after):
    core, cross, down, up, diag_up, diag_down, back = route(count)
    own, from_core, from_cross, from_below, from_above = first
    ahead = jnp.stack([from_cross, from_below, from_above])
    if after is not None:
        (ahead, from_cross), _ = lax.optimization_barrier(((ahead, from_cross), after))
    relayed = send(ahead, core)
    diag_from_below = send(from_cross, diag_up)
    diag_from_above = send(from_cross, diag_down)
    return first + [relayed, diag_from_below, diag_from_above]


def chunk_kernel(forward_mask, queries, out_grad, inputs, head_offset, inv_root):
    slot_in = [(0, ()), (1, ()), (2, ()), (3, ()), (4, ()), (5, (0,)), (5, (1,)), (5, (2,)), (6, ()), (7, ())]
    out_lead = [(), (4,), (), (), (), (), ()]
    slot_out = [(0, ()), (1, (0,)), (2, ()), (3, ()), (4, ()), (1, (1,)), (1, (2,)), (1, (3,)), (5, ()), (6, ())]
    return attention_backward(
        forward_mask, queries, out_grad, inputs, slot_in, out_lead, slot_out, inv_root, head_offset
    )


def return_first(outs, count, after):
    core, cross, down, up, diag_up, diag_down, back = route(count)
    own_part, to_core, cross_part, below_part, above_part, diag_b_part, diag_a_part = outs
    if after is not None:
        (to_core, diag_b_part, diag_a_part), _ = lax.optimization_barrier(
            ((to_core, diag_b_part, diag_a_part), after)
        )
    to_partner = send(to_core, core)
    diag_back_below = send(diag_b_part, back(diag_up))
    diag_back_above = send(diag_a_part, back(diag_down))
    return [to_partner, diag_back_below, diag_back_above]


def return_second(outs, first, count, after):
    core, cross, down, up, diag_up, diag_down, back = route(count)
    own_part, to_core, cross_part, below_part, above_part, diag_b_part, diag_a_part = outs
    to_partner, diag_back_below, diag_back_above = first
    wide = lambda tensor: tensor.astype(jnp.float32)
    cross_sum = wide(cross_part) + wide(to_partner[1]) + wide(diag_back_below) + wide(diag_back_above)
    below_sum = wide(below_part) + wide(to_partner[2])
    above_sum = wide(above_part) + wide(to_partner[3])
    sums = (cross_sum.astype(jnp.bfloat16), below_sum.astype(jnp.bfloat16), above_sum.astype(jnp.bfloat16))
    if after is not None:
        sums, _ = lax.optimization_barrier((sums, after))
    got_cross = send(sums[0], cross)
    got_below = send(sums[1], down)
    got_above = send(sums[2], up)
    summed = wide(own_part) + wide(to_partner[0]) + wide(got_cross) + wide(got_below) + wide(got_above)
    return [got_cross, got_below, got_above], summed


def body(queries, keys, values, out_grad, frame_keep, band_window):
    rows_own, channel_total = queries.shape
    frame_len = QUARTERS * rows_own
    inv_root = 1.0 / math.sqrt(HD)
    count = lax.axis_size("tm")
    device = lax.axis_index("tm")
    quarter = device % QUARTERS
    partner = device ^ 1

    middle = (quarter == 1) | (quarter == 2)
    diag_quarter = QUARTERS - 1 - quarter
    absent = jnp.int32(-(1 << 20))
    sources = [
        device,
        partner,
        device ^ 2,
        device - QUARTERS,
        device + QUARTERS,
        device ^ 3,
        partner - QUARTERS,
        partner + QUARTERS,
        jnp.where(middle, device - quarter - QUARTERS + diag_quarter, absent),
        jnp.where(middle, device - quarter + QUARTERS + diag_quarter, absent),
    ]
    base_rows = jnp.arange(rows_own, dtype=jnp.int32)
    far_rows = jnp.concatenate([source * rows_own + base_rows for source in sources])
    own_rows = device * rows_own + base_rows
    forward_mask = allowed(own_rows, far_rows, frame_keep, band_window, frame_len).astype(jnp.int32)
    heads = channel_total // HD
    chunk_heads = heads // CHUNKS if heads % CHUNKS == 0 else heads
    width = chunk_heads * HD
    starts = list(range(0, channel_total, width))
    firsts, seconds, outs, backs, sums, dqs = [], [], [], [], [], []
    for c, first in enumerate(starts):
        own = jnp.stack([keys[:, first : first + width], values[:, first : first + width]])
        after = (firsts[c - 1][2], seconds[c - 1][6:]) if c else None
        firsts.append(forward_relay(own, count, after))
        seconds.append(forward_second(firsts[c], count, None))
    for c, first in enumerate(starts):
        dq, parts = chunk_kernel(forward_mask, queries, out_grad, seconds[c], first // HD, inv_root)
        dqs.append(dq)
        outs.append(parts)
    for c in range(len(starts)):
        backs.append(return_first(outs[c], count, None))
    got = None
    for c in range(len(starts)):
        got, summed = return_second(outs[c], backs[c], count, None)
        sums.append(summed)
    grads = [(dqs[c], sums[c][0].astype(jnp.bfloat16), sums[c][1].astype(jnp.bfloat16)) for c in range(len(starts))]
    query_grad = jnp.concatenate([grad[0] for grad in grads], axis=1)
    key_grad = jnp.concatenate([grad[1] for grad in grads], axis=1)
    value_grad = jnp.concatenate([grad[2] for grad in grads], axis=1)
    return (query_grad, key_grad, value_grad)


def solution(mesh):
    placed = (
        P(("group", "tm"), None),
        P(("group", "tm"), None),
        P(("group", "tm"), None),
        P(("group", "tm"), None),
        P("group", None),
        P("group"),
    )
    return jax.shard_map(
        body,
        mesh=mesh,
        in_specs=placed,
        out_specs=(P(("group", "tm"), None), P(("group", "tm"), None), P(("group", "tm"), None)),
        check_vma=False,
    )
```

```python
import math

import jax
import jax.numpy as jnp
from jax import lax
from jax.experimental import pallas as pl
from jax.sharding import PartitionSpec as P

HD = 128
QUARTERS = 4
CHUNKS = 2
STEP_HEADS = 2


def send(value, pairs):
    return lax.ppermute(value, "tm", pairs)


def pairs_of(count, target):
    pairs = []
    for source in range(count):
        dest = target(source)
        if dest is not None and 0 <= dest < count:
            pairs.append((source, dest))
    return pairs


def route(count):
    core = pairs_of(count, lambda t: t ^ 1)
    cross = pairs_of(count, lambda t: t ^ 2)
    down = pairs_of(count, lambda t: t - QUARTERS)
    up = pairs_of(count, lambda t: t + QUARTERS)

    def diag(step):
        def target(t):
            q = t % QUARTERS
            if q == 0:
                return t + step * QUARTERS + 1
            if q == QUARTERS - 1:
                return t + step * QUARTERS - 1
            return None

        return pairs_of(count, target)

    diag_up = diag(1)
    diag_down = diag(-1)
    back = lambda pairs: [(dest, source) for source, dest in pairs]
    return core, cross, down, up, diag_up, diag_down, back


def allowed(query_rows, key_rows, frame_keep, band_window, frame_len):
    frame_count = frame_keep.shape[0]
    query_frame = jnp.floor_divide(query_rows, frame_len)
    key_frame = jnp.floor_divide(key_rows, frame_len)
    query_place = query_rows - query_frame * frame_len
    key_place = key_rows - key_frame * frame_len
    query_inside = (query_rows >= 0) & (query_rows < frame_count * frame_len)
    key_inside = (key_rows >= 0) & (key_rows < frame_count * frame_len)
    inside = query_inside[:, None] & key_inside[None, :]
    onehot = (query_frame[:, None] == jnp.arange(frame_count, dtype=jnp.int32)[None, :]).astype(
        jnp.int32
    )
    keep_rows = jnp.sum(onehot[:, :, None] * frame_keep[None, :, :], axis=1)
    window_rows = jnp.sum(onehot * band_window[None, :], axis=1)
    frame_gap = key_frame[None, :] - query_frame[:, None]
    kept_pair = jnp.zeros(frame_gap.shape, jnp.int32)
    for column in range(3):
        kept_pair = kept_pair + jnp.where(
            frame_gap == column - 1, keep_rows[:, column : column + 1], 0
        )
    place_gap = jnp.abs(query_place[:, None] - key_place[None, :])
    nearby = (frame_gap == 0) | (place_gap <= window_rows[:, None])
    return inside & (kept_pair > 0) & nearby


def attention_backward(mask, queries, out_grad, inputs, slot_in, out_lead, slot_out, inv_root, offset, heads):
    rows, channels = queries.shape[0], heads * HD
    slots = len(slot_in)
    n_in = len(inputs)

    def kernel(mask_ref, q_ref, g_ref, *refs):
        in_refs = refs[:n_in]
        dq_ref = refs[n_in]
        out_refs = refs[n_in + 1 :]
        nt = (((1,), (1,)), ((), ()))
        tn = (((0,), (0,)), ((), ()))
        for j in range(STEP_HEADS):
            cols = slice(j * HD, (j + 1) * HD)
            k = jnp.concatenate([in_refs[i][lead + (0, slice(None), cols)] for i, lead in slot_in], axis=0)
            v = jnp.concatenate([in_refs[i][lead + (1, slice(None), cols)] for i, lead in slot_in], axis=0)
            q = q_ref[:, cols]
            g = g_ref[:, cols]
            scores = lax.dot_general(q, k, nt, preferred_element_type=jnp.float32) * inv_root
            masked = jnp.where(mask_ref[...] != 0, scores, -1e30)
            highest = jnp.max(masked, axis=1, keepdims=True)
            total_mass = jnp.sum(jnp.exp(masked - highest), axis=1, keepdims=True)
            log_total = highest + jnp.log(total_mass)
            prob = jnp.exp(masked - log_total)
            prob_low = prob.astype(jnp.bfloat16)
            attended = jnp.dot(prob_low, v, preferred_element_type=jnp.float32)
            delta = jnp.sum(g.astype(jnp.float32) * attended, axis=1, keepdims=True)
            prob_grad = lax.dot_general(g, v, nt, preferred_element_type=jnp.float32)
            score_grad = (prob * (prob_grad - delta)).astype(jnp.bfloat16)
            dq = jnp.dot(score_grad, k, preferred_element_type=jnp.float32) * inv_root
            dq_ref[:, cols] = dq.astype(dq_ref.dtype)
            dk = lax.dot_general(score_grad, q, tn, preferred_element_type=jnp.float32) * inv_root
            dv = lax.dot_general(prob_low, g, tn, preferred_element_type=jnp.float32)
            for slot, (i, lead) in enumerate(slot_out):
                part = slice(slot * rows, (slot + 1) * rows)
                out_refs[i][lead + (0, slice(None), cols)] = dk[part].astype(jnp.bfloat16)
                out_refs[i][lead + (1, slice(None), cols)] = dv[part].astype(jnp.bfloat16)

    def head_spec(lead_shape, shift=0):
        zeros = (0,) * len(lead_shape)
        return pl.BlockSpec(lead_shape + (2, rows, STEP_HEADS * HD), lambda h: zeros + (0, 0, h + shift))

    in_specs = [
        pl.BlockSpec((rows, slots * rows), lambda h: (0, 0)),
        pl.BlockSpec((rows, STEP_HEADS * HD), lambda h: (0, h + offset // STEP_HEADS)),
        pl.BlockSpec((rows, STEP_HEADS * HD), lambda h: (0, h + offset // STEP_HEADS)),
    ] + [head_spec(tuple(x.shape[:-3]), offset // STEP_HEADS) for x in inputs]
    out_specs = [pl.BlockSpec((rows, STEP_HEADS * HD), lambda h: (0, h))] + [head_spec(lead) for lead in out_lead]
    out_shape = [jax.ShapeDtypeStruct((rows, channels), jnp.bfloat16)] + [
        jax.ShapeDtypeStruct(lead + (2, rows, channels), jnp.bfloat16) for lead in out_lead
    ]
    results = pl.pallas_call(
        kernel,
        grid=(heads // STEP_HEADS,),
        in_specs=in_specs,
        out_specs=out_specs,
        out_shape=out_shape,
        cost_estimate=pl.CostEstimate(
            flops=12 * heads * rows * slots * rows * HD,
            transcendentals=2 * heads * rows * slots * rows,
            bytes_accessed=2 * 4 * slots * rows * channels + 6 * rows * channels + 4 * rows * slots * rows,
        ),
    )(mask, queries, out_grad, *inputs)
    return results[0], results[1:]


def forward_relay(own, count, after):
    core, cross, down, up, diag_up, diag_down, back = route(count)
    if after is not None:
        own, _ = lax.optimization_barrier((own, after))
    from_core = send(own, core)
    from_cross = send(own, cross)
    from_below = send(own, up)
    from_above = send(own, down)
    return [own, from_core, from_cross, from_below, from_above]


def forward_second(first, count, after):
    core, cross, down, up, diag_up, diag_down, back = route(count)
    own, from_core, from_cross, from_below, from_above = first
    ahead = jnp.stack([from_cross, from_below, from_above])
    if after is not None:
        (ahead, from_cross), _ = lax.optimization_barrier(((ahead, from_cross), after))
    relayed = send(ahead, core)
    diag_from_below = send(from_cross, diag_up)
    diag_from_above = send(from_cross, diag_down)
    return first + [relayed, diag_from_below, diag_from_above]


def chunk_kernel(forward_mask, queries, out_grad, inputs, head_offset, inv_root, heads):
    slot_in = [(0, ()), (1, ()), (2, ()), (3, ()), (4, ()), (5, (0,)), (5, (1,)), (5, (2,)), (6, ()), (7, ())]
    out_lead = [(), (4,), (), (), (), (), ()]
    slot_out = [(0, ()), (1, (0,)), (2, ()), (3, ()), (4, ()), (1, (1,)), (1, (2,)), (1, (3,)), (5, ()), (6, ())]
    return attention_backward(
        forward_mask, queries, out_grad, inputs, slot_in, out_lead, slot_out, inv_root, head_offset, heads
    )


def return_first(outs, count, after):
    core, cross, down, up, diag_up, diag_down, back = route(count)
    own_part, to_core, cross_part, below_part, above_part, diag_b_part, diag_a_part = outs
    if after is not None:
        (to_core, diag_b_part, diag_a_part), _ = lax.optimization_barrier(
            ((to_core, diag_b_part, diag_a_part), after)
        )
    to_partner = send(to_core, core)
    diag_back_below = send(diag_b_part, back(diag_up))
    diag_back_above = send(diag_a_part, back(diag_down))
    return [to_partner, diag_back_below, diag_back_above]


def return_second(outs, first, count, after):
    core, cross, down, up, diag_up, diag_down, back = route(count)
    own_part, to_core, cross_part, below_part, above_part, diag_b_part, diag_a_part = outs
    to_partner, diag_back_below, diag_back_above = first
    wide = lambda tensor: tensor.astype(jnp.float32)
    cross_sum = wide(cross_part) + wide(to_partner[1]) + wide(diag_back_below) + wide(diag_back_above)
    below_sum = wide(below_part) + wide(to_partner[2])
    above_sum = wide(above_part) + wide(to_partner[3])
    sums = (cross_sum.astype(jnp.bfloat16), below_sum.astype(jnp.bfloat16), above_sum.astype(jnp.bfloat16))
    if after is not None:
        sums, _ = lax.optimization_barrier((sums, after))
    got_cross = send(sums[0], cross)
    got_below = send(sums[1], down)
    got_above = send(sums[2], up)
    summed = wide(own_part) + wide(to_partner[0]) + wide(got_cross) + wide(got_below) + wide(got_above)
    return [got_cross, got_below, got_above], summed


def body(queries, keys, values, out_grad, frame_keep, band_window):
    rows_own, channel_total = queries.shape
    frame_len = QUARTERS * rows_own
    inv_root = 1.0 / math.sqrt(HD)
    count = lax.axis_size("tm")
    device = lax.axis_index("tm")
    quarter = device % QUARTERS
    partner = device ^ 1

    middle = (quarter == 1) | (quarter == 2)
    diag_quarter = QUARTERS - 1 - quarter
    absent = jnp.int32(-(1 << 20))
    sources = [
        device,
        partner,
        device ^ 2,
        device - QUARTERS,
        device + QUARTERS,
        device ^ 3,
        partner - QUARTERS,
        partner + QUARTERS,
        jnp.where(middle, device - quarter - QUARTERS + diag_quarter, absent),
        jnp.where(middle, device - quarter + QUARTERS + diag_quarter, absent),
    ]
    base_rows = jnp.arange(rows_own, dtype=jnp.int32)
    far_rows = jnp.concatenate([source * rows_own + base_rows for source in sources])
    own_rows = device * rows_own + base_rows
    forward_mask = allowed(own_rows, far_rows, frame_keep, band_window, frame_len).astype(jnp.int32)
    heads = channel_total // HD
    chunk_heads = heads // CHUNKS if heads % CHUNKS == 0 else heads
    width = chunk_heads * HD
    starts = list(range(0, channel_total, width))
    outs, backs, sums, dqs = [], [], [], []
    own = jnp.stack([keys, values])
    received = forward_second(forward_relay(own, count, None), count, None)
    for c, first in enumerate(starts):
        dq, parts = chunk_kernel(forward_mask, queries, out_grad, received, first // HD, inv_root, chunk_heads)
        dqs.append(dq)
        outs.append(parts)
    for c in range(len(starts)):
        backs.append(return_first(outs[c], count, None))
    got = None
    for c in range(len(starts)):
        got, summed = return_second(outs[c], backs[c], count, None)
        sums.append(summed)
    grads = [(dqs[c], sums[c][0].astype(jnp.bfloat16), sums[c][1].astype(jnp.bfloat16)) for c in range(len(starts))]
    query_grad = jnp.concatenate([grad[0] for grad in grads], axis=1)
    key_grad = jnp.concatenate([grad[1] for grad in grads], axis=1)
    value_grad = jnp.concatenate([grad[2] for grad in grads], axis=1)
    return (query_grad, key_grad, value_grad)


def solution(mesh):
    placed = (
        P(("group", "tm"), None),
        P(("group", "tm"), None),
        P(("group", "tm"), None),
        P(("group", "tm"), None),
        P("group", None),
        P("group"),
    )
    return jax.shard_map(
        body,
        mesh=mesh,
        in_specs=placed,
        out_specs=(P(("group", "tm"), None), P(("group", "tm"), None), P(("group", "tm"), None)),
        check_vma=False,
    )
```

```python
import math

import jax
import jax.numpy as jnp
from jax import lax
from jax.experimental import pallas as pl
from jax.sharding import PartitionSpec as P

HD = 128
QUARTERS = 4
CHUNKS = 2
STEP_HEADS = 2


def send(value, pairs):
    return lax.ppermute(value, "tm", pairs)


def pairs_of(count, target):
    pairs = []
    for source in range(count):
        dest = target(source)
        if dest is not None and 0 <= dest < count:
            pairs.append((source, dest))
    return pairs


def route(count):
    core = pairs_of(count, lambda t: t ^ 1)
    cross = pairs_of(count, lambda t: t ^ 2)
    down = pairs_of(count, lambda t: t - QUARTERS)
    up = pairs_of(count, lambda t: t + QUARTERS)

    def diag(step):
        def target(t):
            q = t % QUARTERS
            if q == 0:
                return t + step * QUARTERS + 1
            if q == QUARTERS - 1:
                return t + step * QUARTERS - 1
            return None

        return pairs_of(count, target)

    diag_up = diag(1)
    diag_down = diag(-1)
    back = lambda pairs: [(dest, source) for source, dest in pairs]
    return core, cross, down, up, diag_up, diag_down, back


def allowed(query_rows, key_rows, frame_keep, band_window, frame_len):
    frame_count = frame_keep.shape[0]
    query_frame = jnp.floor_divide(query_rows, frame_len)
    key_frame = jnp.floor_divide(key_rows, frame_len)
    query_place = query_rows - query_frame * frame_len
    key_place = key_rows - key_frame * frame_len
    query_inside = (query_rows >= 0) & (query_rows < frame_count * frame_len)
    key_inside = (key_rows >= 0) & (key_rows < frame_count * frame_len)
    inside = query_inside[:, None] & key_inside[None, :]
    onehot = (query_frame[:, None] == jnp.arange(frame_count, dtype=jnp.int32)[None, :]).astype(
        jnp.int32
    )
    keep_rows = jnp.sum(onehot[:, :, None] * frame_keep[None, :, :], axis=1)
    window_rows = jnp.sum(onehot * band_window[None, :], axis=1)
    frame_gap = key_frame[None, :] - query_frame[:, None]
    kept_pair = jnp.zeros(frame_gap.shape, jnp.int32)
    for column in range(3):
        kept_pair = kept_pair + jnp.where(
            frame_gap == column - 1, keep_rows[:, column : column + 1], 0
        )
    place_gap = jnp.abs(query_place[:, None] - key_place[None, :])
    nearby = (frame_gap == 0) | (place_gap <= window_rows[:, None])
    return inside & (kept_pair > 0) & nearby


def attention_backward(mask, queries, out_grad, inputs, slot_in, out_lead, slot_out, inv_root, offset):
    rows, channels = inputs[0].shape[-2:]
    heads = channels // HD
    slots = len(slot_in)
    n_in = len(inputs)

    def kernel(mask_ref, q_ref, g_ref, *refs):
        in_refs = refs[:n_in]
        dq_ref = refs[n_in]
        out_refs = refs[n_in + 1 :]
        nt = (((1,), (1,)), ((), ()))
        tn = (((0,), (0,)), ((), ()))
        for j in range(STEP_HEADS):
            cols = slice(j * HD, (j + 1) * HD)
            k = jnp.concatenate([in_refs[i][lead + (0, slice(None), cols)] for i, lead in slot_in], axis=0)
            v = jnp.concatenate([in_refs[i][lead + (1, slice(None), cols)] for i, lead in slot_in], axis=0)
            q = q_ref[:, cols]
            g = g_ref[:, cols]
            scores = lax.dot_general(q, k, nt, preferred_element_type=jnp.float32) * inv_root
            masked = jnp.where(mask_ref[...] != 0, scores, -1e30)
            highest = jnp.max(masked, axis=1, keepdims=True)
            total_mass = jnp.sum(jnp.exp(masked - highest), axis=1, keepdims=True)
            log_total = highest + jnp.log(total_mass)
            prob = jnp.exp(masked - log_total)
            prob_low = prob.astype(jnp.bfloat16)
            attended = jnp.dot(prob_low, v, preferred_element_type=jnp.float32)
            delta = jnp.sum(g.astype(jnp.float32) * attended, axis=1, keepdims=True)
            prob_grad = lax.dot_general(g, v, nt, preferred_element_type=jnp.float32)
            score_grad = (prob * (prob_grad - delta)).astype(jnp.bfloat16)
            dq = jnp.dot(score_grad, k, preferred_element_type=jnp.float32) * inv_root
            dq_ref[:, cols] = dq.astype(dq_ref.dtype)
            dk = lax.dot_general(score_grad, q, tn, preferred_element_type=jnp.float32) * inv_root
            dv = lax.dot_general(prob_low, g, tn, preferred_element_type=jnp.float32)
            for slot, (i, lead) in enumerate(slot_out):
                part = slice(slot * rows, (slot + 1) * rows)
                out_refs[i][lead + (0, slice(None), cols)] = dk[part].astype(jnp.bfloat16)
                out_refs[i][lead + (1, slice(None), cols)] = dv[part].astype(jnp.bfloat16)

    def head_spec(lead_shape):
        zeros = (0,) * len(lead_shape)
        return pl.BlockSpec(lead_shape + (2, rows, STEP_HEADS * HD), lambda h: zeros + (0, 0, h))

    in_specs = [
        pl.BlockSpec((rows, slots * rows), lambda h: (0, 0)),
        pl.BlockSpec((rows, STEP_HEADS * HD), lambda h: (0, h + offset // STEP_HEADS)),
        pl.BlockSpec((rows, STEP_HEADS * HD), lambda h: (0, h + offset // STEP_HEADS)),
    ] + [head_spec(tuple(x.shape[:-3])) for x in inputs]
    out_specs = [pl.BlockSpec((rows, STEP_HEADS * HD), lambda h: (0, h))] + [head_spec(lead) for lead in out_lead]
    out_shape = [jax.ShapeDtypeStruct((rows, channels), jnp.bfloat16)] + [
        jax.ShapeDtypeStruct(lead + (2, rows, channels), jnp.bfloat16) for lead in out_lead
    ]
    results = pl.pallas_call(
        kernel,
        grid=(heads // STEP_HEADS,),
        in_specs=in_specs,
        out_specs=out_specs,
        out_shape=out_shape,
        cost_estimate=pl.CostEstimate(
            flops=12 * heads * rows * slots * rows * HD,
            transcendentals=2 * heads * rows * slots * rows,
            bytes_accessed=2 * 4 * slots * rows * channels + 6 * rows * channels + 4 * rows * slots * rows,
        ),
    )(mask, queries, out_grad, *inputs)
    return results[0], results[1:]


def forward_relay(own, count, after):
    core, cross, down, up, diag_up, diag_down, back = route(count)
    if after is not None:
        own, _ = lax.optimization_barrier((own, after))
    from_core = send(own, core)
    from_cross = send(own, cross)
    from_below = send(own, up)
    from_above = send(own, down)
    return [own, from_core, from_cross, from_below, from_above]


def forward_second(first, count, after):
    core, cross, down, up, diag_up, diag_down, back = route(count)
    own, from_core, from_cross, from_below, from_above = first
    ahead = jnp.stack([from_cross, from_below, from_above])
    if after is not None:
        (ahead, from_cross), _ = lax.optimization_barrier(((ahead, from_cross), after))
    relayed = send(ahead, core)
    diag_from_below = send(from_cross, diag_up)
    diag_from_above = send(from_cross, diag_down)
    return first + [relayed, diag_from_below, diag_from_above]


def chunk_kernel(forward_mask, queries, out_grad, inputs, head_offset, inv_root):
    slot_in = [(0, ()), (1, ()), (2, ()), (3, ()), (4, ()), (5, (0,)), (5, (1,)), (5, (2,)), (6, ()), (7, ())]
    out_lead = [(), (4,), (), (), (), (), ()]
    slot_out = [(0, ()), (1, (0,)), (2, ()), (3, ()), (4, ()), (1, (1,)), (1, (2,)), (1, (3,)), (5, ()), (6, ())]
    return attention_backward(
        forward_mask, queries, out_grad, inputs, slot_in, out_lead, slot_out, inv_root, head_offset
    )


def return_first(outs, count, after):
    core, cross, down, up, diag_up, diag_down, back = route(count)
    own_part, to_core, cross_part, below_part, above_part, diag_b_part, diag_a_part = outs
    if after is not None:
        (to_core, diag_b_part, diag_a_part), _ = lax.optimization_barrier(
            ((to_core, diag_b_part, diag_a_part), after)
        )
    to_partner = send(to_core, core)
    diag_back_below = send(diag_b_part, back(diag_up))
    diag_back_above = send(diag_a_part, back(diag_down))
    return [to_partner, diag_back_below, diag_back_above]


def return_second(outs, first, count, after):
    core, cross, down, up, diag_up, diag_down, back = route(count)
    own_part, to_core, cross_part, below_part, above_part, diag_b_part, diag_a_part = outs
    to_partner, diag_back_below, diag_back_above = first
    wide = lambda tensor: tensor.astype(jnp.float32)
    cross_sum = wide(cross_part) + wide(to_partner[1]) + wide(diag_back_below) + wide(diag_back_above)
    below_sum = wide(below_part) + wide(to_partner[2])
    above_sum = wide(above_part) + wide(to_partner[3])
    sums = (cross_sum.astype(jnp.bfloat16), below_sum.astype(jnp.bfloat16), above_sum.astype(jnp.bfloat16))
    if after is not None:
        sums, _ = lax.optimization_barrier((sums, after))
    got_cross = send(sums[0], cross)
    got_below = send(sums[1], down)
    got_above = send(sums[2], up)
    summed = wide(own_part) + wide(to_partner[0]) + wide(got_cross) + wide(got_below) + wide(got_above)
    return [got_cross, got_below, got_above], summed


def body(queries, keys, values, out_grad, frame_keep, band_window):
    rows_own, channel_total = queries.shape
    frame_len = QUARTERS * rows_own
    inv_root = 1.0 / math.sqrt(HD)
    count = lax.axis_size("tm")
    device = lax.axis_index("tm")
    quarter = device % QUARTERS
    partner = device ^ 1

    middle = (quarter == 1) | (quarter == 2)
    diag_quarter = QUARTERS - 1 - quarter
    absent = jnp.int32(-(1 << 20))
    sources = [
        device,
        partner,
        device ^ 2,
        device - QUARTERS,
        device + QUARTERS,
        device ^ 3,
        partner - QUARTERS,
        partner + QUARTERS,
        jnp.where(middle, device - quarter - QUARTERS + diag_quarter, absent),
        jnp.where(middle, device - quarter + QUARTERS + diag_quarter, absent),
    ]
    base_rows = jnp.arange(rows_own, dtype=jnp.int32)
    far_rows = jnp.concatenate([source * rows_own + base_rows for source in sources])
    own_rows = device * rows_own + base_rows
    forward_mask = allowed(own_rows, far_rows, frame_keep, band_window, frame_len).astype(jnp.int32)
    heads = channel_total // HD
    chunk_heads = heads // CHUNKS if heads % CHUNKS == 0 else heads
    width = chunk_heads * HD
    starts = list(range(0, channel_total, width))
    chunks = len(starts)
    state = {"own": [jnp.stack([keys[:, f : f + width], values[:, f : f + width]]) for f in starts]}
    state["first"], state["second"], state["parts"], state["back"] = {}, {}, {}, {}
    state["dq"], state["sum"] = {}, {}
    for tick in range(chunks + 4):
        step = {}
        for c in range(chunks):
            lag = tick - c
            if lag == 0:
                step[("first", c)] = forward_relay(state["own"][c], count, None)
            elif lag == 1:
                step[("second", c)] = forward_second(state["first"][c], count, None)
            elif lag == 2:
                dq, parts = chunk_kernel(
                    forward_mask, queries, out_grad, state["second"][c], starts[c] // HD, inv_root
                )
                step[("dq", c)] = dq
                step[("parts", c)] = parts
            elif lag == 3:
                step[("back", c)] = return_first(state["parts"][c], count, None)
            elif lag == 4:
                step[("sum", c)] = return_second(state["parts"][c], state["back"][c], count, None)[1]
        for (kind, c), value in step.items():
            state[kind][c] = value
        if tick < chunks + 3:
            state = lax.optimization_barrier(state)
    sums = [state["sum"][c] for c in range(chunks)]
    dqs = [state["dq"][c] for c in range(chunks)]
    grads = [(dqs[c], sums[c][0].astype(jnp.bfloat16), sums[c][1].astype(jnp.bfloat16)) for c in range(len(starts))]
    query_grad = jnp.concatenate([grad[0] for grad in grads], axis=1)
    key_grad = jnp.concatenate([grad[1] for grad in grads], axis=1)
    value_grad = jnp.concatenate([grad[2] for grad in grads], axis=1)
    return (query_grad, key_grad, value_grad)


def solution(mesh):
    placed = (
        P(("group", "tm"), None),
        P(("group", "tm"), None),
        P(("group", "tm"), None),
        P(("group", "tm"), None),
        P("group", None),
        P("group"),
    )
    return jax.shard_map(
        body,
        mesh=mesh,
        in_specs=placed,
        out_specs=(P(("group", "tm"), None), P(("group", "tm"), None), P(("group", "tm"), None)),
        check_vma=False,
    )
```

```python
import math

import jax
import jax.numpy as jnp
from jax import lax
from jax.experimental import pallas as pl
from jax.sharding import PartitionSpec as P

HD = 128
QUARTERS = 4
CHUNKS = 2
STEP_HEADS = 2


def send(value, pairs):
    return lax.ppermute(value, "tm", pairs)


def pairs_of(count, target):
    pairs = []
    for source in range(count):
        dest = target(source)
        if dest is not None and 0 <= dest < count:
            pairs.append((source, dest))
    return pairs


def route(count):
    core = pairs_of(count, lambda t: t ^ 1)
    cross = pairs_of(count, lambda t: t ^ 2)
    down = pairs_of(count, lambda t: t - QUARTERS)
    up = pairs_of(count, lambda t: t + QUARTERS)

    def diag(step):
        def target(t):
            q = t % QUARTERS
            if q == 0:
                return t + step * QUARTERS + 1
            if q == QUARTERS - 1:
                return t + step * QUARTERS - 1
            return None

        return pairs_of(count, target)

    diag_up = diag(1)
    diag_down = diag(-1)
    back = lambda pairs: [(dest, source) for source, dest in pairs]
    return core, cross, down, up, diag_up, diag_down, back


def allowed(query_rows, key_rows, frame_keep, band_window, frame_len):
    frame_count = frame_keep.shape[0]
    query_frame = jnp.floor_divide(query_rows, frame_len)
    key_frame = jnp.floor_divide(key_rows, frame_len)
    query_place = query_rows - query_frame * frame_len
    key_place = key_rows - key_frame * frame_len
    query_inside = (query_rows >= 0) & (query_rows < frame_count * frame_len)
    key_inside = (key_rows >= 0) & (key_rows < frame_count * frame_len)
    inside = query_inside[:, None] & key_inside[None, :]
    onehot = (query_frame[:, None] == jnp.arange(frame_count, dtype=jnp.int32)[None, :]).astype(
        jnp.int32
    )
    keep_rows = jnp.sum(onehot[:, :, None] * frame_keep[None, :, :], axis=1)
    window_rows = jnp.sum(onehot * band_window[None, :], axis=1)
    frame_gap = key_frame[None, :] - query_frame[:, None]
    kept_pair = jnp.zeros(frame_gap.shape, jnp.int32)
    for column in range(3):
        kept_pair = kept_pair + jnp.where(
            frame_gap == column - 1, keep_rows[:, column : column + 1], 0
        )
    place_gap = jnp.abs(query_place[:, None] - key_place[None, :])
    nearby = (frame_gap == 0) | (place_gap <= window_rows[:, None])
    return inside & (kept_pair > 0) & nearby


def attention_backward(mask, queries, out_grad, inputs, slot_in, out_lead, slot_out, inv_root, offset):
    rows, channels = inputs[0].shape[-2:]
    heads = channels // HD
    slots = len(slot_in)
    n_in = len(inputs)

    def kernel(mask_ref, q_ref, g_ref, *refs):
        in_refs = refs[:n_in]
        dq_ref = refs[n_in]
        out_refs = refs[n_in + 1 :]
        nt = (((1,), (1,)), ((), ()))
        tn = (((0,), (0,)), ((), ()))
        for j in range(STEP_HEADS):
            cols = slice(j * HD, (j + 1) * HD)
            k = jnp.concatenate([in_refs[i][lead + (0, slice(None), cols)] for i, lead in slot_in], axis=0)
            v = jnp.concatenate([in_refs[i][lead + (1, slice(None), cols)] for i, lead in slot_in], axis=0)
            q = q_ref[:, cols]
            g = g_ref[:, cols]
            scores = lax.dot_general(q, k, nt, preferred_element_type=jnp.float32) * inv_root
            masked = jnp.where(mask_ref[...] != 0, scores, -1e30)
            highest = jnp.max(masked, axis=1, keepdims=True)
            total_mass = jnp.sum(jnp.exp(masked - highest), axis=1, keepdims=True)
            log_total = highest + jnp.log(total_mass)
            prob = jnp.exp(masked - log_total)
            prob_low = prob.astype(jnp.bfloat16)
            attended = jnp.dot(prob_low, v, preferred_element_type=jnp.float32)
            delta = jnp.sum(g.astype(jnp.float32) * attended, axis=1, keepdims=True)
            prob_grad = lax.dot_general(g, v, nt, preferred_element_type=jnp.float32)
            score_grad = (prob * (prob_grad - delta)).astype(jnp.bfloat16)
            dq = jnp.dot(score_grad, k, preferred_element_type=jnp.float32) * inv_root
            dq_ref[:, cols] = dq.astype(dq_ref.dtype)
            dk = lax.dot_general(score_grad, q, tn, preferred_element_type=jnp.float32) * inv_root
            dv = lax.dot_general(prob_low, g, tn, preferred_element_type=jnp.float32)
            for slot, (i, lead) in enumerate(slot_out):
                part = slice(slot * rows, (slot + 1) * rows)
                out_refs[i][lead + (0, slice(None), cols)] = dk[part].astype(jnp.bfloat16)
                out_refs[i][lead + (1, slice(None), cols)] = dv[part].astype(jnp.bfloat16)

    def head_spec(lead_shape):
        zeros = (0,) * len(lead_shape)
        return pl.BlockSpec(lead_shape + (2, rows, STEP_HEADS * HD), lambda h: zeros + (0, 0, h))

    in_specs = [
        pl.BlockSpec((rows, slots * rows), lambda h: (0, 0)),
        pl.BlockSpec((rows, STEP_HEADS * HD), lambda h: (0, h + offset // STEP_HEADS)),
        pl.BlockSpec((rows, STEP_HEADS * HD), lambda h: (0, h + offset // STEP_HEADS)),
    ] + [head_spec(tuple(x.shape[:-3])) for x in inputs]
    out_specs = [pl.BlockSpec((rows, STEP_HEADS * HD), lambda h: (0, h))] + [head_spec(lead) for lead in out_lead]
    out_shape = [jax.ShapeDtypeStruct((rows, channels), jnp.bfloat16)] + [
        jax.ShapeDtypeStruct(lead + (2, rows, channels), jnp.bfloat16) for lead in out_lead
    ]
    results = pl.pallas_call(
        kernel,
        grid=(heads // STEP_HEADS,),
        in_specs=in_specs,
        out_specs=out_specs,
        out_shape=out_shape,
        cost_estimate=pl.CostEstimate(
            flops=12 * heads * rows * slots * rows * HD,
            transcendentals=2 * heads * rows * slots * rows,
            bytes_accessed=2 * 4 * slots * rows * channels + 6 * rows * channels + 4 * rows * slots * rows,
        ),
    )(mask, queries, out_grad, *inputs)
    return results[0], results[1:]


def forward_relay(own, count, after):
    core, cross, down, up, diag_up, diag_down, back = route(count)
    if after is not None:
        own, _ = lax.optimization_barrier((own, after))
    from_core = send(own, core)
    from_cross = send(own, cross)
    from_below = send(own, up)
    from_above = send(own, down)
    return [own, from_core, from_cross, from_below, from_above]


def forward_second(first, count, after):
    core, cross, down, up, diag_up, diag_down, back = route(count)
    own, from_core, from_cross, from_below, from_above = first
    ahead = jnp.stack([from_cross, from_below, from_above])
    if after is not None:
        (ahead, from_cross), _ = lax.optimization_barrier(((ahead, from_cross), after))
    relayed = send(ahead, core)
    diag_from_below = send(from_cross, diag_up)
    diag_from_above = send(from_cross, diag_down)
    return first + [relayed, diag_from_below, diag_from_above]


def chunk_kernel(forward_mask, queries, out_grad, inputs, head_offset, inv_root):
    slot_in = [(0, ()), (1, ()), (2, ()), (3, ()), (4, ()), (5, (0,)), (5, (1,)), (5, (2,)), (6, ()), (7, ())]
    out_lead = [(), (4,), (), (), (), (), ()]
    slot_out = [(0, ()), (1, (0,)), (2, ()), (3, ()), (4, ()), (1, (1,)), (1, (2,)), (1, (3,)), (5, ()), (6, ())]
    return attention_backward(
        forward_mask, queries, out_grad, inputs, slot_in, out_lead, slot_out, inv_root, head_offset
    )


def return_first(outs, count, after):
    core, cross, down, up, diag_up, diag_down, back = route(count)
    own_part, to_core, cross_part, below_part, above_part, diag_b_part, diag_a_part = outs
    if after is not None:
        (to_core, diag_b_part, diag_a_part), _ = lax.optimization_barrier(
            ((to_core, diag_b_part, diag_a_part), after)
        )
    to_partner = send(to_core, core)
    diag_back_below = send(diag_b_part, back(diag_up))
    diag_back_above = send(diag_a_part, back(diag_down))
    return [to_partner, diag_back_below, diag_back_above]


def return_second(outs, first, count, after):
    core, cross, down, up, diag_up, diag_down, back = route(count)
    own_part, to_core, cross_part, below_part, above_part, diag_b_part, diag_a_part = outs
    to_partner, diag_back_below, diag_back_above = first
    wide = lambda tensor: tensor.astype(jnp.float32)
    cross_sum = wide(cross_part) + wide(to_partner[1]) + wide(diag_back_below) + wide(diag_back_above)
    below_sum = wide(below_part) + wide(to_partner[2])
    above_sum = wide(above_part) + wide(to_partner[3])
    sums = (cross_sum.astype(jnp.bfloat16), below_sum.astype(jnp.bfloat16), above_sum.astype(jnp.bfloat16))
    if after is not None:
        sums, _ = lax.optimization_barrier((sums, after))
    got_cross = send(sums[0], cross)
    got_below = send(sums[1], down)
    got_above = send(sums[2], up)
    summed = wide(own_part) + wide(to_partner[0]) + wide(got_cross) + wide(got_below) + wide(got_above)
    return [got_cross, got_below, got_above], summed


def body(queries, keys, values, out_grad, frame_keep, band_window):
    rows_own, channel_total = queries.shape
    frame_len = QUARTERS * rows_own
    inv_root = 1.0 / math.sqrt(HD)
    count = lax.axis_size("tm")
    device = lax.axis_index("tm")
    quarter = device % QUARTERS
    partner = device ^ 1

    middle = (quarter == 1) | (quarter == 2)
    diag_quarter = QUARTERS - 1 - quarter
    absent = jnp.int32(-(1 << 20))
    sources = [
        device,
        partner,
        device ^ 2,
        device - QUARTERS,
        device + QUARTERS,
        device ^ 3,
        partner - QUARTERS,
        partner + QUARTERS,
        jnp.where(middle, device - quarter - QUARTERS + diag_quarter, absent),
        jnp.where(middle, device - quarter + QUARTERS + diag_quarter, absent),
    ]
    base_rows = jnp.arange(rows_own, dtype=jnp.int32)
    far_rows = jnp.concatenate([source * rows_own + base_rows for source in sources])
    own_rows = device * rows_own + base_rows
    forward_mask = allowed(own_rows, far_rows, frame_keep, band_window, frame_len).astype(jnp.int32)
    heads = channel_total // HD
    chunk_heads = heads // CHUNKS if heads % CHUNKS == 0 else heads
    width = chunk_heads * HD
    starts = list(range(0, channel_total, width))
    firsts, seconds, outs, backs, sums, dqs = [], [], [], [], [], []
    for c, first in enumerate(starts):
        own = jnp.stack([keys[:, first : first + width], values[:, first : first + width]])
        firsts.append(forward_relay(own, count, None))
    for c in range(len(starts)):
        seconds.append(forward_second(firsts[c], count, None))
    for c, first in enumerate(starts):
        dq, parts = chunk_kernel(forward_mask, queries, out_grad, seconds[c], first // HD, inv_root)
        dqs.append(dq)
        outs.append(parts)
    joined = [jnp.concatenate([part[i] for part in outs], axis=-1) for i in range(len(outs[0]))]
    back_all = return_first(joined, count, None)
    summed = return_second(joined, back_all, count, None)[1]
    query_grad = jnp.concatenate(dqs, axis=1)
    key_grad = summed[0].astype(jnp.bfloat16)
    value_grad = summed[1].astype(jnp.bfloat16)
    return (query_grad, key_grad, value_grad)


def solution(mesh):
    placed = (
        P(("group", "tm"), None),
        P(("group", "tm"), None),
        P(("group", "tm"), None),
        P(("group", "tm"), None),
        P("group", None),
        P("group"),
    )
    return jax.shard_map(
        body,
        mesh=mesh,
        in_specs=placed,
        out_specs=(P(("group", "tm"), None), P(("group", "tm"), None), P(("group", "tm"), None)),
        check_vma=False,
    )
```

```python
import math

import jax
import jax.numpy as jnp
from jax import lax
from jax.experimental import pallas as pl
from jax.sharding import PartitionSpec as P

HD = 128
QUARTERS = 4
CHUNKS = 2
STEP_HEADS = 2


def send(value, pairs):
    return lax.ppermute(value, "tm", pairs)


def pairs_of(count, target):
    pairs = []
    for source in range(count):
        dest = target(source)
        if dest is not None and 0 <= dest < count:
            pairs.append((source, dest))
    return pairs


def route(count):
    core = pairs_of(count, lambda t: t ^ 1)
    cross = pairs_of(count, lambda t: t ^ 2)
    down = pairs_of(count, lambda t: t - QUARTERS)
    up = pairs_of(count, lambda t: t + QUARTERS)

    def diag(step):
        def target(t):
            q = t % QUARTERS
            if q == 0:
                return t + step * QUARTERS + 1
            if q == QUARTERS - 1:
                return t + step * QUARTERS - 1
            return None

        return pairs_of(count, target)

    diag_up = diag(1)
    diag_down = diag(-1)
    back = lambda pairs: [(dest, source) for source, dest in pairs]
    return core, cross, down, up, diag_up, diag_down, back


def allowed(query_rows, key_rows, frame_keep, band_window, frame_len):
    frame_count = frame_keep.shape[0]
    query_frame = jnp.floor_divide(query_rows, frame_len)
    key_frame = jnp.floor_divide(key_rows, frame_len)
    query_place = query_rows - query_frame * frame_len
    key_place = key_rows - key_frame * frame_len
    query_inside = (query_rows >= 0) & (query_rows < frame_count * frame_len)
    key_inside = (key_rows >= 0) & (key_rows < frame_count * frame_len)
    inside = query_inside[:, None] & key_inside[None, :]
    onehot = (query_frame[:, None] == jnp.arange(frame_count, dtype=jnp.int32)[None, :]).astype(
        jnp.int32
    )
    keep_rows = jnp.sum(onehot[:, :, None] * frame_keep[None, :, :], axis=1)
    window_rows = jnp.sum(onehot * band_window[None, :], axis=1)
    frame_gap = key_frame[None, :] - query_frame[:, None]
    kept_pair = jnp.zeros(frame_gap.shape, jnp.int32)
    for column in range(3):
        kept_pair = kept_pair + jnp.where(
            frame_gap == column - 1, keep_rows[:, column : column + 1], 0
        )
    place_gap = jnp.abs(query_place[:, None] - key_place[None, :])
    nearby = (frame_gap == 0) | (place_gap <= window_rows[:, None])
    return inside & (kept_pair > 0) & nearby


def attention_backward(mask, queries, out_grad, inputs, slot_in, out_lead, slot_out, inv_root, offset):
    rows, channels = inputs[0].shape[-2:]
    heads = channels // HD
    slots = len(slot_in)
    n_in = len(inputs)

    def kernel(mask_ref, q_ref, g_ref, *refs):
        in_refs = refs[:n_in]
        dq_ref = refs[n_in]
        out_refs = refs[n_in + 1 :]
        nt = (((1,), (1,)), ((), ()))
        tn = (((0,), (0,)), ((), ()))
        for j in range(STEP_HEADS):
            cols = slice(j * HD, (j + 1) * HD)
            k = jnp.concatenate([in_refs[i][lead + (0, slice(None), cols)] for i, lead in slot_in], axis=0)
            v = jnp.concatenate([in_refs[i][lead + (1, slice(None), cols)] for i, lead in slot_in], axis=0)
            q = q_ref[:, cols]
            g = g_ref[:, cols]
            scores = lax.dot_general(q, k, nt, preferred_element_type=jnp.float32) * inv_root
            masked = jnp.where(mask_ref[...] != 0, scores, -1e30)
            highest = jnp.max(masked, axis=1, keepdims=True)
            total_mass = jnp.sum(jnp.exp(masked - highest), axis=1, keepdims=True)
            log_total = highest + jnp.log(total_mass)
            prob = jnp.exp(masked - log_total)
            prob_low = prob.astype(jnp.bfloat16)
            attended = jnp.dot(prob_low, v, preferred_element_type=jnp.float32)
            delta = jnp.sum(g.astype(jnp.float32) * attended, axis=1, keepdims=True)
            prob_grad = lax.dot_general(g, v, nt, preferred_element_type=jnp.float32)
            score_grad = (prob * (prob_grad - delta)).astype(jnp.bfloat16)
            dq = jnp.dot(score_grad, k, preferred_element_type=jnp.float32) * inv_root
            dq_ref[:, cols] = dq.astype(dq_ref.dtype)
            dk = lax.dot_general(score_grad, q, tn, preferred_element_type=jnp.float32) * inv_root
            dv = lax.dot_general(prob_low, g, tn, preferred_element_type=jnp.float32)
            for slot, (i, lead) in enumerate(slot_out):
                part = slice(slot * rows, (slot + 1) * rows)
                out_refs[i][lead + (0, slice(None), cols)] = dk[part].astype(jnp.bfloat16)
                out_refs[i][lead + (1, slice(None), cols)] = dv[part].astype(jnp.bfloat16)

    def head_spec(lead_shape):
        zeros = (0,) * len(lead_shape)
        return pl.BlockSpec(lead_shape + (2, rows, STEP_HEADS * HD), lambda h: zeros + (0, 0, h))

    in_specs = [
        pl.BlockSpec((rows, slots * rows), lambda h: (0, 0)),
        pl.BlockSpec((rows, STEP_HEADS * HD), lambda h: (0, h + offset // STEP_HEADS)),
        pl.BlockSpec((rows, STEP_HEADS * HD), lambda h: (0, h + offset // STEP_HEADS)),
    ] + [head_spec(tuple(x.shape[:-3])) for x in inputs]
    out_specs = [pl.BlockSpec((rows, STEP_HEADS * HD), lambda h: (0, h))] + [head_spec(lead) for lead in out_lead]
    out_shape = [jax.ShapeDtypeStruct((rows, channels), jnp.bfloat16)] + [
        jax.ShapeDtypeStruct(lead + (2, rows, channels), jnp.bfloat16) for lead in out_lead
    ]
    results = pl.pallas_call(
        kernel,
        grid=(heads // STEP_HEADS,),
        in_specs=in_specs,
        out_specs=out_specs,
        out_shape=out_shape,
        cost_estimate=pl.CostEstimate(
            flops=12 * heads * rows * slots * rows * HD,
            transcendentals=2 * heads * rows * slots * rows,
            bytes_accessed=2 * 4 * slots * rows * channels + 6 * rows * channels + 4 * rows * slots * rows,
        ),
    )(mask, queries, out_grad, *inputs)
    return results[0], results[1:]


def forward_relay(own, count, after):
    core, cross, down, up, diag_up, diag_down, back = route(count)
    if after is not None:
        own, _ = lax.optimization_barrier((own, after))
    from_cross = send(own, cross)
    from_below = send(own, up)
    from_above = send(own, down)
    return [own, from_cross, from_below, from_above]


def forward_second(first, count, after):
    core, cross, down, up, diag_up, diag_down, back = route(count)
    own, from_cross, from_below, from_above = first
    ahead = jnp.stack([own, from_cross, from_below, from_above])
    if after is not None:
        (ahead, from_cross), _ = lax.optimization_barrier(((ahead, from_cross), after))
    relayed = send(ahead, core)
    diag_from_below = send(from_cross, diag_up)
    diag_from_above = send(from_cross, diag_down)
    return first + [relayed, diag_from_below, diag_from_above]


def chunk_kernel(forward_mask, queries, out_grad, inputs, head_offset, inv_root):
    slot_in = [(0, ()), (4, (0,)), (1, ()), (2, ()), (3, ()), (4, (1,)), (4, (2,)), (4, (3,)), (5, ()), (6, ())]
    out_lead = [(), (4,), (), (), (), (), ()]
    slot_out = [(0, ()), (1, (0,)), (2, ()), (3, ()), (4, ()), (1, (1,)), (1, (2,)), (1, (3,)), (5, ()), (6, ())]
    return attention_backward(
        forward_mask, queries, out_grad, inputs, slot_in, out_lead, slot_out, inv_root, head_offset
    )


def return_first(outs, count, after):
    core, cross, down, up, diag_up, diag_down, back = route(count)
    own_part, to_core, cross_part, below_part, above_part, diag_b_part, diag_a_part = outs
    if after is not None:
        (to_core, diag_b_part, diag_a_part), _ = lax.optimization_barrier(
            ((to_core, diag_b_part, diag_a_part), after)
        )
    to_partner = send(to_core, core)
    diag_back_below = send(diag_b_part, back(diag_up))
    diag_back_above = send(diag_a_part, back(diag_down))
    return [to_partner, diag_back_below, diag_back_above]


def return_second(outs, first, count, after):
    core, cross, down, up, diag_up, diag_down, back = route(count)
    own_part, to_core, cross_part, below_part, above_part, diag_b_part, diag_a_part = outs
    to_partner, diag_back_below, diag_back_above = first
    wide = lambda tensor: tensor.astype(jnp.float32)
    cross_sum = wide(cross_part) + wide(to_partner[1]) + wide(diag_back_below) + wide(diag_back_above)
    below_sum = wide(below_part) + wide(to_partner[2])
    above_sum = wide(above_part) + wide(to_partner[3])
    sums = (cross_sum.astype(jnp.bfloat16), below_sum.astype(jnp.bfloat16), above_sum.astype(jnp.bfloat16))
    if after is not None:
        sums, _ = lax.optimization_barrier((sums, after))
    got_cross = send(sums[0], cross)
    got_below = send(sums[1], down)
    got_above = send(sums[2], up)
    summed = wide(own_part) + wide(to_partner[0]) + wide(got_cross) + wide(got_below) + wide(got_above)
    return [got_cross, got_below, got_above], summed


def body(queries, keys, values, out_grad, frame_keep, band_window):
    rows_own, channel_total = queries.shape
    frame_len = QUARTERS * rows_own
    inv_root = 1.0 / math.sqrt(HD)
    count = lax.axis_size("tm")
    device = lax.axis_index("tm")
    quarter = device % QUARTERS
    partner = device ^ 1

    middle = (quarter == 1) | (quarter == 2)
    diag_quarter = QUARTERS - 1 - quarter
    absent = jnp.int32(-(1 << 20))
    sources = [
        device,
        partner,
        device ^ 2,
        device - QUARTERS,
        device + QUARTERS,
        device ^ 3,
        partner - QUARTERS,
        partner + QUARTERS,
        jnp.where(middle, device - quarter - QUARTERS + diag_quarter, absent),
        jnp.where(middle, device - quarter + QUARTERS + diag_quarter, absent),
    ]
    base_rows = jnp.arange(rows_own, dtype=jnp.int32)
    far_rows = jnp.concatenate([source * rows_own + base_rows for source in sources])
    own_rows = device * rows_own + base_rows
    forward_mask = allowed(own_rows, far_rows, frame_keep, band_window, frame_len).astype(jnp.int32)
    heads = channel_total // HD
    chunk_heads = heads // CHUNKS if heads % CHUNKS == 0 else heads
    width = chunk_heads * HD
    starts = list(range(0, channel_total, width))
    firsts, seconds, outs, backs, sums, dqs = [], [], [], [], [], []
    for c, first in enumerate(starts):
        own = jnp.stack([keys[:, first : first + width], values[:, first : first + width]])
        firsts.append(forward_relay(own, count, None))
    for c in range(len(starts)):
        seconds.append(forward_second(firsts[c], count, None))
    for c, first in enumerate(starts):
        dq, parts = chunk_kernel(forward_mask, queries, out_grad, seconds[c], first // HD, inv_root)
        dqs.append(dq)
        outs.append(parts)
    for c in range(len(starts)):
        backs.append(return_first(outs[c], count, None))
    got = None
    for c in range(len(starts)):
        got, summed = return_second(outs[c], backs[c], count, None)
        sums.append(summed)
    grads = [(dqs[c], sums[c][0].astype(jnp.bfloat16), sums[c][1].astype(jnp.bfloat16)) for c in range(len(starts))]
    query_grad = jnp.concatenate([grad[0] for grad in grads], axis=1)
    key_grad = jnp.concatenate([grad[1] for grad in grads], axis=1)
    value_grad = jnp.concatenate([grad[2] for grad in grads], axis=1)
    return (query_grad, key_grad, value_grad)


def solution(mesh):
    placed = (
        P(("group", "tm"), None),
        P(("group", "tm"), None),
        P(("group", "tm"), None),
        P(("group", "tm"), None),
        P("group", None),
        P("group"),
    )
    return jax.shard_map(
        body,
        mesh=mesh,
        in_specs=placed,
        out_specs=(P(("group", "tm"), None), P(("group", "tm"), None), P(("group", "tm"), None)),
        check_vma=False,
    )
```

```python
import math

import jax
import jax.numpy as jnp
from jax import lax
from jax.experimental import pallas as pl
from jax.sharding import PartitionSpec as P

HD = 128
QUARTERS = 4
CHUNKS = 2
STEP_HEADS = 2


def send(value, pairs):
    return lax.ppermute(value, "tm", pairs)


def pairs_of(count, target):
    pairs = []
    for source in range(count):
        dest = target(source)
        if dest is not None and 0 <= dest < count:
            pairs.append((source, dest))
    return pairs


def route(count):
    core = pairs_of(count, lambda t: t ^ 1)
    cross = pairs_of(count, lambda t: t ^ 2)
    down = pairs_of(count, lambda t: t - QUARTERS)
    up = pairs_of(count, lambda t: t + QUARTERS)

    def diag(step):
        def target(t):
            q = t % QUARTERS
            if q == 0:
                return t + step * QUARTERS + 1
            if q == QUARTERS - 1:
                return t + step * QUARTERS - 1
            return None

        return pairs_of(count, target)

    diag_up = diag(1)
    diag_down = diag(-1)
    back = lambda pairs: [(dest, source) for source, dest in pairs]
    return core, cross, down, up, diag_up, diag_down, back


def allowed(query_rows, key_rows, frame_keep, band_window, frame_len):
    frame_count = frame_keep.shape[0]
    query_frame = jnp.floor_divide(query_rows, frame_len)
    key_frame = jnp.floor_divide(key_rows, frame_len)
    query_place = query_rows - query_frame * frame_len
    key_place = key_rows - key_frame * frame_len
    query_inside = (query_rows >= 0) & (query_rows < frame_count * frame_len)
    key_inside = (key_rows >= 0) & (key_rows < frame_count * frame_len)
    inside = query_inside[:, None] & key_inside[None, :]
    onehot = (query_frame[:, None] == jnp.arange(frame_count, dtype=jnp.int32)[None, :]).astype(
        jnp.int32
    )
    keep_rows = jnp.sum(onehot[:, :, None] * frame_keep[None, :, :], axis=1)
    window_rows = jnp.sum(onehot * band_window[None, :], axis=1)
    frame_gap = key_frame[None, :] - query_frame[:, None]
    kept_pair = jnp.zeros(frame_gap.shape, jnp.int32)
    for column in range(3):
        kept_pair = kept_pair + jnp.where(
            frame_gap == column - 1, keep_rows[:, column : column + 1], 0
        )
    place_gap = jnp.abs(query_place[:, None] - key_place[None, :])
    nearby = (frame_gap == 0) | (place_gap <= window_rows[:, None])
    return inside & (kept_pair > 0) & nearby


def attention_backward(mask, queries, out_grad, inputs, slot_in, out_lead, slot_out, inv_root, offset):
    rows, channels = inputs[0].shape[-2:]
    heads = channels // HD
    slots = len(slot_in)
    n_in = len(inputs)

    def kernel(mask_ref, q_ref, g_ref, *refs):
        in_refs = refs[:n_in]
        dq_ref = refs[n_in]
        out_refs = refs[n_in + 1 :]
        nt = (((1,), (1,)), ((), ()))
        tn = (((0,), (0,)), ((), ()))
        for j in range(STEP_HEADS):
            cols = slice(j * HD, (j + 1) * HD)
            k = jnp.concatenate([in_refs[i][lead + (0, slice(None), cols)] for i, lead in slot_in], axis=0)
            v = jnp.concatenate([in_refs[i][lead + (1, slice(None), cols)] for i, lead in slot_in], axis=0)
            q = q_ref[:, cols]
            g = g_ref[:, cols]
            scores = lax.dot_general(q, k, nt, preferred_element_type=jnp.float32) * inv_root
            masked = jnp.where(mask_ref[...] != 0, scores, -1e30)
            highest = jnp.max(masked, axis=1, keepdims=True)
            total_mass = jnp.sum(jnp.exp(masked - highest), axis=1, keepdims=True)
            log_total = highest + jnp.log(total_mass)
            prob = jnp.exp(masked - log_total)
            prob_low = prob.astype(jnp.bfloat16)
            attended = jnp.dot(prob_low, v, preferred_element_type=jnp.float32)
            delta = jnp.sum(g.astype(jnp.float32) * attended, axis=1, keepdims=True)
            prob_grad = lax.dot_general(g, v, nt, preferred_element_type=jnp.float32)
            score_grad = (prob * (prob_grad - delta)).astype(jnp.bfloat16)
            dq = jnp.dot(score_grad, k, preferred_element_type=jnp.float32) * inv_root
            dq_ref[:, cols] = dq.astype(dq_ref.dtype)
            dk = lax.dot_general(score_grad, q, tn, preferred_element_type=jnp.float32) * inv_root
            dv = lax.dot_general(prob_low, g, tn, preferred_element_type=jnp.float32)
            for slot, (i, lead) in enumerate(slot_out):
                part = slice(slot * rows, (slot + 1) * rows)
                out_refs[i][lead + (0, slice(None), cols)] = dk[part].astype(jnp.bfloat16)
                out_refs[i][lead + (1, slice(None), cols)] = dv[part].astype(jnp.bfloat16)

    def head_spec(lead_shape):
        zeros = (0,) * len(lead_shape)
        return pl.BlockSpec(lead_shape + (2, rows, STEP_HEADS * HD), lambda h: zeros + (0, 0, h))

    in_specs = [
        pl.BlockSpec((rows, slots * rows), lambda h: (0, 0)),
        pl.BlockSpec((rows, STEP_HEADS * HD), lambda h: (0, h + offset // STEP_HEADS)),
        pl.BlockSpec((rows, STEP_HEADS * HD), lambda h: (0, h + offset // STEP_HEADS)),
    ] + [head_spec(tuple(x.shape[:-3])) for x in inputs]
    out_specs = [pl.BlockSpec((rows, STEP_HEADS * HD), lambda h: (0, h))] + [head_spec(lead) for lead in out_lead]
    out_shape = [jax.ShapeDtypeStruct((rows, channels), jnp.bfloat16)] + [
        jax.ShapeDtypeStruct(lead + (2, rows, channels), jnp.bfloat16) for lead in out_lead
    ]
    results = pl.pallas_call(
        kernel,
        grid=(heads // STEP_HEADS,),
        in_specs=in_specs,
        out_specs=out_specs,
        out_shape=out_shape,
        cost_estimate=pl.CostEstimate(
            flops=12 * heads * rows * slots * rows * HD,
            transcendentals=2 * heads * rows * slots * rows,
            bytes_accessed=2 * 4 * slots * rows * channels + 6 * rows * channels + 4 * rows * slots * rows,
        ),
    )(mask, queries, out_grad, *inputs)
    return results[0], results[1:]


def forward_relay(own, count, after):
    core, cross, down, up, diag_up, diag_down, back = route(count)
    if after is not None:
        own, _ = lax.optimization_barrier((own, after))
    from_cross = send(own, cross)
    from_below = send(own, up)
    from_above = send(own, down)
    return [own, from_cross, from_below, from_above]


def forward_second(first, count, after):
    core, cross, down, up, diag_up, diag_down, back = route(count)
    own, from_cross, from_below, from_above = first
    ahead = jnp.stack([own, from_cross, from_below, from_above])
    if after is not None:
        (ahead, from_cross), _ = lax.optimization_barrier(((ahead, from_cross), after))
    relayed = send(ahead, core)
    diag_from_below = send(from_cross, diag_up)
    diag_from_above = send(from_cross, diag_down)
    return first + [relayed, diag_from_below, diag_from_above]


def chunk_kernel(forward_mask, queries, out_grad, inputs, head_offset, inv_root):
    slot_in = [(0, ()), (4, (0,)), (1, ()), (2, ()), (3, ()), (4, (1,)), (4, (2,)), (4, (3,)), (5, ()), (6, ())]
    out_lead = [(), (4,), (), (), (), (), ()]
    slot_out = [(0, ()), (1, (0,)), (2, ()), (3, ()), (4, ()), (1, (1,)), (1, (2,)), (1, (3,)), (5, ()), (6, ())]
    return attention_backward(
        forward_mask, queries, out_grad, inputs, slot_in, out_lead, slot_out, inv_root, head_offset
    )


def return_first(outs, count, after):
    core, cross, down, up, diag_up, diag_down, back = route(count)
    own_part, to_core, cross_part, below_part, above_part, diag_b_part, diag_a_part = outs
    if after is not None:
        (to_core, diag_b_part, diag_a_part), _ = lax.optimization_barrier(
            ((to_core, diag_b_part, diag_a_part), after)
        )
    to_partner = send(to_core, core)
    diag_back_below = send(diag_b_part, back(diag_up))
    diag_back_above = send(diag_a_part, back(diag_down))
    return [to_partner, diag_back_below, diag_back_above]


def return_second(outs, first, count, after):
    core, cross, down, up, diag_up, diag_down, back = route(count)
    own_part, to_core, cross_part, below_part, above_part, diag_b_part, diag_a_part = outs
    to_partner, diag_back_below, diag_back_above = first
    wide = lambda tensor: tensor.astype(jnp.float32)
    cross_sum = wide(cross_part) + wide(to_partner[1]) + wide(diag_back_below) + wide(diag_back_above)
    below_sum = wide(below_part) + wide(to_partner[2])
    above_sum = wide(above_part) + wide(to_partner[3])
    sums = (cross_sum.astype(jnp.bfloat16), below_sum.astype(jnp.bfloat16), above_sum.astype(jnp.bfloat16))
    if after is not None:
        sums, _ = lax.optimization_barrier((sums, after))
    got_cross = send(sums[0], cross)
    got_below = send(sums[1], down)
    got_above = send(sums[2], up)
    summed = wide(own_part) + wide(to_partner[0]) + wide(got_cross) + wide(got_below) + wide(got_above)
    return [got_cross, got_below, got_above], summed


def body(queries, keys, values, out_grad, frame_keep, band_window):
    rows_own, channel_total = queries.shape
    frame_len = QUARTERS * rows_own
    inv_root = 1.0 / math.sqrt(HD)
    count = lax.axis_size("tm")
    device = lax.axis_index("tm")
    quarter = device % QUARTERS
    partner = device ^ 1

    middle = (quarter == 1) | (quarter == 2)
    diag_quarter = QUARTERS - 1 - quarter
    absent = jnp.int32(-(1 << 20))
    sources = [
        device,
        partner,
        device ^ 2,
        device - QUARTERS,
        device + QUARTERS,
        device ^ 3,
        partner - QUARTERS,
        partner + QUARTERS,
        jnp.where(middle, device - quarter - QUARTERS + diag_quarter, absent),
        jnp.where(middle, device - quarter + QUARTERS + diag_quarter, absent),
    ]
    base_rows = jnp.arange(rows_own, dtype=jnp.int32)
    far_rows = jnp.concatenate([source * rows_own + base_rows for source in sources])
    own_rows = device * rows_own + base_rows
    forward_mask = allowed(own_rows, far_rows, frame_keep, band_window, frame_len).astype(jnp.int32)
    heads = channel_total // HD
    chunk_heads = heads // CHUNKS if heads % CHUNKS == 0 else heads
    width = chunk_heads * HD
    starts = list(range(0, channel_total, width))
    firsts, seconds, outs, backs, sums, dqs = [], [], [], [], [], []
    for c, first in enumerate(starts):
        own = jnp.stack([keys[:, first : first + width], values[:, first : first + width]])
        firsts.append(forward_relay(own, count, None))
    for c, first in enumerate(starts):
        seconds.append(forward_second(firsts[c], count, dqs[c - 1] if c else None))
        dq, parts = chunk_kernel(forward_mask, queries, out_grad, seconds[c], first // HD, inv_root)
        dqs.append(dq)
        outs.append(parts)
    for c in range(len(starts)):
        backs.append(return_first(outs[c], count, None))
    got = None
    for c in range(len(starts)):
        got, summed = return_second(outs[c], backs[c], count, None)
        sums.append(summed)
    grads = [(dqs[c], sums[c][0].astype(jnp.bfloat16), sums[c][1].astype(jnp.bfloat16)) for c in range(len(starts))]
    query_grad = jnp.concatenate([grad[0] for grad in grads], axis=1)
    key_grad = jnp.concatenate([grad[1] for grad in grads], axis=1)
    value_grad = jnp.concatenate([grad[2] for grad in grads], axis=1)
    return (query_grad, key_grad, value_grad)


def solution(mesh):
    placed = (
        P(("group", "tm"), None),
        P(("group", "tm"), None),
        P(("group", "tm"), None),
        P(("group", "tm"), None),
        P("group", None),
        P("group"),
    )
    return jax.shard_map(
        body,
        mesh=mesh,
        in_specs=placed,
        out_specs=(P(("group", "tm"), None), P(("group", "tm"), None), P(("group", "tm"), None)),
        check_vma=False,
    )
```

```python
import math

import jax
import jax.numpy as jnp
from jax import lax
from jax.experimental import pallas as pl
from jax.sharding import PartitionSpec as P

HD = 128
QUARTERS = 4
CHUNKS = 2
STEP_HEADS = 2


def send(value, pairs):
    return lax.ppermute(value, "tm", pairs)


def pairs_of(count, target):
    pairs = []
    for source in range(count):
        dest = target(source)
        if dest is not None and 0 <= dest < count:
            pairs.append((source, dest))
    return pairs


def route(count):
    core = pairs_of(count, lambda t: t ^ 1)
    cross = pairs_of(count, lambda t: t ^ 2)
    down = pairs_of(count, lambda t: t - QUARTERS)
    up = pairs_of(count, lambda t: t + QUARTERS)

    def diag(step):
        def target(t):
            q = t % QUARTERS
            if q == 0:
                return t + step * QUARTERS + 1
            if q == QUARTERS - 1:
                return t + step * QUARTERS - 1
            return None

        return pairs_of(count, target)

    diag_up = diag(1)
    diag_down = diag(-1)
    back = lambda pairs: [(dest, source) for source, dest in pairs]
    return core, cross, down, up, diag_up, diag_down, back


def allowed(query_rows, key_rows, frame_keep, band_window, frame_len):
    frame_count = frame_keep.shape[0]
    query_frame = jnp.floor_divide(query_rows, frame_len)
    key_frame = jnp.floor_divide(key_rows, frame_len)
    query_place = query_rows - query_frame * frame_len
    key_place = key_rows - key_frame * frame_len
    query_inside = (query_rows >= 0) & (query_rows < frame_count * frame_len)
    key_inside = (key_rows >= 0) & (key_rows < frame_count * frame_len)
    inside = query_inside[:, None] & key_inside[None, :]
    onehot = (query_frame[:, None] == jnp.arange(frame_count, dtype=jnp.int32)[None, :]).astype(
        jnp.int32
    )
    keep_rows = jnp.sum(onehot[:, :, None] * frame_keep[None, :, :], axis=1)
    window_rows = jnp.sum(onehot * band_window[None, :], axis=1)
    frame_gap = key_frame[None, :] - query_frame[:, None]
    kept_pair = jnp.zeros(frame_gap.shape, jnp.int32)
    for column in range(3):
        kept_pair = kept_pair + jnp.where(
            frame_gap == column - 1, keep_rows[:, column : column + 1], 0
        )
    place_gap = jnp.abs(query_place[:, None] - key_place[None, :])
    nearby = (frame_gap == 0) | (place_gap <= window_rows[:, None])
    return inside & (kept_pair > 0) & nearby


def attention_backward(mask, queries, out_grad, inputs, slot_in, out_lead, slot_out, inv_root, offset):
    rows, channels = inputs[0].shape[-2:]
    heads = channels // HD
    slots = len(slot_in)
    n_in = len(inputs)

    def kernel(mask_ref, q_ref, g_ref, *refs):
        in_refs = refs[:n_in]
        dq_ref = refs[n_in]
        out_refs = refs[n_in + 1 :]
        nt = (((1,), (1,)), ((), ()))
        tn = (((0,), (0,)), ((), ()))
        for j in range(STEP_HEADS):
            cols = slice(j * HD, (j + 1) * HD)
            k = jnp.concatenate([in_refs[i][lead + (0, slice(None), cols)] for i, lead in slot_in], axis=0)
            v = jnp.concatenate([in_refs[i][lead + (1, slice(None), cols)] for i, lead in slot_in], axis=0)
            q = q_ref[:, cols]
            g = g_ref[:, cols]
            scores = lax.dot_general(q, k, nt, preferred_element_type=jnp.float32) * inv_root
            masked = jnp.where(mask_ref[...] != 0, scores, -1e30)
            highest = jnp.max(masked, axis=1, keepdims=True)
            total_mass = jnp.sum(jnp.exp(masked - highest), axis=1, keepdims=True)
            log_total = highest + jnp.log(total_mass)
            prob = jnp.exp(masked - log_total)
            prob_low = prob.astype(jnp.bfloat16)
            attended = jnp.dot(prob_low, v, preferred_element_type=jnp.float32)
            delta = jnp.sum(g.astype(jnp.float32) * attended, axis=1, keepdims=True)
            prob_grad = lax.dot_general(g, v, nt, preferred_element_type=jnp.float32)
            score_grad = (prob * (prob_grad - delta)).astype(jnp.bfloat16)
            dq = jnp.dot(score_grad, k, preferred_element_type=jnp.float32) * inv_root
            dq_ref[:, cols] = dq.astype(dq_ref.dtype)
            dk = lax.dot_general(score_grad, q, tn, preferred_element_type=jnp.float32) * inv_root
            dv = lax.dot_general(prob_low, g, tn, preferred_element_type=jnp.float32)
            for slot, (i, lead) in enumerate(slot_out):
                part = slice(slot * rows, (slot + 1) * rows)
                out_refs[i][lead + (0, slice(None), cols)] = dk[part].astype(jnp.bfloat16)
                out_refs[i][lead + (1, slice(None), cols)] = dv[part].astype(jnp.bfloat16)

    def head_spec(lead_shape):
        zeros = (0,) * len(lead_shape)
        return pl.BlockSpec(lead_shape + (2, rows, STEP_HEADS * HD), lambda h: zeros + (0, 0, h))

    in_specs = [
        pl.BlockSpec((rows, slots * rows), lambda h: (0, 0)),
        pl.BlockSpec((rows, STEP_HEADS * HD), lambda h: (0, h + offset // STEP_HEADS)),
        pl.BlockSpec((rows, STEP_HEADS * HD), lambda h: (0, h + offset // STEP_HEADS)),
    ] + [head_spec(tuple(x.shape[:-3])) for x in inputs]
    out_specs = [pl.BlockSpec((rows, STEP_HEADS * HD), lambda h: (0, h))] + [head_spec(lead) for lead in out_lead]
    out_shape = [jax.ShapeDtypeStruct((rows, channels), jnp.bfloat16)] + [
        jax.ShapeDtypeStruct(lead + (2, rows, channels), jnp.bfloat16) for lead in out_lead
    ]
    results = pl.pallas_call(
        kernel,
        grid=(heads // STEP_HEADS,),
        in_specs=in_specs,
        out_specs=out_specs,
        out_shape=out_shape,
        cost_estimate=pl.CostEstimate(
            flops=12 * heads * rows * slots * rows * HD,
            transcendentals=2 * heads * rows * slots * rows,
            bytes_accessed=2 * 4 * slots * rows * channels + 6 * rows * channels + 4 * rows * slots * rows,
        ),
    )(mask, queries, out_grad, *inputs)
    return results[0], results[1:]


def forward_relay(own, count, after):
    core, cross, down, up, diag_up, diag_down, back = route(count)
    if after is not None:
        own, _ = lax.optimization_barrier((own, after))
    from_cross = send(own, cross)
    from_below = send(own, up)
    from_above = send(own, down)
    return [own, from_cross, from_below, from_above]


def forward_second(first, count, after):
    core, cross, down, up, diag_up, diag_down, back = route(count)
    own, from_cross, from_below, from_above = first
    ahead = jnp.stack([own, from_cross, from_below, from_above])
    if after is not None:
        (ahead, from_cross), _ = lax.optimization_barrier(((ahead, from_cross), after))
    relayed = send(ahead, core)
    diag_from_below = send(from_cross, diag_up)
    diag_from_above = send(from_cross, diag_down)
    return first + [relayed, diag_from_below, diag_from_above]


def chunk_kernel(forward_mask, queries, out_grad, inputs, head_offset, inv_root):
    slot_in = [(0, ()), (4, (0,)), (1, ()), (2, ()), (3, ()), (4, (1,)), (4, (2,)), (4, (3,)), (5, ()), (6, ())]
    out_lead = [(), (4,), (), (), (), (), ()]
    slot_out = [(0, ()), (1, (0,)), (2, ()), (3, ()), (4, ()), (1, (1,)), (1, (2,)), (1, (3,)), (5, ()), (6, ())]
    return attention_backward(
        forward_mask, queries, out_grad, inputs, slot_in, out_lead, slot_out, inv_root, head_offset
    )


def return_first(outs, count, after):
    core, cross, down, up, diag_up, diag_down, back = route(count)
    own_part, to_core, cross_part, below_part, above_part, diag_b_part, diag_a_part = outs
    if after is not None:
        (to_core, diag_b_part, diag_a_part), _ = lax.optimization_barrier(
            ((to_core, diag_b_part, diag_a_part), after)
        )
    to_partner = send(to_core, core)
    diag_back_below = send(diag_b_part, back(diag_up))
    diag_back_above = send(diag_a_part, back(diag_down))
    return [to_partner, diag_back_below, diag_back_above]


def return_sums(outs, first):
    own_part, to_core, cross_part, below_part, above_part, diag_b_part, diag_a_part = outs
    to_partner, diag_back_below, diag_back_above = first
    wide = lambda tensor: tensor.astype(jnp.float32)
    cross_sum = wide(cross_part) + wide(to_partner[1]) + wide(diag_back_below) + wide(diag_back_above)
    below_sum = wide(below_part) + wide(to_partner[2])
    above_sum = wide(above_part) + wide(to_partner[3])
    return (cross_sum.astype(jnp.bfloat16), below_sum.astype(jnp.bfloat16), above_sum.astype(jnp.bfloat16))


def return_second(outs, first, count, after, sums=None):
    core, cross, down, up, diag_up, diag_down, back = route(count)
    own_part, to_core, cross_part, below_part, above_part, diag_b_part, diag_a_part = outs
    to_partner, diag_back_below, diag_back_above = first
    wide = lambda tensor: tensor.astype(jnp.float32)
    if sums is None:
        sums = return_sums(outs, first)
    if after is not None:
        sums, _ = lax.optimization_barrier((sums, after))
    got_cross = send(sums[0], cross)
    got_below = send(sums[1], down)
    got_above = send(sums[2], up)
    summed = wide(own_part) + wide(to_partner[0]) + wide(got_cross) + wide(got_below) + wide(got_above)
    return [got_cross, got_below, got_above], summed


def body(queries, keys, values, out_grad, frame_keep, band_window):
    rows_own, channel_total = queries.shape
    frame_len = QUARTERS * rows_own
    inv_root = 1.0 / math.sqrt(HD)
    count = lax.axis_size("tm")
    device = lax.axis_index("tm")
    quarter = device % QUARTERS
    partner = device ^ 1

    middle = (quarter == 1) | (quarter == 2)
    diag_quarter = QUARTERS - 1 - quarter
    absent = jnp.int32(-(1 << 20))
    sources = [
        device,
        partner,
        device ^ 2,
        device - QUARTERS,
        device + QUARTERS,
        device ^ 3,
        partner - QUARTERS,
        partner + QUARTERS,
        jnp.where(middle, device - quarter - QUARTERS + diag_quarter, absent),
        jnp.where(middle, device - quarter + QUARTERS + diag_quarter, absent),
    ]
    base_rows = jnp.arange(rows_own, dtype=jnp.int32)
    far_rows = jnp.concatenate([source * rows_own + base_rows for source in sources])
    own_rows = device * rows_own + base_rows
    forward_mask = allowed(own_rows, far_rows, frame_keep, band_window, frame_len).astype(jnp.int32)
    heads = channel_total // HD
    chunk_heads = heads // CHUNKS if heads % CHUNKS == 0 else heads
    width = chunk_heads * HD
    starts = list(range(0, channel_total, width))
    firsts, seconds, outs, backs, sums, dqs = [], [], [], [], [], []
    for c, first in enumerate(starts):
        own = jnp.stack([keys[:, first : first + width], values[:, first : first + width]])
        firsts.append(forward_relay(own, count, None))
    for c in range(len(starts)):
        seconds.append(forward_second(firsts[c], count, None))
    for c, first in enumerate(starts):
        inputs = seconds[c]
        if c:
            done_back = return_first(outs[c - 1], count, None)
            backs.append(done_back)
            (inputs, ready), _ = lax.optimization_barrier(((inputs, return_sums(outs[c - 1], done_back)), 0))
        dq, parts = chunk_kernel(forward_mask, queries, out_grad, inputs, first // HD, inv_root)
        if c:
            got, summed = return_second(outs[c - 1], done_back, count, None, ready)
            (dq, parts, summed), _ = lax.optimization_barrier(((dq, parts, summed), 0))
            sums.append(summed)
        dqs.append(dq)
        outs.append(parts)
    last = len(starts) - 1
    backs.append(return_first(outs[last], count, None))
    sums.append(return_second(outs[last], backs[last], count, None)[1])
    grads = [(dqs[c], sums[c][0].astype(jnp.bfloat16), sums[c][1].astype(jnp.bfloat16)) for c in range(len(starts))]
    query_grad = jnp.concatenate([grad[0] for grad in grads], axis=1)
    key_grad = jnp.concatenate([grad[1] for grad in grads], axis=1)
    value_grad = jnp.concatenate([grad[2] for grad in grads], axis=1)
    return (query_grad, key_grad, value_grad)


def solution(mesh):
    placed = (
        P(("group", "tm"), None),
        P(("group", "tm"), None),
        P(("group", "tm"), None),
        P(("group", "tm"), None),
        P("group", None),
        P("group"),
    )
    return jax.shard_map(
        body,
        mesh=mesh,
        in_specs=placed,
        out_specs=(P(("group", "tm"), None), P(("group", "tm"), None), P(("group", "tm"), None)),
        check_vma=False,
    )
```

```python
import math

import jax
import jax.numpy as jnp
from jax import lax
from jax.experimental import pallas as pl
from jax.sharding import PartitionSpec as P

HD = 128
QUARTERS = 4
STEP_HEADS = 2


def send(value, pairs):
    return lax.ppermute(value, "tm", pairs)


def pairs_of(count, target):
    pairs = []
    for source in range(count):
        dest = target(source)
        if dest is not None and 0 <= dest < count:
            pairs.append((source, dest))
    return pairs


def route(count):
    core = pairs_of(count, lambda t: t ^ 1)
    cross = pairs_of(count, lambda t: t ^ 2)
    down = pairs_of(count, lambda t: t - QUARTERS)
    up = pairs_of(count, lambda t: t + QUARTERS)

    def diag(step):
        def target(t):
            q = t % QUARTERS
            if q == 0:
                return t + step * QUARTERS + 1
            if q == QUARTERS - 1:
                return t + step * QUARTERS - 1
            return None

        return pairs_of(count, target)

    diag_up = diag(1)
    diag_down = diag(-1)
    back = lambda pairs: [(dest, source) for source, dest in pairs]
    return core, cross, down, up, diag_up, diag_down, back


def allowed(query_rows, key_rows, frame_keep, band_window, frame_len):
    frame_count = frame_keep.shape[0]
    query_frame = jnp.floor_divide(query_rows, frame_len)
    key_frame = jnp.floor_divide(key_rows, frame_len)
    query_place = query_rows - query_frame * frame_len
    key_place = key_rows - key_frame * frame_len
    query_inside = (query_rows >= 0) & (query_rows < frame_count * frame_len)
    key_inside = (key_rows >= 0) & (key_rows < frame_count * frame_len)
    inside = query_inside[:, None] & key_inside[None, :]
    onehot = (query_frame[:, None] == jnp.arange(frame_count, dtype=jnp.int32)[None, :]).astype(
        jnp.int32
    )
    keep_rows = jnp.sum(onehot[:, :, None] * frame_keep[None, :, :], axis=1)
    window_rows = jnp.sum(onehot * band_window[None, :], axis=1)
    frame_gap = key_frame[None, :] - query_frame[:, None]
    kept_pair = jnp.zeros(frame_gap.shape, jnp.int32)
    for column in range(3):
        kept_pair = kept_pair + jnp.where(
            frame_gap == column - 1, keep_rows[:, column : column + 1], 0
        )
    place_gap = jnp.abs(query_place[:, None] - key_place[None, :])
    nearby = (frame_gap == 0) | (place_gap <= window_rows[:, None])
    return inside & (kept_pair > 0) & nearby


def attention_backward(mask, queries, out_grad, inputs, slot_in, out_lead, slot_out, inv_root, offset):
    rows, channels = inputs[0].shape[-2:]
    heads = channels // HD
    slots = len(slot_in)
    n_in = len(inputs)

    def kernel(mask_ref, q_ref, g_ref, *refs):
        in_refs = refs[:n_in]
        dq_ref = refs[n_in]
        out_refs = refs[n_in + 1 :]
        nt = (((1,), (1,)), ((), ()))
        tn = (((0,), (0,)), ((), ()))
        for j in range(STEP_HEADS):
            cols = slice(j * HD, (j + 1) * HD)
            k = jnp.concatenate([in_refs[i][lead + (0, slice(None), cols)] for i, lead in slot_in], axis=0)
            v = jnp.concatenate([in_refs[i][lead + (1, slice(None), cols)] for i, lead in slot_in], axis=0)
            q = q_ref[:, cols]
            g = g_ref[:, cols]
            scores = lax.dot_general(q, k, nt, preferred_element_type=jnp.float32) * inv_root
            masked = jnp.where(mask_ref[...] != 0, scores, -1e30)
            highest = jnp.max(masked, axis=1, keepdims=True)
            total_mass = jnp.sum(jnp.exp(masked - highest), axis=1, keepdims=True)
            log_total = highest + jnp.log(total_mass)
            prob = jnp.exp(masked - log_total)
            prob_low = prob.astype(jnp.bfloat16)
            attended = jnp.dot(prob_low, v, preferred_element_type=jnp.float32)
            delta = jnp.sum(g.astype(jnp.float32) * attended, axis=1, keepdims=True)
            prob_grad = lax.dot_general(g, v, nt, preferred_element_type=jnp.float32)
            score_grad = (prob * (prob_grad - delta)).astype(jnp.bfloat16)
            dq = jnp.dot(score_grad, k, preferred_element_type=jnp.float32) * inv_root
            dq_ref[:, cols] = dq.astype(dq_ref.dtype)
            dk = lax.dot_general(score_grad, q, tn, preferred_element_type=jnp.float32) * inv_root
            dv = lax.dot_general(prob_low, g, tn, preferred_element_type=jnp.float32)
            for slot, (i, lead) in enumerate(slot_out):
                part = slice(slot * rows, (slot + 1) * rows)
                out_refs[i][lead + (0, slice(None), cols)] = dk[part].astype(jnp.bfloat16)
                out_refs[i][lead + (1, slice(None), cols)] = dv[part].astype(jnp.bfloat16)

    def head_spec(lead_shape):
        zeros = (0,) * len(lead_shape)
        return pl.BlockSpec(lead_shape + (2, rows, STEP_HEADS * HD), lambda h: zeros + (0, 0, h))

    in_specs = [
        pl.BlockSpec((rows, slots * rows), lambda h: (0, 0)),
        pl.BlockSpec((rows, STEP_HEADS * HD), lambda h: (0, h + offset // STEP_HEADS)),
        pl.BlockSpec((rows, STEP_HEADS * HD), lambda h: (0, h + offset // STEP_HEADS)),
    ] + [head_spec(tuple(x.shape[:-3])) for x in inputs]
    out_specs = [pl.BlockSpec((rows, STEP_HEADS * HD), lambda h: (0, h))] + [head_spec(lead) for lead in out_lead]
    out_shape = [jax.ShapeDtypeStruct((rows, channels), jnp.bfloat16)] + [
        jax.ShapeDtypeStruct(lead + (2, rows, channels), jnp.bfloat16) for lead in out_lead
    ]
    results = pl.pallas_call(
        kernel,
        grid=(heads // STEP_HEADS,),
        in_specs=in_specs,
        out_specs=out_specs,
        out_shape=out_shape,
        cost_estimate=pl.CostEstimate(
            flops=12 * heads * rows * slots * rows * HD,
            transcendentals=2 * heads * rows * slots * rows,
            bytes_accessed=2 * 4 * slots * rows * channels + 6 * rows * channels + 4 * rows * slots * rows,
        ),
    )(mask, queries, out_grad, *inputs)
    return results[0], results[1:]


def forward_relay(own, count, after):
    core, cross, down, up, diag_up, diag_down, back = route(count)
    if after is not None:
        own, _ = lax.optimization_barrier((own, after))
    from_cross = send(own, cross)
    from_below = send(own, up)
    from_above = send(own, down)
    return [own, from_cross, from_below, from_above]


def forward_second(first, count, after):
    core, cross, down, up, diag_up, diag_down, back = route(count)
    own, from_cross, from_below, from_above = first
    ahead = jnp.stack([own, from_cross, from_below, from_above])
    if after is not None:
        (ahead, from_cross), _ = lax.optimization_barrier(((ahead, from_cross), after))
    relayed = send(ahead, core)
    diag_from_below = send(from_cross, diag_up)
    diag_from_above = send(from_cross, diag_down)
    return first + [relayed, diag_from_below, diag_from_above]


def chunk_kernel(forward_mask, queries, out_grad, inputs, head_offset, inv_root):
    slot_in = [(0, ()), (4, (0,)), (1, ()), (2, ()), (3, ()), (4, (1,)), (4, (2,)), (4, (3,)), (5, ()), (6, ())]
    out_lead = [(), (4,), (), (), (), (), ()]
    slot_out = [(0, ()), (1, (0,)), (2, ()), (3, ()), (4, ()), (1, (1,)), (1, (2,)), (1, (3,)), (5, ()), (6, ())]
    return attention_backward(
        forward_mask, queries, out_grad, inputs, slot_in, out_lead, slot_out, inv_root, head_offset
    )


def return_first(outs, count, after):
    core, cross, down, up, diag_up, diag_down, back = route(count)
    own_part, to_core, cross_part, below_part, above_part, diag_b_part, diag_a_part = outs
    if after is not None:
        (to_core, diag_b_part, diag_a_part), _ = lax.optimization_barrier(
            ((to_core, diag_b_part, diag_a_part), after)
        )
    to_partner = send(to_core, core)
    diag_back_below = send(diag_b_part, back(diag_up))
    diag_back_above = send(diag_a_part, back(diag_down))
    return [to_partner, diag_back_below, diag_back_above]


def return_second(outs, first, count, after):
    core, cross, down, up, diag_up, diag_down, back = route(count)
    own_part, to_core, cross_part, below_part, above_part, diag_b_part, diag_a_part = outs
    to_partner, diag_back_below, diag_back_above = first
    wide = lambda tensor: tensor.astype(jnp.float32)
    cross_sum = wide(cross_part) + wide(to_partner[1]) + wide(diag_back_below) + wide(diag_back_above)
    below_sum = wide(below_part) + wide(to_partner[2])
    above_sum = wide(above_part) + wide(to_partner[3])
    sums = (cross_sum.astype(jnp.bfloat16), below_sum.astype(jnp.bfloat16), above_sum.astype(jnp.bfloat16))
    if after is not None:
        sums, _ = lax.optimization_barrier((sums, after))
    got_cross = send(sums[0], cross)
    got_below = send(sums[1], down)
    got_above = send(sums[2], up)
    summed = wide(own_part) + wide(to_partner[0]) + wide(got_cross) + wide(got_below) + wide(got_above)
    return [got_cross, got_below, got_above], summed


def body(queries, keys, values, out_grad, frame_keep, band_window):
    rows_own, channel_total = queries.shape
    frame_len = QUARTERS * rows_own
    inv_root = 1.0 / math.sqrt(HD)
    count = lax.axis_size("tm")
    device = lax.axis_index("tm")
    quarter = device % QUARTERS
    partner = device ^ 1

    middle = (quarter == 1) | (quarter == 2)
    diag_quarter = QUARTERS - 1 - quarter
    absent = jnp.int32(-(1 << 20))
    sources = [
        device,
        partner,
        device ^ 2,
        device - QUARTERS,
        device + QUARTERS,
        device ^ 3,
        partner - QUARTERS,
        partner + QUARTERS,
        jnp.where(middle, device - quarter - QUARTERS + diag_quarter, absent),
        jnp.where(middle, device - quarter + QUARTERS + diag_quarter, absent),
    ]
    base_rows = jnp.arange(rows_own, dtype=jnp.int32)
    far_rows = jnp.concatenate([source * rows_own + base_rows for source in sources])
    own_rows = device * rows_own + base_rows
    forward_mask = allowed(own_rows, far_rows, frame_keep, band_window, frame_len).astype(jnp.int32)
    heads = channel_total // HD
    lead_heads = (heads * 3 // 10) // STEP_HEADS * STEP_HEADS
    if lead_heads < STEP_HEADS or heads % STEP_HEADS:
        lead_heads = heads
    bounds = [0, lead_heads * HD, channel_total] if lead_heads < heads else [0, channel_total]
    starts = bounds[:-1]
    widths = [b - a for a, b in zip(bounds[:-1], bounds[1:])]
    firsts, seconds, outs, backs, sums, dqs = [], [], [], [], [], []
    for c, first in enumerate(starts):
        width = widths[c]
        own = jnp.stack([keys[:, first : first + width], values[:, first : first + width]])
        firsts.append(forward_relay(own, count, None))
    for c in range(len(starts)):
        seconds.append(forward_second(firsts[c], count, None))
    for c, first in enumerate(starts):
        dq, parts = chunk_kernel(forward_mask, queries, out_grad, seconds[c], first // HD, inv_root)
        dqs.append(dq)
        outs.append(parts)
    for c in range(len(starts)):
        backs.append(return_first(outs[c], count, None))
    got = None
    for c in range(len(starts)):
        got, summed = return_second(outs[c], backs[c], count, None)
        sums.append(summed)
    grads = [(dqs[c], sums[c][0].astype(jnp.bfloat16), sums[c][1].astype(jnp.bfloat16)) for c in range(len(starts))]
    query_grad = jnp.concatenate([grad[0] for grad in grads], axis=1)
    key_grad = jnp.concatenate([grad[1] for grad in grads], axis=1)
    value_grad = jnp.concatenate([grad[2] for grad in grads], axis=1)
    return (query_grad, key_grad, value_grad)


def solution(mesh):
    placed = (
        P(("group", "tm"), None),
        P(("group", "tm"), None),
        P(("group", "tm"), None),
        P(("group", "tm"), None),
        P("group", None),
        P("group"),
    )
    return jax.shard_map(
        body,
        mesh=mesh,
        in_specs=placed,
        out_specs=(P(("group", "tm"), None), P(("group", "tm"), None), P(("group", "tm"), None)),
        check_vma=False,
    )
```

```python
import math

import jax
import jax.numpy as jnp
from jax import lax
from jax.experimental import pallas as pl
from jax.sharding import PartitionSpec as P

HD = 128
QUARTERS = 4
CHUNKS = 3
STEP_HEADS = 2


def send(value, pairs):
    return lax.ppermute(value, "tm", pairs)


def pairs_of(count, target):
    pairs = []
    for source in range(count):
        dest = target(source)
        if dest is not None and 0 <= dest < count:
            pairs.append((source, dest))
    return pairs


def route(count):
    core = pairs_of(count, lambda t: t ^ 1)
    cross = pairs_of(count, lambda t: t ^ 2)
    down = pairs_of(count, lambda t: t - QUARTERS)
    up = pairs_of(count, lambda t: t + QUARTERS)

    def diag(step):
        def target(t):
            q = t % QUARTERS
            if q == 0:
                return t + step * QUARTERS + 1
            if q == QUARTERS - 1:
                return t + step * QUARTERS - 1
            return None

        return pairs_of(count, target)

    diag_up = diag(1)
    diag_down = diag(-1)
    back = lambda pairs: [(dest, source) for source, dest in pairs]
    return core, cross, down, up, diag_up, diag_down, back


def allowed(query_rows, key_rows, frame_keep, band_window, frame_len):
    frame_count = frame_keep.shape[0]
    query_frame = jnp.floor_divide(query_rows, frame_len)
    key_frame = jnp.floor_divide(key_rows, frame_len)
    query_place = query_rows - query_frame * frame_len
    key_place = key_rows - key_frame * frame_len
    query_inside = (query_rows >= 0) & (query_rows < frame_count * frame_len)
    key_inside = (key_rows >= 0) & (key_rows < frame_count * frame_len)
    inside = query_inside[:, None] & key_inside[None, :]
    onehot = (query_frame[:, None] == jnp.arange(frame_count, dtype=jnp.int32)[None, :]).astype(
        jnp.int32
    )
    keep_rows = jnp.sum(onehot[:, :, None] * frame_keep[None, :, :], axis=1)
    window_rows = jnp.sum(onehot * band_window[None, :], axis=1)
    frame_gap = key_frame[None, :] - query_frame[:, None]
    kept_pair = jnp.zeros(frame_gap.shape, jnp.int32)
    for column in range(3):
        kept_pair = kept_pair + jnp.where(
            frame_gap == column - 1, keep_rows[:, column : column + 1], 0
        )
    place_gap = jnp.abs(query_place[:, None] - key_place[None, :])
    nearby = (frame_gap == 0) | (place_gap <= window_rows[:, None])
    return inside & (kept_pair > 0) & nearby


def attention_backward(mask, queries, out_grad, inputs, slot_in, out_lead, slot_out, inv_root, offset):
    rows, channels = inputs[0].shape[-2:]
    heads = channels // HD
    slots = len(slot_in)
    n_in = len(inputs)

    def kernel(mask_ref, q_ref, g_ref, *refs):
        in_refs = refs[:n_in]
        dq_ref = refs[n_in]
        out_refs = refs[n_in + 1 :]
        nt = (((1,), (1,)), ((), ()))
        tn = (((0,), (0,)), ((), ()))
        for j in range(STEP_HEADS):
            cols = slice(j * HD, (j + 1) * HD)
            k = jnp.concatenate([in_refs[i][lead + (0, slice(None), cols)] for i, lead in slot_in], axis=0)
            v = jnp.concatenate([in_refs[i][lead + (1, slice(None), cols)] for i, lead in slot_in], axis=0)
            q = q_ref[:, cols]
            g = g_ref[:, cols]
            scores = lax.dot_general(q, k, nt, preferred_element_type=jnp.float32) * inv_root
            masked = jnp.where(mask_ref[...] != 0, scores, -1e30)
            highest = jnp.max(masked, axis=1, keepdims=True)
            total_mass = jnp.sum(jnp.exp(masked - highest), axis=1, keepdims=True)
            log_total = highest + jnp.log(total_mass)
            prob = jnp.exp(masked - log_total)
            prob_low = prob.astype(jnp.bfloat16)
            attended = jnp.dot(prob_low, v, preferred_element_type=jnp.float32)
            delta = jnp.sum(g.astype(jnp.float32) * attended, axis=1, keepdims=True)
            prob_grad = lax.dot_general(g, v, nt, preferred_element_type=jnp.float32)
            score_grad = (prob * (prob_grad - delta)).astype(jnp.bfloat16)
            dq = jnp.dot(score_grad, k, preferred_element_type=jnp.float32) * inv_root
            dq_ref[:, cols] = dq.astype(dq_ref.dtype)
            dk = lax.dot_general(score_grad, q, tn, preferred_element_type=jnp.float32) * inv_root
            dv = lax.dot_general(prob_low, g, tn, preferred_element_type=jnp.float32)
            for slot, (i, lead) in enumerate(slot_out):
                part = slice(slot * rows, (slot + 1) * rows)
                out_refs[i][lead + (0, slice(None), cols)] = dk[part].astype(jnp.bfloat16)
                out_refs[i][lead + (1, slice(None), cols)] = dv[part].astype(jnp.bfloat16)

    def head_spec(lead_shape):
        zeros = (0,) * len(lead_shape)
        return pl.BlockSpec(lead_shape + (2, rows, STEP_HEADS * HD), lambda h: zeros + (0, 0, h))

    in_specs = [
        pl.BlockSpec((rows, slots * rows), lambda h: (0, 0)),
        pl.BlockSpec((rows, STEP_HEADS * HD), lambda h: (0, h + offset // STEP_HEADS)),
        pl.BlockSpec((rows, STEP_HEADS * HD), lambda h: (0, h + offset // STEP_HEADS)),
    ] + [head_spec(tuple(x.shape[:-3])) for x in inputs]
    out_specs = [pl.BlockSpec((rows, STEP_HEADS * HD), lambda h: (0, h))] + [head_spec(lead) for lead in out_lead]
    out_shape = [jax.ShapeDtypeStruct((rows, channels), jnp.bfloat16)] + [
        jax.ShapeDtypeStruct(lead + (2, rows, channels), jnp.bfloat16) for lead in out_lead
    ]
    results = pl.pallas_call(
        kernel,
        grid=(heads // STEP_HEADS,),
        in_specs=in_specs,
        out_specs=out_specs,
        out_shape=out_shape,
        cost_estimate=pl.CostEstimate(
            flops=12 * heads * rows * slots * rows * HD,
            transcendentals=2 * heads * rows * slots * rows,
            bytes_accessed=2 * 4 * slots * rows * channels + 6 * rows * channels + 4 * rows * slots * rows,
        ),
    )(mask, queries, out_grad, *inputs)
    return results[0], results[1:]


def forward_relay(own, count, after):
    core, cross, down, up, diag_up, diag_down, back = route(count)
    if after is not None:
        own, _ = lax.optimization_barrier((own, after))
    from_cross = send(own, cross)
    from_below = send(own, up)
    from_above = send(own, down)
    return [own, from_cross, from_below, from_above]


def forward_second(first, count, after):
    core, cross, down, up, diag_up, diag_down, back = route(count)
    own, from_cross, from_below, from_above = first
    ahead = jnp.stack([own, from_cross, from_below, from_above])
    if after is not None:
        (ahead, from_cross), _ = lax.optimization_barrier(((ahead, from_cross), after))
    relayed = send(ahead, core)
    diag_from_below = send(from_cross, diag_up)
    diag_from_above = send(from_cross, diag_down)
    return first + [relayed, diag_from_below, diag_from_above]


def chunk_kernel(forward_mask, queries, out_grad, inputs, head_offset, inv_root):
    slot_in = [(0, ()), (4, (0,)), (1, ()), (2, ()), (3, ()), (4, (1,)), (4, (2,)), (4, (3,)), (5, ()), (6, ())]
    out_lead = [(), (4,), (), (), (), (), ()]
    slot_out = [(0, ()), (1, (0,)), (2, ()), (3, ()), (4, ()), (1, (1,)), (1, (2,)), (1, (3,)), (5, ()), (6, ())]
    return attention_backward(
        forward_mask, queries, out_grad, inputs, slot_in, out_lead, slot_out, inv_root, head_offset
    )


def return_first(outs, count, after):
    core, cross, down, up, diag_up, diag_down, back = route(count)
    own_part, to_core, cross_part, below_part, above_part, diag_b_part, diag_a_part = outs
    if after is not None:
        (to_core, diag_b_part, diag_a_part), _ = lax.optimization_barrier(
            ((to_core, diag_b_part, diag_a_part), after)
        )
    to_partner = send(to_core, core)
    diag_back_below = send(diag_b_part, back(diag_up))
    diag_back_above = send(diag_a_part, back(diag_down))
    return [to_partner, diag_back_below, diag_back_above]


def return_second(outs, first, count, after):
    core, cross, down, up, diag_up, diag_down, back = route(count)
    own_part, to_core, cross_part, below_part, above_part, diag_b_part, diag_a_part = outs
    to_partner, diag_back_below, diag_back_above = first
    wide = lambda tensor: tensor.astype(jnp.float32)
    cross_sum = wide(cross_part) + wide(to_partner[1]) + wide(diag_back_below) + wide(diag_back_above)
    below_sum = wide(below_part) + wide(to_partner[2])
    above_sum = wide(above_part) + wide(to_partner[3])
    sums = (cross_sum.astype(jnp.bfloat16), below_sum.astype(jnp.bfloat16), above_sum.astype(jnp.bfloat16))
    if after is not None:
        sums, _ = lax.optimization_barrier((sums, after))
    got_cross = send(sums[0], cross)
    got_below = send(sums[1], down)
    got_above = send(sums[2], up)
    summed = wide(own_part) + wide(to_partner[0]) + wide(got_cross) + wide(got_below) + wide(got_above)
    return [got_cross, got_below, got_above], summed


def body(queries, keys, values, out_grad, frame_keep, band_window):
    rows_own, channel_total = queries.shape
    frame_len = QUARTERS * rows_own
    inv_root = 1.0 / math.sqrt(HD)
    count = lax.axis_size("tm")
    device = lax.axis_index("tm")
    quarter = device % QUARTERS
    partner = device ^ 1

    middle = (quarter == 1) | (quarter == 2)
    diag_quarter = QUARTERS - 1 - quarter
    absent = jnp.int32(-(1 << 20))
    sources = [
        device,
        partner,
        device ^ 2,
        device - QUARTERS,
        device + QUARTERS,
        device ^ 3,
        partner - QUARTERS,
        partner + QUARTERS,
        jnp.where(middle, device - quarter - QUARTERS + diag_quarter, absent),
        jnp.where(middle, device - quarter + QUARTERS + diag_quarter, absent),
    ]
    base_rows = jnp.arange(rows_own, dtype=jnp.int32)
    far_rows = jnp.concatenate([source * rows_own + base_rows for source in sources])
    own_rows = device * rows_own + base_rows
    forward_mask = allowed(own_rows, far_rows, frame_keep, band_window, frame_len).astype(jnp.int32)
    heads = channel_total // HD
    units = heads // STEP_HEADS if heads % STEP_HEADS == 0 else 0
    pieces = min(CHUNKS, units) if units else 1
    cuts = [(units * k // pieces) * STEP_HEADS * HD for k in range(pieces + 1)] if units else [0, channel_total]
    starts = cuts[:-1]
    widths = [b - a for a, b in zip(cuts[:-1], cuts[1:])]
    firsts, seconds, outs, backs, sums, dqs = [], [], [], [], [], []
    for c, first in enumerate(starts):
        width = widths[c]
        own = jnp.stack([keys[:, first : first + width], values[:, first : first + width]])
        firsts.append(forward_relay(own, count, None))
    for c in range(len(starts)):
        seconds.append(forward_second(firsts[c], count, None))
    for c, first in enumerate(starts):
        dq, parts = chunk_kernel(forward_mask, queries, out_grad, seconds[c], first // HD, inv_root)
        dqs.append(dq)
        outs.append(parts)
    for c in range(len(starts)):
        backs.append(return_first(outs[c], count, None))
    got = None
    for c in range(len(starts)):
        got, summed = return_second(outs[c], backs[c], count, None)
        sums.append(summed)
    grads = [(dqs[c], sums[c][0].astype(jnp.bfloat16), sums[c][1].astype(jnp.bfloat16)) for c in range(len(starts))]
    query_grad = jnp.concatenate([grad[0] for grad in grads], axis=1)
    key_grad = jnp.concatenate([grad[1] for grad in grads], axis=1)
    value_grad = jnp.concatenate([grad[2] for grad in grads], axis=1)
    return (query_grad, key_grad, value_grad)


def solution(mesh):
    placed = (
        P(("group", "tm"), None),
        P(("group", "tm"), None),
        P(("group", "tm"), None),
        P(("group", "tm"), None),
        P("group", None),
        P("group"),
    )
    return jax.shard_map(
        body,
        mesh=mesh,
        in_specs=placed,
        out_specs=(P(("group", "tm"), None), P(("group", "tm"), None), P(("group", "tm"), None)),
        check_vma=False,
    )
```

```python
import math

import jax
import jax.numpy as jnp
from jax import lax
from jax.experimental import pallas as pl
from jax.sharding import PartitionSpec as P

HD = 128
QUARTERS = 4
CHUNKS = 2
STEP_HEADS = 2


def send(value, pairs):
    return lax.ppermute(value, "tm", pairs)


def pairs_of(count, target):
    pairs = []
    for source in range(count):
        dest = target(source)
        if dest is not None and 0 <= dest < count:
            pairs.append((source, dest))
    return pairs


def route(count):
    core = pairs_of(count, lambda t: t ^ 1)
    cross = pairs_of(count, lambda t: t ^ 2)
    down = pairs_of(count, lambda t: t - QUARTERS)
    up = pairs_of(count, lambda t: t + QUARTERS)

    def diag(step):
        def target(t):
            q = t % QUARTERS
            if q == 0:
                return t + step * QUARTERS + 1
            if q == QUARTERS - 1:
                return t + step * QUARTERS - 1
            return None

        return pairs_of(count, target)

    diag_up = diag(1)
    diag_down = diag(-1)
    back = lambda pairs: [(dest, source) for source, dest in pairs]
    return core, cross, down, up, diag_up, diag_down, back


def allowed(query_rows, key_rows, frame_keep, band_window, frame_len):
    frame_count = frame_keep.shape[0]
    query_frame = jnp.floor_divide(query_rows, frame_len)
    key_frame = jnp.floor_divide(key_rows, frame_len)
    query_place = query_rows - query_frame * frame_len
    key_place = key_rows - key_frame * frame_len
    query_inside = (query_rows >= 0) & (query_rows < frame_count * frame_len)
    key_inside = (key_rows >= 0) & (key_rows < frame_count * frame_len)
    inside = query_inside[:, None] & key_inside[None, :]
    onehot = (query_frame[:, None] == jnp.arange(frame_count, dtype=jnp.int32)[None, :]).astype(
        jnp.int32
    )
    keep_rows = jnp.sum(onehot[:, :, None] * frame_keep[None, :, :], axis=1)
    window_rows = jnp.sum(onehot * band_window[None, :], axis=1)
    frame_gap = key_frame[None, :] - query_frame[:, None]
    kept_pair = jnp.zeros(frame_gap.shape, jnp.int32)
    for column in range(3):
        kept_pair = kept_pair + jnp.where(
            frame_gap == column - 1, keep_rows[:, column : column + 1], 0
        )
    place_gap = jnp.abs(query_place[:, None] - key_place[None, :])
    nearby = (frame_gap == 0) | (place_gap <= window_rows[:, None])
    return inside & (kept_pair > 0) & nearby


def attention_backward(mask, queries, out_grad, inputs, slot_in, out_lead, slot_out, inv_root, offset):
    rows, channels = inputs[0].shape[-2:]
    heads = channels // HD
    slots = len(slot_in)
    n_in = len(inputs)

    def kernel(mask_ref, q_ref, g_ref, *refs):
        in_refs = refs[:n_in]
        dq_ref = refs[n_in]
        out_refs = refs[n_in + 1 :]
        nt = (((1,), (1,)), ((), ()))
        tn = (((0,), (0,)), ((), ()))
        for j in range(STEP_HEADS):
            cols = slice(j * HD, (j + 1) * HD)
            k = jnp.concatenate([in_refs[i][lead + (0, slice(None), cols)] for i, lead in slot_in], axis=0)
            v = jnp.concatenate([in_refs[i][lead + (1, slice(None), cols)] for i, lead in slot_in], axis=0)
            q = q_ref[:, cols]
            g = g_ref[:, cols]
            scores = lax.dot_general(q, k, nt, preferred_element_type=jnp.float32) * inv_root
            masked = jnp.where(mask_ref[...] != 0, scores, -1e30)
            highest = jnp.max(masked, axis=1, keepdims=True)
            total_mass = jnp.sum(jnp.exp(masked - highest), axis=1, keepdims=True)
            log_total = highest + jnp.log(total_mass)
            prob = jnp.exp(masked - log_total)
            prob_low = prob.astype(jnp.bfloat16)
            attended = jnp.dot(prob_low, v, preferred_element_type=jnp.float32)
            delta = jnp.sum(g.astype(jnp.float32) * attended, axis=1, keepdims=True)
            prob_grad = lax.dot_general(g, v, nt, preferred_element_type=jnp.float32)
            score_grad = (prob * (prob_grad - delta)).astype(jnp.bfloat16)
            dq = jnp.dot(score_grad, k, preferred_element_type=jnp.float32) * inv_root
            dq_ref[:, cols] = dq.astype(dq_ref.dtype)
            dk = lax.dot_general(score_grad, q, tn, preferred_element_type=jnp.float32) * inv_root
            dv = lax.dot_general(prob_low, g, tn, preferred_element_type=jnp.float32)
            for slot, (i, lead) in enumerate(slot_out):
                part = slice(slot * rows, (slot + 1) * rows)
                out_refs[i][lead + (0, slice(None), cols)] = dk[part].astype(jnp.bfloat16)
                out_refs[i][lead + (1, slice(None), cols)] = dv[part].astype(jnp.bfloat16)

    def head_spec(lead_shape):
        zeros = (0,) * len(lead_shape)
        return pl.BlockSpec(lead_shape + (2, rows, STEP_HEADS * HD), lambda h: zeros + (0, 0, h))

    in_specs = [
        pl.BlockSpec((rows, slots * rows), lambda h: (0, 0)),
        pl.BlockSpec((rows, STEP_HEADS * HD), lambda h: (0, h + offset // STEP_HEADS)),
        pl.BlockSpec((rows, STEP_HEADS * HD), lambda h: (0, h + offset // STEP_HEADS)),
    ] + [head_spec(tuple(x.shape[:-3])) for x in inputs]
    out_specs = [pl.BlockSpec((rows, STEP_HEADS * HD), lambda h: (0, h))] + [head_spec(lead) for lead in out_lead]
    out_shape = [jax.ShapeDtypeStruct((rows, channels), jnp.bfloat16)] + [
        jax.ShapeDtypeStruct(lead + (2, rows, channels), jnp.bfloat16) for lead in out_lead
    ]
    results = pl.pallas_call(
        kernel,
        grid=(heads // STEP_HEADS,),
        in_specs=in_specs,
        out_specs=out_specs,
        out_shape=out_shape,
        cost_estimate=pl.CostEstimate(
            flops=12 * heads * rows * slots * rows * HD,
            transcendentals=2 * heads * rows * slots * rows,
            bytes_accessed=2 * 4 * slots * rows * channels + 6 * rows * channels + 4 * rows * slots * rows,
        ),
    )(mask, queries, out_grad, *inputs)
    return results[0], results[1:]


def forward_relay(own, count, after):
    core, cross, down, up, diag_up, diag_down, back = route(count)
    if after is not None:
        own, _ = lax.optimization_barrier((own, after))
    from_cross = send(own, cross)
    from_below = send(own, up)
    from_above = send(own, down)
    return [own, from_cross, from_below, from_above]


def forward_second(first, count, after):
    core, cross, down, up, diag_up, diag_down, back = route(count)
    own, from_cross, from_below, from_above = first
    relayed = [send(block, core) for block in first]
    diag_from_below = send(from_cross, diag_up)
    diag_from_above = send(from_cross, diag_down)
    return first + relayed + [diag_from_below, diag_from_above]


def chunk_kernel(forward_mask, queries, out_grad, inputs, head_offset, inv_root):
    slot_in = [(0, ()), (4, ()), (1, ()), (2, ()), (3, ()), (5, ()), (6, ()), (7, ()), (8, ()), (9, ())]
    out_lead = [(), (4,), (), (), (), (), ()]
    slot_out = [(0, ()), (1, (0,)), (2, ()), (3, ()), (4, ()), (1, (1,)), (1, (2,)), (1, (3,)), (5, ()), (6, ())]
    return attention_backward(
        forward_mask, queries, out_grad, inputs, slot_in, out_lead, slot_out, inv_root, head_offset
    )


def return_first(outs, count, after):
    core, cross, down, up, diag_up, diag_down, back = route(count)
    own_part, to_core, cross_part, below_part, above_part, diag_b_part, diag_a_part = outs
    if after is not None:
        (to_core, diag_b_part, diag_a_part), _ = lax.optimization_barrier(
            ((to_core, diag_b_part, diag_a_part), after)
        )
    to_partner = send(to_core, core)
    diag_back_below = send(diag_b_part, back(diag_up))
    diag_back_above = send(diag_a_part, back(diag_down))
    return [to_partner, diag_back_below, diag_back_above]


def return_second(outs, first, count, after):
    core, cross, down, up, diag_up, diag_down, back = route(count)
    own_part, to_core, cross_part, below_part, above_part, diag_b_part, diag_a_part = outs
    to_partner, diag_back_below, diag_back_above = first
    wide = lambda tensor: tensor.astype(jnp.float32)
    cross_sum = wide(cross_part) + wide(to_partner[1]) + wide(diag_back_below) + wide(diag_back_above)
    below_sum = wide(below_part) + wide(to_partner[2])
    above_sum = wide(above_part) + wide(to_partner[3])
    sums = (cross_sum.astype(jnp.bfloat16), below_sum.astype(jnp.bfloat16), above_sum.astype(jnp.bfloat16))
    if after is not None:
        sums, _ = lax.optimization_barrier((sums, after))
    got_cross = send(sums[0], cross)
    got_below = send(sums[1], down)
    got_above = send(sums[2], up)
    summed = wide(own_part) + wide(to_partner[0]) + wide(got_cross) + wide(got_below) + wide(got_above)
    return [got_cross, got_below, got_above], summed


def body(queries, keys, values, out_grad, frame_keep, band_window):
    rows_own, channel_total = queries.shape
    frame_len = QUARTERS * rows_own
    inv_root = 1.0 / math.sqrt(HD)
    count = lax.axis_size("tm")
    device = lax.axis_index("tm")
    quarter = device % QUARTERS
    partner = device ^ 1

    middle = (quarter == 1) | (quarter == 2)
    diag_quarter = QUARTERS - 1 - quarter
    absent = jnp.int32(-(1 << 20))
    sources = [
        device,
        partner,
        device ^ 2,
        device - QUARTERS,
        device + QUARTERS,
        device ^ 3,
        partner - QUARTERS,
        partner + QUARTERS,
        jnp.where(middle, device - quarter - QUARTERS + diag_quarter, absent),
        jnp.where(middle, device - quarter + QUARTERS + diag_quarter, absent),
    ]
    base_rows = jnp.arange(rows_own, dtype=jnp.int32)
    far_rows = jnp.concatenate([source * rows_own + base_rows for source in sources])
    own_rows = device * rows_own + base_rows
    forward_mask = allowed(own_rows, far_rows, frame_keep, band_window, frame_len).astype(jnp.int32)
    heads = channel_total // HD
    chunk_heads = heads // CHUNKS if heads % CHUNKS == 0 else heads
    width = chunk_heads * HD
    starts = list(range(0, channel_total, width))
    firsts, seconds, outs, backs, sums, dqs = [], [], [], [], [], []
    for c, first in enumerate(starts):
        own = jnp.stack([keys[:, first : first + width], values[:, first : first + width]])
        firsts.append(forward_relay(own, count, None))
    for c in range(len(starts)):
        seconds.append(forward_second(firsts[c], count, None))
    for c, first in enumerate(starts):
        dq, parts = chunk_kernel(forward_mask, queries, out_grad, seconds[c], first // HD, inv_root)
        dqs.append(dq)
        outs.append(parts)
    for c in range(len(starts)):
        backs.append(return_first(outs[c], count, None))
    got = None
    for c in range(len(starts)):
        got, summed = return_second(outs[c], backs[c], count, None)
        sums.append(summed)
    grads = [(dqs[c], sums[c][0].astype(jnp.bfloat16), sums[c][1].astype(jnp.bfloat16)) for c in range(len(starts))]
    query_grad = jnp.concatenate([grad[0] for grad in grads], axis=1)
    key_grad = jnp.concatenate([grad[1] for grad in grads], axis=1)
    value_grad = jnp.concatenate([grad[2] for grad in grads], axis=1)
    return (query_grad, key_grad, value_grad)


def solution(mesh):
    placed = (
        P(("group", "tm"), None),
        P(("group", "tm"), None),
        P(("group", "tm"), None),
        P(("group", "tm"), None),
        P("group", None),
        P("group"),
    )
    return jax.shard_map(
        body,
        mesh=mesh,
        in_specs=placed,
        out_specs=(P(("group", "tm"), None), P(("group", "tm"), None), P(("group", "tm"), None)),
        check_vma=False,
    )
```

```python
import math

import jax
import jax.numpy as jnp
from jax import lax
from jax.experimental import pallas as pl
from jax.sharding import PartitionSpec as P

HD = 128
QUARTERS = 4
CHUNKS = 2
STEP_HEADS = 2


def send(value, pairs):
    return lax.ppermute(value, "tm", pairs)


def pairs_of(count, target):
    pairs = []
    for source in range(count):
        dest = target(source)
        if dest is not None and 0 <= dest < count:
            pairs.append((source, dest))
    return pairs


def route(count):
    core = pairs_of(count, lambda t: t ^ 1)
    cross = pairs_of(count, lambda t: t ^ 2)
    down = pairs_of(count, lambda t: t - QUARTERS)
    up = pairs_of(count, lambda t: t + QUARTERS)

    def diag(step):
        def target(t):
            q = t % QUARTERS
            if q == 0:
                return t + step * QUARTERS + 1
            if q == QUARTERS - 1:
                return t + step * QUARTERS - 1
            return None

        return pairs_of(count, target)

    diag_up = diag(1)
    diag_down = diag(-1)
    back = lambda pairs: [(dest, source) for source, dest in pairs]
    return core, cross, down, up, diag_up, diag_down, back


def allowed(query_rows, key_rows, frame_keep, band_window, frame_len):
    frame_count = frame_keep.shape[0]
    query_frame = jnp.floor_divide(query_rows[0], frame_len)
    query_place = query_rows - query_frame * frame_len
    key_frame = jnp.floor_divide(key_rows, frame_len)
    key_place = key_rows - key_frame * frame_len
    query_inside = (query_rows >= 0) & (query_rows < frame_count * frame_len)
    key_inside = (key_rows >= 0) & (key_rows < frame_count * frame_len)
    keep = lax.dynamic_index_in_dim(frame_keep, query_frame, 0, keepdims=False)
    window = lax.dynamic_index_in_dim(band_window, query_frame, 0, keepdims=False)
    frame_gap = key_frame - query_frame
    kept_pair = jnp.zeros(frame_gap.shape, jnp.int32)
    for column in range(3):
        kept_pair = kept_pair + jnp.where(frame_gap == column - 1, keep[column], 0)
    key_ok = key_inside & (kept_pair > 0)
    place_gap = jnp.abs(query_place[:, None] - key_place[None, :])
    nearby = (frame_gap == 0)[None, :] | (place_gap <= window)
    return query_inside[:, None] & key_ok[None, :] & nearby


def attention_backward(mask, queries, out_grad, inputs, slot_in, out_lead, slot_out, inv_root, offset):
    rows, channels = inputs[0].shape[-2:]
    heads = channels // HD
    slots = len(slot_in)
    n_in = len(inputs)

    def kernel(mask_ref, q_ref, g_ref, *refs):
        in_refs = refs[:n_in]
        dq_ref = refs[n_in]
        out_refs = refs[n_in + 1 :]
        nt = (((1,), (1,)), ((), ()))
        tn = (((0,), (0,)), ((), ()))
        for j in range(STEP_HEADS):
            cols = slice(j * HD, (j + 1) * HD)
            k = jnp.concatenate([in_refs[i][lead + (0, slice(None), cols)] for i, lead in slot_in], axis=0)
            v = jnp.concatenate([in_refs[i][lead + (1, slice(None), cols)] for i, lead in slot_in], axis=0)
            q = q_ref[:, cols]
            g = g_ref[:, cols]
            scores = lax.dot_general(q, k, nt, preferred_element_type=jnp.float32) * inv_root
            masked = jnp.where(mask_ref[...] != 0, scores, -1e30)
            highest = jnp.max(masked, axis=1, keepdims=True)
            total_mass = jnp.sum(jnp.exp(masked - highest), axis=1, keepdims=True)
            log_total = highest + jnp.log(total_mass)
            prob = jnp.exp(masked - log_total)
            prob_low = prob.astype(jnp.bfloat16)
            attended = jnp.dot(prob_low, v, preferred_element_type=jnp.float32)
            delta = jnp.sum(g.astype(jnp.float32) * attended, axis=1, keepdims=True)
            prob_grad = lax.dot_general(g, v, nt, preferred_element_type=jnp.float32)
            score_grad = (prob * (prob_grad - delta)).astype(jnp.bfloat16)
            dq = jnp.dot(score_grad, k, preferred_element_type=jnp.float32) * inv_root
            dq_ref[:, cols] = dq.astype(dq_ref.dtype)
            dk = lax.dot_general(score_grad, q, tn, preferred_element_type=jnp.float32) * inv_root
            dv = lax.dot_general(prob_low, g, tn, preferred_element_type=jnp.float32)
            for slot, (i, lead) in enumerate(slot_out):
                part = slice(slot * rows, (slot + 1) * rows)
                out_refs[i][lead + (0, slice(None), cols)] = dk[part].astype(jnp.bfloat16)
                out_refs[i][lead + (1, slice(None), cols)] = dv[part].astype(jnp.bfloat16)

    def head_spec(lead_shape):
        zeros = (0,) * len(lead_shape)
        return pl.BlockSpec(lead_shape + (2, rows, STEP_HEADS * HD), lambda h: zeros + (0, 0, h))

    in_specs = [
        pl.BlockSpec((rows, slots * rows), lambda h: (0, 0)),
        pl.BlockSpec((rows, STEP_HEADS * HD), lambda h: (0, h + offset // STEP_HEADS)),
        pl.BlockSpec((rows, STEP_HEADS * HD), lambda h: (0, h + offset // STEP_HEADS)),
    ] + [head_spec(tuple(x.shape[:-3])) for x in inputs]
    out_specs = [pl.BlockSpec((rows, STEP_HEADS * HD), lambda h: (0, h))] + [head_spec(lead) for lead in out_lead]
    out_shape = [jax.ShapeDtypeStruct((rows, channels), jnp.bfloat16)] + [
        jax.ShapeDtypeStruct(lead + (2, rows, channels), jnp.bfloat16) for lead in out_lead
    ]
    results = pl.pallas_call(
        kernel,
        grid=(heads // STEP_HEADS,),
        in_specs=in_specs,
        out_specs=out_specs,
        out_shape=out_shape,
        cost_estimate=pl.CostEstimate(
            flops=12 * heads * rows * slots * rows * HD,
            transcendentals=2 * heads * rows * slots * rows,
            bytes_accessed=2 * 4 * slots * rows * channels + 6 * rows * channels + 4 * rows * slots * rows,
        ),
    )(mask, queries, out_grad, *inputs)
    return results[0], results[1:]


def forward_relay(own, count, after):
    core, cross, down, up, diag_up, diag_down, back = route(count)
    if after is not None:
        own, _ = lax.optimization_barrier((own, after))
    from_cross = send(own, cross)
    from_below = send(own, up)
    from_above = send(own, down)
    return [own, from_cross, from_below, from_above]


def forward_second(first, count, after):
    core, cross, down, up, diag_up, diag_down, back = route(count)
    own, from_cross, from_below, from_above = first
    relayed = [send(block, core) for block in first]
    diag_from_below = send(from_cross, diag_up)
    diag_from_above = send(from_cross, diag_down)
    return first + relayed + [diag_from_below, diag_from_above]


def chunk_kernel(forward_mask, queries, out_grad, inputs, head_offset, inv_root):
    slot_in = [(0, ()), (4, ()), (1, ()), (2, ()), (3, ()), (5, ()), (6, ()), (7, ()), (8, ()), (9, ())]
    out_lead = [(), (4,), (), (), (), (), ()]
    slot_out = [(0, ()), (1, (0,)), (2, ()), (3, ()), (4, ()), (1, (1,)), (1, (2,)), (1, (3,)), (5, ()), (6, ())]
    return attention_backward(
        forward_mask, queries, out_grad, inputs, slot_in, out_lead, slot_out, inv_root, head_offset
    )


def return_first(outs, count, after):
    core, cross, down, up, diag_up, diag_down, back = route(count)
    own_part, to_core, cross_part, below_part, above_part, diag_b_part, diag_a_part = outs
    if after is not None:
        (to_core, diag_b_part, diag_a_part), _ = lax.optimization_barrier(
            ((to_core, diag_b_part, diag_a_part), after)
        )
    to_partner = send(to_core, core)
    diag_back_below = send(diag_b_part, back(diag_up))
    diag_back_above = send(diag_a_part, back(diag_down))
    return [to_partner, diag_back_below, diag_back_above]


def return_second(outs, first, count, after):
    core, cross, down, up, diag_up, diag_down, back = route(count)
    own_part, to_core, cross_part, below_part, above_part, diag_b_part, diag_a_part = outs
    to_partner, diag_back_below, diag_back_above = first
    wide = lambda tensor: tensor.astype(jnp.float32)
    cross_sum = wide(cross_part) + wide(to_partner[1]) + wide(diag_back_below) + wide(diag_back_above)
    below_sum = wide(below_part) + wide(to_partner[2])
    above_sum = wide(above_part) + wide(to_partner[3])
    sums = (cross_sum.astype(jnp.bfloat16), below_sum.astype(jnp.bfloat16), above_sum.astype(jnp.bfloat16))
    if after is not None:
        sums, _ = lax.optimization_barrier((sums, after))
    got_cross = send(sums[0], cross)
    got_below = send(sums[1], down)
    got_above = send(sums[2], up)
    summed = wide(own_part) + wide(to_partner[0]) + wide(got_cross) + wide(got_below) + wide(got_above)
    return [got_cross, got_below, got_above], summed


def body(queries, keys, values, out_grad, frame_keep, band_window):
    rows_own, channel_total = queries.shape
    frame_len = QUARTERS * rows_own
    inv_root = 1.0 / math.sqrt(HD)
    count = lax.axis_size("tm")
    device = lax.axis_index("tm")
    quarter = device % QUARTERS
    partner = device ^ 1

    middle = (quarter == 1) | (quarter == 2)
    diag_quarter = QUARTERS - 1 - quarter
    absent = jnp.int32(-(1 << 20))
    sources = [
        device,
        partner,
        device ^ 2,
        device - QUARTERS,
        device + QUARTERS,
        device ^ 3,
        partner - QUARTERS,
        partner + QUARTERS,
        jnp.where(middle, device - quarter - QUARTERS + diag_quarter, absent),
        jnp.where(middle, device - quarter + QUARTERS + diag_quarter, absent),
    ]
    base_rows = jnp.arange(rows_own, dtype=jnp.int32)
    far_rows = jnp.concatenate([source * rows_own + base_rows for source in sources])
    own_rows = device * rows_own + base_rows
    forward_mask = allowed(own_rows, far_rows, frame_keep, band_window, frame_len).astype(jnp.int32)
    heads = channel_total // HD
    chunk_heads = heads // CHUNKS if heads % CHUNKS == 0 else heads
    width = chunk_heads * HD
    starts = list(range(0, channel_total, width))
    firsts, seconds, outs, backs, sums, dqs = [], [], [], [], [], []
    for c, first in enumerate(starts):
        own = jnp.stack([keys[:, first : first + width], values[:, first : first + width]])
        firsts.append(forward_relay(own, count, None))
    for c in range(len(starts)):
        seconds.append(forward_second(firsts[c], count, None))
    for c, first in enumerate(starts):
        dq, parts = chunk_kernel(forward_mask, queries, out_grad, seconds[c], first // HD, inv_root)
        dqs.append(dq)
        outs.append(parts)
    for c in range(len(starts)):
        backs.append(return_first(outs[c], count, None))
    got = None
    for c in range(len(starts)):
        got, summed = return_second(outs[c], backs[c], count, None)
        sums.append(summed)
    grads = [(dqs[c], sums[c][0].astype(jnp.bfloat16), sums[c][1].astype(jnp.bfloat16)) for c in range(len(starts))]
    query_grad = jnp.concatenate([grad[0] for grad in grads], axis=1)
    key_grad = jnp.concatenate([grad[1] for grad in grads], axis=1)
    value_grad = jnp.concatenate([grad[2] for grad in grads], axis=1)
    return (query_grad, key_grad, value_grad)


def solution(mesh):
    placed = (
        P(("group", "tm"), None),
        P(("group", "tm"), None),
        P(("group", "tm"), None),
        P(("group", "tm"), None),
        P("group", None),
        P("group"),
    )
    return jax.shard_map(
        body,
        mesh=mesh,
        in_specs=placed,
        out_specs=(P(("group", "tm"), None), P(("group", "tm"), None), P(("group", "tm"), None)),
        check_vma=False,
    )
```

```python
import math

import jax
import jax.numpy as jnp
from jax import lax
from jax.experimental import pallas as pl
from jax.sharding import PartitionSpec as P

HD = 128
QUARTERS = 4
CHUNKS = 2
STEP_HEADS = 2


def send(value, pairs):
    return lax.ppermute(value, "tm", pairs)


def pairs_of(count, target):
    pairs = []
    for source in range(count):
        dest = target(source)
        if dest is not None and 0 <= dest < count:
            pairs.append((source, dest))
    return pairs


def route(count):
    core = pairs_of(count, lambda t: t ^ 1)
    cross = pairs_of(count, lambda t: t ^ 2)
    down = pairs_of(count, lambda t: t - QUARTERS)
    up = pairs_of(count, lambda t: t + QUARTERS)

    def diag(step):
        def target(t):
            q = t % QUARTERS
            if q == 0:
                return t + step * QUARTERS + 1
            if q == QUARTERS - 1:
                return t + step * QUARTERS - 1
            return None

        return pairs_of(count, target)

    diag_up = diag(1)
    diag_down = diag(-1)
    back = lambda pairs: [(dest, source) for source, dest in pairs]
    return core, cross, down, up, diag_up, diag_down, back


def allowed(query_rows, key_rows, frame_keep, band_window, frame_len):
    frame_count = frame_keep.shape[0]
    query_frame = jnp.floor_divide(query_rows[0], frame_len)
    query_place = query_rows - query_frame * frame_len
    key_frame = jnp.floor_divide(key_rows, frame_len)
    key_place = key_rows - key_frame * frame_len
    query_inside = (query_rows >= 0) & (query_rows < frame_count * frame_len)
    key_inside = (key_rows >= 0) & (key_rows < frame_count * frame_len)
    keep = lax.dynamic_index_in_dim(frame_keep, query_frame, 0, keepdims=False)
    window = lax.dynamic_index_in_dim(band_window, query_frame, 0, keepdims=False)
    frame_gap = key_frame - query_frame
    kept_pair = jnp.zeros(frame_gap.shape, jnp.int32)
    for column in range(3):
        kept_pair = kept_pair + jnp.where(frame_gap == column - 1, keep[column], 0)
    key_ok = key_inside & (kept_pair > 0)
    place_gap = jnp.abs(query_place[:, None] - key_place[None, :])
    nearby = (frame_gap == 0)[None, :] | (place_gap <= window)
    return query_inside[:, None] & key_ok[None, :] & nearby


def attention_backward(mask, queries, out_grad, inputs, slot_in, out_lead, slot_out, inv_root, offset, dq_into):
    rows, channels = inputs[0].shape[-2:]
    heads = channels // HD
    slots = len(slot_in)
    n_in = len(inputs)

    def kernel(mask_ref, q_ref, g_ref, *refs):
        in_refs = refs[:n_in]
        skip = 0 if dq_into is None else 1
        dq_ref = refs[n_in + skip]
        out_refs = refs[n_in + skip + 1 :]
        nt = (((1,), (1,)), ((), ()))
        tn = (((0,), (0,)), ((), ()))
        for j in range(STEP_HEADS):
            cols = slice(j * HD, (j + 1) * HD)
            k = jnp.concatenate([in_refs[i][lead + (0, slice(None), cols)] for i, lead in slot_in], axis=0)
            v = jnp.concatenate([in_refs[i][lead + (1, slice(None), cols)] for i, lead in slot_in], axis=0)
            q = q_ref[:, cols]
            g = g_ref[:, cols]
            scores = lax.dot_general(q, k, nt, preferred_element_type=jnp.float32) * inv_root
            masked = jnp.where(mask_ref[...] != 0, scores, -1e30)
            highest = jnp.max(masked, axis=1, keepdims=True)
            total_mass = jnp.sum(jnp.exp(masked - highest), axis=1, keepdims=True)
            log_total = highest + jnp.log(total_mass)
            prob = jnp.exp(masked - log_total)
            prob_low = prob.astype(jnp.bfloat16)
            attended = jnp.dot(prob_low, v, preferred_element_type=jnp.float32)
            delta = jnp.sum(g.astype(jnp.float32) * attended, axis=1, keepdims=True)
            prob_grad = lax.dot_general(g, v, nt, preferred_element_type=jnp.float32)
            score_grad = (prob * (prob_grad - delta)).astype(jnp.bfloat16)
            dq = jnp.dot(score_grad, k, preferred_element_type=jnp.float32) * inv_root
            dq_ref[:, cols] = dq.astype(dq_ref.dtype)
            dk = lax.dot_general(score_grad, q, tn, preferred_element_type=jnp.float32) * inv_root
            dv = lax.dot_general(prob_low, g, tn, preferred_element_type=jnp.float32)
            for slot, (i, lead) in enumerate(slot_out):
                part = slice(slot * rows, (slot + 1) * rows)
                out_refs[i][lead + (0, slice(None), cols)] = dk[part].astype(jnp.bfloat16)
                out_refs[i][lead + (1, slice(None), cols)] = dv[part].astype(jnp.bfloat16)

    def head_spec(lead_shape):
        zeros = (0,) * len(lead_shape)
        return pl.BlockSpec(lead_shape + (2, rows, STEP_HEADS * HD), lambda h: zeros + (0, 0, h))

    in_specs = [
        pl.BlockSpec((rows, slots * rows), lambda h: (0, 0)),
        pl.BlockSpec((rows, STEP_HEADS * HD), lambda h: (0, h + offset // STEP_HEADS)),
        pl.BlockSpec((rows, STEP_HEADS * HD), lambda h: (0, h + offset // STEP_HEADS)),
    ] + [head_spec(tuple(x.shape[:-3])) for x in inputs]
    out_specs = [pl.BlockSpec((rows, STEP_HEADS * HD), lambda h: (0, h + offset // STEP_HEADS))] + [head_spec(lead) for lead in out_lead]
    out_shape = [jax.ShapeDtypeStruct(queries.shape, jnp.bfloat16)] + [
        jax.ShapeDtypeStruct(lead + (2, rows, channels), jnp.bfloat16) for lead in out_lead
    ]
    extra = [] if dq_into is None else [dq_into]
    if dq_into is not None:
        in_specs = in_specs + [pl.BlockSpec(memory_space=pl.ANY)]
    results = pl.pallas_call(
        kernel,
        grid=(heads // STEP_HEADS,),
        input_output_aliases={} if dq_into is None else {3 + n_in: 0},
        in_specs=in_specs,
        out_specs=out_specs,
        out_shape=out_shape,
        cost_estimate=pl.CostEstimate(
            flops=12 * heads * rows * slots * rows * HD,
            transcendentals=2 * heads * rows * slots * rows,
            bytes_accessed=2 * 4 * slots * rows * channels + 6 * rows * channels + 4 * rows * slots * rows,
        ),
    )(mask, queries, out_grad, *inputs, *extra)
    return results[0], results[1:]


def forward_relay(own, count, after):
    core, cross, down, up, diag_up, diag_down, back = route(count)
    if after is not None:
        own, _ = lax.optimization_barrier((own, after))
    from_cross = send(own, cross)
    from_below = send(own, up)
    from_above = send(own, down)
    return [own, from_cross, from_below, from_above]


def forward_second(first, count, after):
    core, cross, down, up, diag_up, diag_down, back = route(count)
    own, from_cross, from_below, from_above = first
    relayed = [send(block, core) for block in first]
    diag_from_below = send(from_cross, diag_up)
    diag_from_above = send(from_cross, diag_down)
    return first + relayed + [diag_from_below, diag_from_above]


def chunk_kernel(forward_mask, queries, out_grad, inputs, head_offset, inv_root, dq_into):
    slot_in = [(0, ()), (4, ()), (1, ()), (2, ()), (3, ()), (5, ()), (6, ()), (7, ()), (8, ()), (9, ())]
    out_lead = [(), (4,), (), (), (), (), ()]
    slot_out = [(0, ()), (1, (0,)), (2, ()), (3, ()), (4, ()), (1, (1,)), (1, (2,)), (1, (3,)), (5, ()), (6, ())]
    return attention_backward(
        forward_mask, queries, out_grad, inputs, slot_in, out_lead, slot_out, inv_root, head_offset, dq_into
    )


def return_first(outs, count, after):
    core, cross, down, up, diag_up, diag_down, back = route(count)
    own_part, to_core, cross_part, below_part, above_part, diag_b_part, diag_a_part = outs
    if after is not None:
        (to_core, diag_b_part, diag_a_part), _ = lax.optimization_barrier(
            ((to_core, diag_b_part, diag_a_part), after)
        )
    to_partner = send(to_core, core)
    diag_back_below = send(diag_b_part, back(diag_up))
    diag_back_above = send(diag_a_part, back(diag_down))
    return [to_partner, diag_back_below, diag_back_above]


def return_second(outs, first, count, after):
    core, cross, down, up, diag_up, diag_down, back = route(count)
    own_part, to_core, cross_part, below_part, above_part, diag_b_part, diag_a_part = outs
    to_partner, diag_back_below, diag_back_above = first
    wide = lambda tensor: tensor.astype(jnp.float32)
    cross_sum = wide(cross_part) + wide(to_partner[1]) + wide(diag_back_below) + wide(diag_back_above)
    below_sum = wide(below_part) + wide(to_partner[2])
    above_sum = wide(above_part) + wide(to_partner[3])
    sums = (cross_sum.astype(jnp.bfloat16), below_sum.astype(jnp.bfloat16), above_sum.astype(jnp.bfloat16))
    if after is not None:
        sums, _ = lax.optimization_barrier((sums, after))
    got_cross = send(sums[0], cross)
    got_below = send(sums[1], down)
    got_above = send(sums[2], up)
    summed = wide(own_part) + wide(to_partner[0]) + wide(got_cross) + wide(got_below) + wide(got_above)
    return [got_cross, got_below, got_above], summed


def body(queries, keys, values, out_grad, frame_keep, band_window):
    rows_own, channel_total = queries.shape
    frame_len = QUARTERS * rows_own
    inv_root = 1.0 / math.sqrt(HD)
    count = lax.axis_size("tm")
    device = lax.axis_index("tm")
    quarter = device % QUARTERS
    partner = device ^ 1

    middle = (quarter == 1) | (quarter == 2)
    diag_quarter = QUARTERS - 1 - quarter
    absent = jnp.int32(-(1 << 20))
    sources = [
        device,
        partner,
        device ^ 2,
        device - QUARTERS,
        device + QUARTERS,
        device ^ 3,
        partner - QUARTERS,
        partner + QUARTERS,
        jnp.where(middle, device - quarter - QUARTERS + diag_quarter, absent),
        jnp.where(middle, device - quarter + QUARTERS + diag_quarter, absent),
    ]
    base_rows = jnp.arange(rows_own, dtype=jnp.int32)
    far_rows = jnp.concatenate([source * rows_own + base_rows for source in sources])
    own_rows = device * rows_own + base_rows
    forward_mask = allowed(own_rows, far_rows, frame_keep, band_window, frame_len).astype(jnp.int32)
    heads = channel_total // HD
    chunk_heads = heads // CHUNKS if heads % CHUNKS == 0 else heads
    width = chunk_heads * HD
    starts = list(range(0, channel_total, width))
    firsts, seconds, outs, backs, sums, dqs = [], [], [], [], [], []
    for c, first in enumerate(starts):
        own = jnp.stack([keys[:, first : first + width], values[:, first : first + width]])
        firsts.append(forward_relay(own, count, None))
    for c in range(len(starts)):
        seconds.append(forward_second(firsts[c], count, None))
    for c, first in enumerate(starts):
        dq, parts = chunk_kernel(
            forward_mask, queries, out_grad, seconds[c], first // HD, inv_root, dqs[-1] if dqs else None
        )
        dqs.append(dq)
        outs.append(parts)
    for c in range(len(starts)):
        backs.append(return_first(outs[c], count, None))
    got = None
    for c in range(len(starts)):
        got, summed = return_second(outs[c], backs[c], count, None)
        sums.append(summed)
    grads = [(dqs[c], sums[c][0].astype(jnp.bfloat16), sums[c][1].astype(jnp.bfloat16)) for c in range(len(starts))]
    query_grad = dqs[-1]
    key_grad = jnp.concatenate([grad[1] for grad in grads], axis=1)
    value_grad = jnp.concatenate([grad[2] for grad in grads], axis=1)
    return (query_grad, key_grad, value_grad)


def solution(mesh):
    placed = (
        P(("group", "tm"), None),
        P(("group", "tm"), None),
        P(("group", "tm"), None),
        P(("group", "tm"), None),
        P("group", None),
        P("group"),
    )
    return jax.shard_map(
        body,
        mesh=mesh,
        in_specs=placed,
        out_specs=(P(("group", "tm"), None), P(("group", "tm"), None), P(("group", "tm"), None)),
        check_vma=False,
    )
```

```python
import math

import jax
import jax.numpy as jnp
from jax import lax
from jax.experimental import pallas as pl
from jax.sharding import PartitionSpec as P

HD = 128
QUARTERS = 4
CHUNKS = 2
STEP_HEADS = 2


def send(value, pairs):
    return lax.ppermute(value, "tm", pairs)


def pairs_of(count, target):
    pairs = []
    for source in range(count):
        dest = target(source)
        if dest is not None and 0 <= dest < count:
            pairs.append((source, dest))
    return pairs


def route(count):
    core = pairs_of(count, lambda t: t ^ 1)
    cross = pairs_of(count, lambda t: t ^ 2)
    down = pairs_of(count, lambda t: t - QUARTERS)
    up = pairs_of(count, lambda t: t + QUARTERS)

    def diag(step):
        def target(t):
            q = t % QUARTERS
            if q == 0:
                return t + step * QUARTERS + 1
            if q == QUARTERS - 1:
                return t + step * QUARTERS - 1
            return None

        return pairs_of(count, target)

    diag_up = diag(1)
    diag_down = diag(-1)
    back = lambda pairs: [(dest, source) for source, dest in pairs]
    return core, cross, down, up, diag_up, diag_down, back


def allowed(query_rows, key_rows, frame_keep, band_window, frame_len):
    frame_count = frame_keep.shape[0]
    query_frame = jnp.floor_divide(query_rows[0], frame_len)
    query_place = query_rows - query_frame * frame_len
    key_frame = jnp.floor_divide(key_rows, frame_len)
    key_place = key_rows - key_frame * frame_len
    query_inside = (query_rows >= 0) & (query_rows < frame_count * frame_len)
    key_inside = (key_rows >= 0) & (key_rows < frame_count * frame_len)
    keep = lax.dynamic_index_in_dim(frame_keep, query_frame, 0, keepdims=False)
    window = lax.dynamic_index_in_dim(band_window, query_frame, 0, keepdims=False)
    frame_gap = key_frame - query_frame
    kept_pair = jnp.zeros(frame_gap.shape, jnp.int32)
    for column in range(3):
        kept_pair = kept_pair + jnp.where(frame_gap == column - 1, keep[column], 0)
    key_ok = key_inside & (kept_pair > 0)
    place_gap = jnp.abs(query_place[:, None] - key_place[None, :])
    nearby = (frame_gap == 0)[None, :] | (place_gap <= window)
    return query_inside[:, None] & key_ok[None, :] & nearby


def attention_backward(mask, queries, out_grad, inputs, slot_in, out_lead, slot_out, inv_root, offset):
    rows, channels = inputs[0].shape[-2:]
    heads = channels // HD
    slots = len(slot_in)
    n_in = len(inputs)

    def kernel(mask_ref, q_ref, g_ref, *refs):
        in_refs = refs[:n_in]
        dq_ref = refs[n_in]
        out_refs = refs[n_in + 1 :]
        nt = (((1,), (1,)), ((), ()))
        tn = (((0,), (0,)), ((), ()))
        for j in range(STEP_HEADS):
            cols = slice(j * HD, (j + 1) * HD)
            k = jnp.concatenate([in_refs[i][lead + (0, slice(None), cols)] for i, lead in slot_in], axis=0)
            v = jnp.concatenate([in_refs[i][lead + (1, slice(None), cols)] for i, lead in slot_in], axis=0)
            q = q_ref[:, cols]
            g = g_ref[:, cols]
            scores = lax.dot_general(q, k, nt, preferred_element_type=jnp.float32) * inv_root
            masked = jnp.where(mask_ref[...] != 0, scores, -1e30)
            highest = jnp.max(masked, axis=1, keepdims=True)
            total_mass = jnp.sum(jnp.exp(masked - highest), axis=1, keepdims=True)
            log_total = highest + jnp.log(total_mass)
            prob = jnp.exp(masked - log_total)
            prob_low = prob.astype(jnp.bfloat16)
            attended = jnp.dot(prob_low, v, preferred_element_type=jnp.float32)
            delta = jnp.sum(g.astype(jnp.float32) * attended, axis=1, keepdims=True)
            prob_grad = lax.dot_general(g, v, nt, preferred_element_type=jnp.float32)
            score_grad = (prob * (prob_grad - delta)).astype(jnp.bfloat16)
            dq = jnp.dot(score_grad, k, preferred_element_type=jnp.float32) * inv_root
            dq_ref[:, cols] = dq.astype(dq_ref.dtype)
            dk = lax.dot_general(score_grad, q, tn, preferred_element_type=jnp.float32) * inv_root
            dv = lax.dot_general(prob_low, g, tn, preferred_element_type=jnp.float32)
            for slot, (i, lead) in enumerate(slot_out):
                part = slice(slot * rows, (slot + 1) * rows)
                out_refs[i][lead + (0, slice(None), cols)] = dk[part].astype(jnp.bfloat16)
                out_refs[i][lead + (1, slice(None), cols)] = dv[part].astype(jnp.bfloat16)

    def head_spec(lead_shape):
        zeros = (0,) * len(lead_shape)
        return pl.BlockSpec(lead_shape + (2, rows, STEP_HEADS * HD), lambda h: zeros + (0, 0, h))

    in_specs = [
        pl.BlockSpec((rows, slots * rows), lambda h: (0, 0)),
        pl.BlockSpec((rows, STEP_HEADS * HD), lambda h: (0, h + offset // STEP_HEADS)),
        pl.BlockSpec((rows, STEP_HEADS * HD), lambda h: (0, h + offset // STEP_HEADS)),
    ] + [head_spec(tuple(x.shape[:-3])) for x in inputs]
    out_specs = [pl.BlockSpec((rows, STEP_HEADS * HD), lambda h: (0, h))] + [head_spec(lead) for lead in out_lead]
    out_shape = [jax.ShapeDtypeStruct((rows, channels), jnp.bfloat16)] + [
        jax.ShapeDtypeStruct(lead + (2, rows, channels), jnp.bfloat16) for lead in out_lead
    ]
    results = pl.pallas_call(
        kernel,
        grid=(heads // STEP_HEADS,),
        in_specs=in_specs,
        out_specs=out_specs,
        out_shape=out_shape,
        cost_estimate=pl.CostEstimate(
            flops=12 * heads * rows * slots * rows * HD,
            transcendentals=2 * heads * rows * slots * rows,
            bytes_accessed=2 * 4 * slots * rows * channels + 6 * rows * channels + 4 * rows * slots * rows,
        ),
    )(mask, queries, out_grad, *inputs)
    return results[0], results[1:]


def forward_relay(own, count, after):
    core, cross, down, up, diag_up, diag_down, back = route(count)
    if after is not None:
        own, _ = lax.optimization_barrier((own, after))
    from_cross = send(own, cross)
    from_below = send(own, up)
    from_above = send(own, down)
    return [own, from_cross, from_below, from_above]


def forward_second(first, count, after):
    core, cross, down, up, diag_up, diag_down, back = route(count)
    own, from_cross, from_below, from_above = first
    relayed = [send(block, core) for block in first]
    diag_from_below = send(from_cross, diag_up)
    diag_from_above = send(from_cross, diag_down)
    return first + relayed + [diag_from_below, diag_from_above]


def chunk_kernel(forward_mask, queries, out_grad, inputs, head_offset, inv_root):
    slot_in = [(0, ()), (4, ()), (1, ()), (2, ()), (3, ()), (5, ()), (6, ()), (7, ()), (8, ()), (9, ())]
    out_lead = [(), (4,), (), (), (), (), ()]
    slot_out = [(0, ()), (1, (0,)), (2, ()), (3, ()), (4, ()), (1, (1,)), (1, (2,)), (1, (3,)), (5, ()), (6, ())]
    return attention_backward(
        forward_mask, queries, out_grad, inputs, slot_in, out_lead, slot_out, inv_root, head_offset
    )


def return_first(outs, count, after):
    core, cross, down, up, diag_up, diag_down, back = route(count)
    own_part, to_core, cross_part, below_part, above_part, diag_b_part, diag_a_part = outs
    if after is not None:
        (to_core, diag_b_part, diag_a_part), _ = lax.optimization_barrier(
            ((to_core, diag_b_part, diag_a_part), after)
        )
    to_partner = send(to_core, core)
    diag_back_below = send(diag_b_part, back(diag_up))
    diag_back_above = send(diag_a_part, back(diag_down))
    return [to_partner, diag_back_below, diag_back_above]


def return_second(outs, first, count, after):
    core, cross, down, up, diag_up, diag_down, back = route(count)
    own_part, to_core, cross_part, below_part, above_part, diag_b_part, diag_a_part = outs
    to_partner, diag_back_below, diag_back_above = first
    wide = lambda tensor: tensor.astype(jnp.float32)
    cross_sum = wide(cross_part) + wide(to_partner[1]) + wide(diag_back_below) + wide(diag_back_above)
    below_sum = wide(below_part) + wide(to_partner[2])
    above_sum = wide(above_part) + wide(to_partner[3])
    sums = (cross_sum.astype(jnp.bfloat16), below_sum.astype(jnp.bfloat16), above_sum.astype(jnp.bfloat16))
    if after is not None:
        sums, _ = lax.optimization_barrier((sums, after))
    got_cross = send(sums[0], cross)
    got_below = send(sums[1], down)
    got_above = send(sums[2], up)
    summed = wide(own_part) + wide(to_partner[0]) + wide(got_cross) + wide(got_below) + wide(got_above)
    return [got_cross, got_below, got_above], summed


def body(queries, keys, values, out_grad, frame_keep, band_window):
    rows_own, channel_total = queries.shape
    frame_len = QUARTERS * rows_own
    inv_root = 1.0 / math.sqrt(HD)
    count = lax.axis_size("tm")
    device = lax.axis_index("tm")
    quarter = device % QUARTERS
    partner = device ^ 1

    middle = (quarter == 1) | (quarter == 2)
    diag_quarter = QUARTERS - 1 - quarter
    absent = jnp.int32(-(1 << 20))
    sources = [
        device,
        partner,
        device ^ 2,
        device - QUARTERS,
        device + QUARTERS,
        device ^ 3,
        partner - QUARTERS,
        partner + QUARTERS,
        jnp.where(middle, device - quarter - QUARTERS + diag_quarter, absent),
        jnp.where(middle, device - quarter + QUARTERS + diag_quarter, absent),
    ]
    base_rows = jnp.arange(rows_own, dtype=jnp.int32)
    far_rows = jnp.concatenate([source * rows_own + base_rows for source in sources])
    own_rows = device * rows_own + base_rows
    forward_mask = allowed(own_rows, far_rows, frame_keep, band_window, frame_len).astype(jnp.int32)
    heads = channel_total // HD
    chunk_heads = heads // CHUNKS if heads % CHUNKS == 0 else heads
    width = chunk_heads * HD
    starts = list(range(0, channel_total, width))
    firsts, seconds, outs, backs, sums, dqs = [], [], [], [], [], []
    for c, first in enumerate(starts):
        own = jnp.stack([keys[:, first : first + width], values[:, first : first + width]])
        if c == 0:
            (keys, values), _ = lax.optimization_barrier(((keys, values), own))
        firsts.append(forward_relay(own, count, None))
    for c in range(len(starts)):
        seconds.append(forward_second(firsts[c], count, None))
    for c, first in enumerate(starts):
        dq, parts = chunk_kernel(forward_mask, queries, out_grad, seconds[c], first // HD, inv_root)
        dqs.append(dq)
        outs.append(parts)
    for c in range(len(starts)):
        backs.append(return_first(outs[c], count, None))
    got = None
    for c in range(len(starts)):
        got, summed = return_second(outs[c], backs[c], count, None)
        sums.append(summed)
    grads = [(dqs[c], sums[c][0].astype(jnp.bfloat16), sums[c][1].astype(jnp.bfloat16)) for c in range(len(starts))]
    query_grad = jnp.concatenate([grad[0] for grad in grads], axis=1)
    key_grad = jnp.concatenate([grad[1] for grad in grads], axis=1)
    value_grad = jnp.concatenate([grad[2] for grad in grads], axis=1)
    return (query_grad, key_grad, value_grad)


def solution(mesh):
    placed = (
        P(("group", "tm"), None),
        P(("group", "tm"), None),
        P(("group", "tm"), None),
        P(("group", "tm"), None),
        P("group", None),
        P("group"),
    )
    return jax.shard_map(
        body,
        mesh=mesh,
        in_specs=placed,
        out_specs=(P(("group", "tm"), None), P(("group", "tm"), None), P(("group", "tm"), None)),
        check_vma=False,
    )
```

```python
import math

import jax
import jax.numpy as jnp
from jax import lax
from jax.experimental import pallas as pl
from jax.sharding import PartitionSpec as P

HD = 128
QUARTERS = 4
CHUNKS = 2
STEP_HEADS = 5


def send(value, pairs):
    return lax.ppermute(value, "tm", pairs)


def pairs_of(count, target):
    pairs = []
    for source in range(count):
        dest = target(source)
        if dest is not None and 0 <= dest < count:
            pairs.append((source, dest))
    return pairs


def route(count):
    core = pairs_of(count, lambda t: t ^ 1)
    cross = pairs_of(count, lambda t: t ^ 2)
    down = pairs_of(count, lambda t: t - QUARTERS)
    up = pairs_of(count, lambda t: t + QUARTERS)

    def diag(step):
        def target(t):
            q = t % QUARTERS
            if q == 0:
                return t + step * QUARTERS + 1
            if q == QUARTERS - 1:
                return t + step * QUARTERS - 1
            return None

        return pairs_of(count, target)

    diag_up = diag(1)
    diag_down = diag(-1)
    back = lambda pairs: [(dest, source) for source, dest in pairs]
    return core, cross, down, up, diag_up, diag_down, back


def allowed(query_rows, key_rows, frame_keep, band_window, frame_len):
    frame_count = frame_keep.shape[0]
    query_frame = jnp.floor_divide(query_rows[0], frame_len)
    query_place = query_rows - query_frame * frame_len
    key_frame = jnp.floor_divide(key_rows, frame_len)
    key_place = key_rows - key_frame * frame_len
    query_inside = (query_rows >= 0) & (query_rows < frame_count * frame_len)
    key_inside = (key_rows >= 0) & (key_rows < frame_count * frame_len)
    keep = lax.dynamic_index_in_dim(frame_keep, query_frame, 0, keepdims=False)
    window = lax.dynamic_index_in_dim(band_window, query_frame, 0, keepdims=False)
    frame_gap = key_frame - query_frame
    kept_pair = jnp.zeros(frame_gap.shape, jnp.int32)
    for column in range(3):
        kept_pair = kept_pair + jnp.where(frame_gap == column - 1, keep[column], 0)
    key_ok = key_inside & (kept_pair > 0)
    place_gap = jnp.abs(query_place[:, None] - key_place[None, :])
    nearby = (frame_gap == 0)[None, :] | (place_gap <= window)
    return query_inside[:, None] & key_ok[None, :] & nearby


def attention_backward(mask, queries, out_grad, inputs, slot_in, out_lead, slot_out, inv_root, offset):
    rows, channels = inputs[0].shape[-2:]
    heads = channels // HD
    slots = len(slot_in)
    n_in = len(inputs)

    def kernel(mask_ref, q_ref, g_ref, *refs):
        in_refs = refs[:n_in]
        dq_ref = refs[n_in]
        out_refs = refs[n_in + 1 :]
        nt = (((1,), (1,)), ((), ()))
        tn = (((0,), (0,)), ((), ()))
        for j in range(STEP_HEADS):
            cols = slice(j * HD, (j + 1) * HD)
            k = jnp.concatenate([in_refs[i][lead + (0, slice(None), cols)] for i, lead in slot_in], axis=0)
            v = jnp.concatenate([in_refs[i][lead + (1, slice(None), cols)] for i, lead in slot_in], axis=0)
            q = q_ref[:, cols]
            g = g_ref[:, cols]
            scores = lax.dot_general(q, k, nt, preferred_element_type=jnp.float32) * inv_root
            masked = jnp.where(mask_ref[...] != 0, scores, -1e30)
            highest = jnp.max(masked, axis=1, keepdims=True)
            total_mass = jnp.sum(jnp.exp(masked - highest), axis=1, keepdims=True)
            log_total = highest + jnp.log(total_mass)
            prob = jnp.exp(masked - log_total)
            prob_low = prob.astype(jnp.bfloat16)
            attended = jnp.dot(prob_low, v, preferred_element_type=jnp.float32)
            delta = jnp.sum(g.astype(jnp.float32) * attended, axis=1, keepdims=True)
            prob_grad = lax.dot_general(g, v, nt, preferred_element_type=jnp.float32)
            score_grad = (prob * (prob_grad - delta)).astype(jnp.bfloat16)
            dq = jnp.dot(score_grad, k, preferred_element_type=jnp.float32) * inv_root
            dq_ref[:, cols] = dq.astype(dq_ref.dtype)
            dk = lax.dot_general(score_grad, q, tn, preferred_element_type=jnp.float32) * inv_root
            dv = lax.dot_general(prob_low, g, tn, preferred_element_type=jnp.float32)
            for slot, (i, lead) in enumerate(slot_out):
                part = slice(slot * rows, (slot + 1) * rows)
                out_refs[i][lead + (0, slice(None), cols)] = dk[part].astype(jnp.bfloat16)
                out_refs[i][lead + (1, slice(None), cols)] = dv[part].astype(jnp.bfloat16)

    def head_spec(lead_shape):
        zeros = (0,) * len(lead_shape)
        return pl.BlockSpec(lead_shape + (2, rows, STEP_HEADS * HD), lambda h: zeros + (0, 0, h))

    in_specs = [
        pl.BlockSpec((rows, slots * rows), lambda h: (0, 0)),
        pl.BlockSpec((rows, STEP_HEADS * HD), lambda h: (0, h + offset // STEP_HEADS)),
        pl.BlockSpec((rows, STEP_HEADS * HD), lambda h: (0, h + offset // STEP_HEADS)),
    ] + [head_spec(tuple(x.shape[:-3])) for x in inputs]
    out_specs = [pl.BlockSpec((rows, STEP_HEADS * HD), lambda h: (0, h))] + [head_spec(lead) for lead in out_lead]
    out_shape = [jax.ShapeDtypeStruct((rows, channels), jnp.bfloat16)] + [
        jax.ShapeDtypeStruct(lead + (2, rows, channels), jnp.bfloat16) for lead in out_lead
    ]
    results = pl.pallas_call(
        kernel,
        grid=(heads // STEP_HEADS,),
        in_specs=in_specs,
        out_specs=out_specs,
        out_shape=out_shape,
        cost_estimate=pl.CostEstimate(
            flops=12 * heads * rows * slots * rows * HD,
            transcendentals=2 * heads * rows * slots * rows,
            bytes_accessed=2 * 4 * slots * rows * channels + 6 * rows * channels + 4 * rows * slots * rows,
        ),
    )(mask, queries, out_grad, *inputs)
    return results[0], results[1:]


def forward_relay(own, count, after):
    core, cross, down, up, diag_up, diag_down, back = route(count)
    if after is not None:
        own, _ = lax.optimization_barrier((own, after))
    from_cross = send(own, cross)
    from_below = send(own, up)
    from_above = send(own, down)
    return [own, from_cross, from_below, from_above]


def forward_second(first, count, after):
    core, cross, down, up, diag_up, diag_down, back = route(count)
    own, from_cross, from_below, from_above = first
    relayed = [send(block, core) for block in first]
    diag_from_below = send(from_cross, diag_up)
    diag_from_above = send(from_cross, diag_down)
    return first + relayed + [diag_from_below, diag_from_above]


def chunk_kernel(forward_mask, queries, out_grad, inputs, head_offset, inv_root):
    slot_in = [(0, ()), (4, ()), (1, ()), (2, ()), (3, ()), (5, ()), (6, ()), (7, ()), (8, ()), (9, ())]
    out_lead = [(), (4,), (), (), (), (), ()]
    slot_out = [(0, ()), (1, (0,)), (2, ()), (3, ()), (4, ()), (1, (1,)), (1, (2,)), (1, (3,)), (5, ()), (6, ())]
    return attention_backward(
        forward_mask, queries, out_grad, inputs, slot_in, out_lead, slot_out, inv_root, head_offset
    )


def return_first(outs, count, after):
    core, cross, down, up, diag_up, diag_down, back = route(count)
    own_part, to_core, cross_part, below_part, above_part, diag_b_part, diag_a_part = outs
    if after is not None:
        (to_core, diag_b_part, diag_a_part), _ = lax.optimization_barrier(
            ((to_core, diag_b_part, diag_a_part), after)
        )
    to_partner = send(to_core, core)
    diag_back_below = send(diag_b_part, back(diag_up))
    diag_back_above = send(diag_a_part, back(diag_down))
    return [to_partner, diag_back_below, diag_back_above]


def return_second(outs, first, count, after):
    core, cross, down, up, diag_up, diag_down, back = route(count)
    own_part, to_core, cross_part, below_part, above_part, diag_b_part, diag_a_part = outs
    to_partner, diag_back_below, diag_back_above = first
    wide = lambda tensor: tensor.astype(jnp.float32)
    cross_sum = wide(cross_part) + wide(to_partner[1]) + wide(diag_back_below) + wide(diag_back_above)
    below_sum = wide(below_part) + wide(to_partner[2])
    above_sum = wide(above_part) + wide(to_partner[3])
    sums = (cross_sum.astype(jnp.bfloat16), below_sum.astype(jnp.bfloat16), above_sum.astype(jnp.bfloat16))
    if after is not None:
        sums, _ = lax.optimization_barrier((sums, after))
    got_cross = send(sums[0], cross)
    got_below = send(sums[1], down)
    got_above = send(sums[2], up)
    summed = wide(own_part) + wide(to_partner[0]) + wide(got_cross) + wide(got_below) + wide(got_above)
    return [got_cross, got_below, got_above], summed


def body(queries, keys, values, out_grad, frame_keep, band_window):
    rows_own, channel_total = queries.shape
    frame_len = QUARTERS * rows_own
    inv_root = 1.0 / math.sqrt(HD)
    count = lax.axis_size("tm")
    device = lax.axis_index("tm")
    quarter = device % QUARTERS
    partner = device ^ 1

    middle = (quarter == 1) | (quarter == 2)
    diag_quarter = QUARTERS - 1 - quarter
    absent = jnp.int32(-(1 << 20))
    sources = [
        device,
        partner,
        device ^ 2,
        device - QUARTERS,
        device + QUARTERS,
        device ^ 3,
        partner - QUARTERS,
        partner + QUARTERS,
        jnp.where(middle, device - quarter - QUARTERS + diag_quarter, absent),
        jnp.where(middle, device - quarter + QUARTERS + diag_quarter, absent),
    ]
    base_rows = jnp.arange(rows_own, dtype=jnp.int32)
    far_rows = jnp.concatenate([source * rows_own + base_rows for source in sources])
    own_rows = device * rows_own + base_rows
    forward_mask = allowed(own_rows, far_rows, frame_keep, band_window, frame_len).astype(jnp.int32)
    heads = channel_total // HD
    chunk_heads = heads // CHUNKS if heads % CHUNKS == 0 else heads
    width = chunk_heads * HD
    starts = list(range(0, channel_total, width))
    firsts, seconds, outs, backs, sums, dqs = [], [], [], [], [], []
    for c, first in enumerate(starts):
        own = jnp.stack([keys[:, first : first + width], values[:, first : first + width]])
        firsts.append(forward_relay(own, count, None))
    for c in range(len(starts)):
        seconds.append(forward_second(firsts[c], count, None))
    for c, first in enumerate(starts):
        dq, parts = chunk_kernel(forward_mask, queries, out_grad, seconds[c], first // HD, inv_root)
        dqs.append(dq)
        outs.append(parts)
    for c in range(len(starts)):
        backs.append(return_first(outs[c], count, None))
    got = None
    for c in range(len(starts)):
        got, summed = return_second(outs[c], backs[c], count, None)
        sums.append(summed)
    grads = [(dqs[c], sums[c][0].astype(jnp.bfloat16), sums[c][1].astype(jnp.bfloat16)) for c in range(len(starts))]
    query_grad = jnp.concatenate([grad[0] for grad in grads], axis=1)
    key_grad = jnp.concatenate([grad[1] for grad in grads], axis=1)
    value_grad = jnp.concatenate([grad[2] for grad in grads], axis=1)
    return (query_grad, key_grad, value_grad)


def solution(mesh):
    placed = (
        P(("group", "tm"), None),
        P(("group", "tm"), None),
        P(("group", "tm"), None),
        P(("group", "tm"), None),
        P("group", None),
        P("group"),
    )
    return jax.shard_map(
        body,
        mesh=mesh,
        in_specs=placed,
        out_specs=(P(("group", "tm"), None), P(("group", "tm"), None), P(("group", "tm"), None)),
        check_vma=False,
    )
```

```python
import math

import jax
import jax.numpy as jnp
from jax import lax
from jax.experimental import pallas as pl
from jax.sharding import PartitionSpec as P

HD = 128
QUARTERS = 4
CHUNKS = 2
STEP_HEADS = 2


def send(value, pairs):
    return lax.ppermute(value, "tm", pairs)


def pairs_of(count, target):
    pairs = []
    for source in range(count):
        dest = target(source)
        if dest is not None and 0 <= dest < count:
            pairs.append((source, dest))
    return pairs


def route(count):
    core = pairs_of(count, lambda t: t ^ 1)
    cross = pairs_of(count, lambda t: t ^ 2)
    down = pairs_of(count, lambda t: t - QUARTERS)
    up = pairs_of(count, lambda t: t + QUARTERS)

    def diag(step):
        def target(t):
            q = t % QUARTERS
            if q == 0:
                return t + step * QUARTERS + 1
            if q == QUARTERS - 1:
                return t + step * QUARTERS - 1
            return None

        return pairs_of(count, target)

    diag_up = diag(1)
    diag_down = diag(-1)
    back = lambda pairs: [(dest, source) for source, dest in pairs]
    return core, cross, down, up, diag_up, diag_down, back


def allowed(query_rows, key_rows, frame_keep, band_window, frame_len):
    frame_count = frame_keep.shape[0]
    query_frame = jnp.floor_divide(query_rows[0], frame_len)
    query_place = query_rows - query_frame * frame_len
    key_frame = jnp.floor_divide(key_rows, frame_len)
    key_place = key_rows - key_frame * frame_len
    query_inside = (query_rows >= 0) & (query_rows < frame_count * frame_len)
    key_inside = (key_rows >= 0) & (key_rows < frame_count * frame_len)
    keep = lax.dynamic_index_in_dim(frame_keep, query_frame, 0, keepdims=False)
    window = lax.dynamic_index_in_dim(band_window, query_frame, 0, keepdims=False)
    frame_gap = key_frame - query_frame
    kept_pair = jnp.zeros(frame_gap.shape, jnp.int32)
    for column in range(3):
        kept_pair = kept_pair + jnp.where(frame_gap == column - 1, keep[column], 0)
    key_ok = key_inside & (kept_pair > 0)
    place_gap = jnp.abs(query_place[:, None] - key_place[None, :])
    nearby = (frame_gap == 0)[None, :] | (place_gap <= window)
    return query_inside[:, None] & key_ok[None, :] & nearby


def attention_backward(mask, queries, out_grad, inputs, slot_in, out_lead, slot_out, inv_root, offset):
    rows, channels = inputs[0].shape[-2:]
    heads = channels // HD
    slots = len(slot_in)
    n_in = len(inputs)

    def kernel(mask_ref, q_ref, g_ref, *refs):
        in_refs = refs[:n_in]
        dq_ref = refs[n_in]
        out_refs = refs[n_in + 1 :]
        nt = (((1,), (1,)), ((), ()))
        tn = (((0,), (0,)), ((), ()))
        for j in range(STEP_HEADS):
            cols = slice(j * HD, (j + 1) * HD)
            k = jnp.concatenate([in_refs[i][lead + (0, slice(None), cols)] for i, lead in slot_in], axis=0)
            v = jnp.concatenate([in_refs[i][lead + (1, slice(None), cols)] for i, lead in slot_in], axis=0)
            q = q_ref[:, cols]
            g = g_ref[:, cols]
            scores = lax.dot_general(q, k, nt, preferred_element_type=jnp.float32) * inv_root
            masked = scores + mask_ref[...]
            highest = jnp.max(masked, axis=1, keepdims=True)
            total_mass = jnp.sum(jnp.exp(masked - highest), axis=1, keepdims=True)
            log_total = highest + jnp.log(total_mass)
            prob = jnp.exp(masked - log_total)
            prob_low = prob.astype(jnp.bfloat16)
            attended = jnp.dot(prob_low, v, preferred_element_type=jnp.float32)
            delta = jnp.sum(g.astype(jnp.float32) * attended, axis=1, keepdims=True)
            prob_grad = lax.dot_general(g, v, nt, preferred_element_type=jnp.float32)
            score_grad = (prob * (prob_grad - delta)).astype(jnp.bfloat16)
            dq = jnp.dot(score_grad, k, preferred_element_type=jnp.float32) * inv_root
            dq_ref[:, cols] = dq.astype(dq_ref.dtype)
            dk = lax.dot_general(score_grad, q, tn, preferred_element_type=jnp.float32) * inv_root
            dv = lax.dot_general(prob_low, g, tn, preferred_element_type=jnp.float32)
            for slot, (i, lead) in enumerate(slot_out):
                part = slice(slot * rows, (slot + 1) * rows)
                out_refs[i][lead + (0, slice(None), cols)] = dk[part].astype(jnp.bfloat16)
                out_refs[i][lead + (1, slice(None), cols)] = dv[part].astype(jnp.bfloat16)

    def head_spec(lead_shape):
        zeros = (0,) * len(lead_shape)
        return pl.BlockSpec(lead_shape + (2, rows, STEP_HEADS * HD), lambda h: zeros + (0, 0, h))

    in_specs = [
        pl.BlockSpec((rows, slots * rows), lambda h: (0, 0)),
        pl.BlockSpec((rows, STEP_HEADS * HD), lambda h: (0, h + offset // STEP_HEADS)),
        pl.BlockSpec((rows, STEP_HEADS * HD), lambda h: (0, h + offset // STEP_HEADS)),
    ] + [head_spec(tuple(x.shape[:-3])) for x in inputs]
    out_specs = [pl.BlockSpec((rows, STEP_HEADS * HD), lambda h: (0, h))] + [head_spec(lead) for lead in out_lead]
    out_shape = [jax.ShapeDtypeStruct((rows, channels), jnp.bfloat16)] + [
        jax.ShapeDtypeStruct(lead + (2, rows, channels), jnp.bfloat16) for lead in out_lead
    ]
    results = pl.pallas_call(
        kernel,
        grid=(heads // STEP_HEADS,),
        in_specs=in_specs,
        out_specs=out_specs,
        out_shape=out_shape,
        cost_estimate=pl.CostEstimate(
            flops=12 * heads * rows * slots * rows * HD,
            transcendentals=2 * heads * rows * slots * rows,
            bytes_accessed=2 * 4 * slots * rows * channels + 6 * rows * channels + 4 * rows * slots * rows,
        ),
    )(mask, queries, out_grad, *inputs)
    return results[0], results[1:]


def forward_relay(own, count, after):
    core, cross, down, up, diag_up, diag_down, back = route(count)
    if after is not None:
        own, _ = lax.optimization_barrier((own, after))
    from_cross = send(own, cross)
    from_below = send(own, up)
    from_above = send(own, down)
    return [own, from_cross, from_below, from_above]


def forward_second(first, count, after):
    core, cross, down, up, diag_up, diag_down, back = route(count)
    own, from_cross, from_below, from_above = first
    relayed = [send(block, core) for block in first]
    diag_from_below = send(from_cross, diag_up)
    diag_from_above = send(from_cross, diag_down)
    return first + relayed + [diag_from_below, diag_from_above]


def chunk_kernel(forward_mask, queries, out_grad, inputs, head_offset, inv_root):
    slot_in = [(0, ()), (4, ()), (1, ()), (2, ()), (3, ()), (5, ()), (6, ()), (7, ()), (8, ()), (9, ())]
    out_lead = [(), (4,), (), (), (), (), ()]
    slot_out = [(0, ()), (1, (0,)), (2, ()), (3, ()), (4, ()), (1, (1,)), (1, (2,)), (1, (3,)), (5, ()), (6, ())]
    return attention_backward(
        forward_mask, queries, out_grad, inputs, slot_in, out_lead, slot_out, inv_root, head_offset
    )


def return_first(outs, count, after):
    core, cross, down, up, diag_up, diag_down, back = route(count)
    own_part, to_core, cross_part, below_part, above_part, diag_b_part, diag_a_part = outs
    if after is not None:
        (to_core, diag_b_part, diag_a_part), _ = lax.optimization_barrier(
            ((to_core, diag_b_part, diag_a_part), after)
        )
    to_partner = send(to_core, core)
    diag_back_below = send(diag_b_part, back(diag_up))
    diag_back_above = send(diag_a_part, back(diag_down))
    return [to_partner, diag_back_below, diag_back_above]


def return_second(outs, first, count, after):
    core, cross, down, up, diag_up, diag_down, back = route(count)
    own_part, to_core, cross_part, below_part, above_part, diag_b_part, diag_a_part = outs
    to_partner, diag_back_below, diag_back_above = first
    wide = lambda tensor: tensor.astype(jnp.float32)
    cross_sum = wide(cross_part) + wide(to_partner[1]) + wide(diag_back_below) + wide(diag_back_above)
    below_sum = wide(below_part) + wide(to_partner[2])
    above_sum = wide(above_part) + wide(to_partner[3])
    sums = (cross_sum.astype(jnp.bfloat16), below_sum.astype(jnp.bfloat16), above_sum.astype(jnp.bfloat16))
    if after is not None:
        sums, _ = lax.optimization_barrier((sums, after))
    got_cross = send(sums[0], cross)
    got_below = send(sums[1], down)
    got_above = send(sums[2], up)
    summed = wide(own_part) + wide(to_partner[0]) + wide(got_cross) + wide(got_below) + wide(got_above)
    return [got_cross, got_below, got_above], summed


def body(queries, keys, values, out_grad, frame_keep, band_window):
    rows_own, channel_total = queries.shape
    frame_len = QUARTERS * rows_own
    inv_root = 1.0 / math.sqrt(HD)
    count = lax.axis_size("tm")
    device = lax.axis_index("tm")
    quarter = device % QUARTERS
    partner = device ^ 1

    middle = (quarter == 1) | (quarter == 2)
    diag_quarter = QUARTERS - 1 - quarter
    absent = jnp.int32(-(1 << 20))
    sources = [
        device,
        partner,
        device ^ 2,
        device - QUARTERS,
        device + QUARTERS,
        device ^ 3,
        partner - QUARTERS,
        partner + QUARTERS,
        jnp.where(middle, device - quarter - QUARTERS + diag_quarter, absent),
        jnp.where(middle, device - quarter + QUARTERS + diag_quarter, absent),
    ]
    base_rows = jnp.arange(rows_own, dtype=jnp.int32)
    far_rows = jnp.concatenate([source * rows_own + base_rows for source in sources])
    own_rows = device * rows_own + base_rows
    forward_mask = jnp.where(allowed(own_rows, far_rows, frame_keep, band_window, frame_len), 0.0, -1e30)
    heads = channel_total // HD
    chunk_heads = heads // CHUNKS if heads % CHUNKS == 0 else heads
    width = chunk_heads * HD
    starts = list(range(0, channel_total, width))
    firsts, seconds, outs, backs, sums, dqs = [], [], [], [], [], []
    for c, first in enumerate(starts):
        own = jnp.stack([keys[:, first : first + width], values[:, first : first + width]])
        firsts.append(forward_relay(own, count, None))
    for c in range(len(starts)):
        seconds.append(forward_second(firsts[c], count, None))
    for c, first in enumerate(starts):
        dq, parts = chunk_kernel(forward_mask, queries, out_grad, seconds[c], first // HD, inv_root)
        dqs.append(dq)
        outs.append(parts)
    for c in range(len(starts)):
        backs.append(return_first(outs[c], count, None))
    got = None
    for c in range(len(starts)):
        got, summed = return_second(outs[c], backs[c], count, None)
        sums.append(summed)
    grads = [(dqs[c], sums[c][0].astype(jnp.bfloat16), sums[c][1].astype(jnp.bfloat16)) for c in range(len(starts))]
    query_grad = jnp.concatenate([grad[0] for grad in grads], axis=1)
    key_grad = jnp.concatenate([grad[1] for grad in grads], axis=1)
    value_grad = jnp.concatenate([grad[2] for grad in grads], axis=1)
    return (query_grad, key_grad, value_grad)


def solution(mesh):
    placed = (
        P(("group", "tm"), None),
        P(("group", "tm"), None),
        P(("group", "tm"), None),
        P(("group", "tm"), None),
        P("group", None),
        P("group"),
    )
    return jax.shard_map(
        body,
        mesh=mesh,
        in_specs=placed,
        out_specs=(P(("group", "tm"), None), P(("group", "tm"), None), P(("group", "tm"), None)),
        check_vma=False,
    )
```
